32 devices in a mesh: wide: 16 (over z, y, core), narrow: 2 (over x).
Axes of the slice: x: 2, y: 2, z: 4, core: 2. Of those that a mesh axis runs over, the one named last changes fastest.
Arguments:
- inputs: bfloat16 [32, 680, 1024], P(('wide', 'narrow')), may hold values from -6 to 6
- condition: bfloat16 [32, 1024], P(('wide', 'narrow')), may hold values from -6 to 6
- scale_tokens: int32 [10], replicated, may hold values from 1 to 256, 680 in all
- w_ada: bfloat16 [1024, 6144], P(('wide', 'narrow')), may hold values from -0.1875 to 0.1875
- bias_ada: bfloat16 [6144], P(('wide', 'narrow')), may hold values from -3 to 3
- w_qkv: bfloat16 [1024, 3072], P(('wide', 'narrow')), may hold values from -0.1875 to 0.1875
- bias_query: bfloat16 [1024], P(('wide', 'narrow')), may hold values from -3 to 3
- bias_value: bfloat16 [1024], P(('wide', 'narrow')), may hold values from -3 to 3
- gain_query: bfloat16 [1024], P(('wide', 'narrow')), may hold values from 1 to 2
- gain_key: bfloat16 [1024], P(('wide', 'narrow')), may hold values from 1 to 2
- w_proj: bfloat16 [1024, 1024], P(('wide', 'narrow')), may hold values from -0.75 to 0.75
- bias_proj: bfloat16 [1024], P(('wide', 'narrow')), may hold values from -3 to 3
- w_up: bfloat16 [1024, 4096], P(('wide', 'narrow')), may hold values from -0.1875 to 0.1875
- bias_up: bfloat16 [4096], P(('wide', 'narrow')), may hold values from -3 to 3
- w_down: bfloat16 [4096, 1024], P(('wide', 'narrow')), may hold values from -0.1875 to 0.1875
- bias_down: bfloat16 [1024], P(('wide', 'narrow')), may hold values from -3 to 3
- cotangent: bfloat16 [32, 680, 1024], P(('wide', 'narrow')), may hold values from -6 to 6
Outputs:
- layer_output: bfloat16 [32, 680, 1024], P(('wide', 'narrow'))
- input_grad: float32 [32, 680, 1024], P(('wide', 'narrow'))
- condition_grad: float32 [32, 1024], P(('wide', 'narrow'))
- w_ada_grad: float32 [1024, 6144], P(('wide', 'narrow'))
- bias_ada_grad: float32 [6144], P(('wide', 'narrow'))
- w_qkv_grad: float32 [1024, 3072], P(('wide', 'narrow'))
- bias_query_grad: float32 [1024], P(('wide', 'narrow'))
- bias_value_grad: float32 [1024], P(('wide', 'narrow'))
- gain_query_grad: float32 [1024], P(('wide', 'narrow'))
- gain_key_grad: float32 [1024], P(('wide', 'narrow'))
- w_proj_grad: float32 [1024, 1024], P(('wide', 'narrow'))
- bias_proj_grad: float32 [1024], P(('wide', 'narrow'))
- w_up_grad: float32 [1024, 4096], P(('wide', 'narrow'))
- bias_up_grad: float32 [4096], P(('wide', 'narrow'))
- w_down_grad: float32 [4096, 1024], P(('wide', 'narrow'))
- bias_down_grad: float32 [1024], P(('wide', 'narrow'))
The draws below stay inside these ranges and needn't reach their ends.
Inputs may be any that keep to these rules, and one draw needn't show every extreme that they name: `scale_tokens`: the 10 counts sum to 680; the largest is 256; they may come in any order.
All inputs are finite; a program needn't handle non-finite values.
Results may differ from the reference program's by a relative error of at most 0.02.
Values may be sent and summed in bfloat16 or wider, within the bound.
No kernel may reach another device: no remote copies, remote signals or barrier semaphores. Data moves between devices by JAX's collectives and lax.ppermute only.
A program may use at most 256 MiB of HBM per device.

```python
import math
import jax
import jax.numpy as jnp
import numpy as np
from jax import lax

D = 1024
HEADS = 16
HEAD_DIM = 64
FF = 4096
COND = 1024
SEQ_LEN = 680
SCALES = 10
SCALE_MOST = 256
SEQ_DEV = 1
SEQS = 32


def with_spikes(values, rng, source, target, shards_of, factor):
    def block_of(dim):
        return (jnp.arange(values.shape[dim]) // (values.shape[dim] // shards_of)).reshape((-1,) + (1,) * (values.ndim - 1 - dim))

    first = jax.random.permutation(rng, shards_of)[block_of(target)]
    other_side = (block_of(target) + shards_of // 2) % shards_of
    return jnp.where((block_of(source) == first) | (block_of(source) == other_side), factor * values, values)


def steps_of(stream_key, extent, cuts, least, high):
    loudness, own = 1.0, jax.random.fold_in(stream_key, 6)
    for axis_at, shards_of in cuts:
        heights = jnp.exp(jax.random.uniform(jax.random.fold_in(own, axis_at), (shards_of,), jnp.float32, least / len(cuts), high / len(cuts)))
        loudness = loudness * jnp.repeat(heights, extent[axis_at] // shards_of).reshape([-1 if axis == axis_at else 1 for axis in range(len(extent))])
    return loudness


def split_up(amount, total, bound, slope):
    portions = [(1 << 20) // math.isqrt(standing ** slope) + 1 for standing in range(2, amount + 1)]
    rest, given = total - bound - (amount - 1), [1] * (amount - 1)
    while rest > 0:
        free = [i for i in range(amount - 1) if given[i] < bound]
        mass, remaining = sum([portions[i] for i in free]), rest
        for i in free:
            addition = min(bound - given[i], max(1, remaining * portions[i] // mass), rest)
            given[i] = given[i] + addition
            rest = rest - addition
    return np.array([bound] + given)


def uneven_parts(key, number_of, total, most, skew):
    if number_of == 2:
        one = jax.random.randint(key, (), max(1, total - most), min(most, total - 1) + 1)
        return jnp.stack([one, total - one])
    tallies = jnp.asarray(split_up(number_of, total, most, skew), jnp.int32)
    pairs = (number_of - 1) // 2
    donor, receiver = tallies[1:1 + 2 * pairs:2], tallies[2:2 + 2 * pairs:2]
    slack = jnp.minimum(donor - 1, most - receiver)
    moved = jax.random.randint(jax.random.fold_in(key, 1), (pairs,), 0, 1 << 20) % (slack + 1)
    tallies = tallies.at[1:1 + 2 * pairs:2].set(donor - moved).at[2:2 + 2 * pairs:2].set(receiver + moved)
    return tallies[jax.random.permutation(jax.random.fold_in(key, 2), number_of)]


def gaussian(rng, extent, width, most, cuts=(), held_as=jnp.bfloat16):
    drawn = jax.random.normal(rng, extent, jnp.float32) * width
    if len(cuts) > 0:
        drawn = steps_of(rng, extent, cuts, -0.22, 0.18) * drawn
    return jnp.clip(drawn, min=-most, max=most).astype(held_as)


def gaussian_with(stream_key, extent, spread, bound, shards, heavy, held_as=jnp.bfloat16):
    drawn = spread * jax.random.normal(stream_key, extent, jnp.float32)
    if shards:
        drawn = drawn * steps_of(stream_key, extent, shards, -0.22, 0.18)
    return jnp.clip(with_spikes(drawn, jax.random.fold_in(stream_key, 3), *heavy), -bound, bound).astype(held_as)


def setup_inputs(seed: int = 0) -> dict:
    splits = jax.random.split(jax.random.key(seed), 18)
    inputs = gaussian(splits[0], (SEQS, SEQ_LEN, D), 1.0, 6.0, ((0, 32),))
    condition = gaussian(splits[1], (SEQS, COND), 1.0, 6.0, ((0, 32),))
    scale_tokens = uneven_parts(splits[2], SCALES, SEQ_LEN, SCALE_MOST, 1).astype(jnp.int32)
    w_ada = gaussian(splits[3], (COND, 6 * D), COND ** -0.5, 0.1875, ((0, 32),))
    bias_ada = gaussian(splits[4], (6 * D,), 0.5, 3.0, ((0, 32),))
    w_qkv = gaussian(splits[5], (D, 3 * D), D ** -0.5, 0.1875, ((0, 32),))
    bias_query = gaussian(splits[6], (D,), 0.5, 3.0, ((0, 32),))
    bias_value = gaussian(splits[7], (D,), 0.5, 3.0, ((0, 32),))
    gain_query = jnp.clip(1.0 + 1.0 * jax.random.uniform(splits[8], (D,), jnp.float32) ** steps_of(splits[8], (D,), ((0, 32),), -0.2, 0.2), 1.0, 2.0).astype(jnp.bfloat16)
    gain_key = jnp.clip(1.0 + 1.0 * jax.random.uniform(splits[9], (D,), jnp.float32) ** steps_of(splits[9], (D,), ((0, 32),), -0.2, 0.2), 1.0, 2.0).astype(jnp.bfloat16)
    w_proj = gaussian(splits[10], (D, D), (D // 16) ** -0.5, 0.75, ((0, 32),))
    bias_proj = gaussian(splits[11], (D,), 0.5, 3.0, ((0, 32),))
    w_up = gaussian(splits[12], (D, FF), D ** -0.5, 0.1875, ((0, 32),))
    bias_up = gaussian(splits[13], (FF,), 0.5, 3.0, ((0, 32),))
    w_down = gaussian(splits[14], (FF, D), (FF // 4) ** -0.5, 0.1875, ((0, 32),))
    bias_down = gaussian(splits[15], (D,), 0.5, 3.0, ((0, 32),))
    cotangent = gaussian_with(splits[16], (SEQS, SEQ_LEN, D), 1.0, 6.0, ((0, 32),), (0, 2, 32, 2.75))
    return {"inputs": inputs, "condition": condition, "scale_tokens": scale_tokens, "w_ada": w_ada, "bias_ada": bias_ada, "w_qkv": w_qkv, "bias_query": bias_query, "bias_value": bias_value, "gain_query": gain_query, "gain_key": gain_key, "w_proj": w_proj, "bias_proj": bias_proj, "w_up": w_up, "bias_up": bias_up, "w_down": w_down, "bias_down": bias_down, "cotangent": cotangent}


@jax.custom_vjp
def low(v):
    return lax.optimization_barrier(v.astype(jnp.bfloat16)).astype(jnp.float32)

@jax.custom_vjp
def low_back(v):
    return v

def low_keep(v):
    return (low(v), None)

def low_pass(kept, grad):
    return (grad,)

def back_keep(v):
    return (v, None)

def back_low(kept, grad):
    return (low(grad),)
low.defvjp(low_keep, low_pass)
low_back.defvjp(back_keep, back_low)
EPSILON = 1e-06
MASKED = -1000000000.0

def product(first_operand, second_operand):
    return jnp.matmul(first_operand, second_operand, precision=lax.Precision.HIGHEST)

def layer_norm(values):
    centred = values - lax.optimization_barrier(jnp.mean(values, axis=-1, keepdims=True))
    return centred * lax.rsqrt(lax.optimization_barrier(jnp.mean(centred * centred, axis=-1, keepdims=True)) + EPSILON)

def modulate(values, scaling, offset):
    return layer_norm(values) * (1.0 + scaling[:, None, :]) + offset[:, None, :]

def head_norm(values, channel_gain):
    shaped = values.reshape(values.shape[0], values.shape[1], HEADS, HEAD_DIM)
    scaled = shaped * lax.rsqrt(lax.optimization_barrier(jnp.mean(shaped * shaped, axis=-1, keepdims=True)) + EPSILON)
    return scaled * channel_gain.reshape(HEADS, HEAD_DIM)

def block_mask(scale_tokens):
    block_ends = jnp.cumsum(scale_tokens).astype(jnp.int32)
    places = jnp.arange(SEQ_LEN, dtype=jnp.int32)
    limits = lax.optimization_barrier(jnp.min(jnp.where(block_ends[None, :] > places[:, None], block_ends[None, :], SEQ_LEN), axis=1))
    return places[None, :] < limits[:, None]

def forward(inputs, condition, weights, allowed):
    w_ada, bias_ada, w_qkv, bias_query, bias_value, gain_query, gain_key, w_proj, bias_proj, w_up, bias_up, w_down, bias_down = weights
    activated = low(jax.nn.silu(condition))
    adaptive = low_back(product(activated, w_ada) + bias_ada)
    gamma_attn, gamma_mlp, scale_attn, scale_mlp, shift_attn, shift_mlp = jnp.split(adaptive, 6, axis=1)
    normed_attn = low(modulate(inputs, scale_attn, shift_attn))
    projected = low_back(product(normed_attn, w_qkv))
    queries = low(head_norm(projected[..., :D] + bias_query, gain_query))
    key_rows = low(head_norm(projected[..., D:2 * D], gain_key))
    value_rows = low(projected[..., 2 * D:] + bias_value).reshape(inputs.shape[0], inputs.shape[1], HEADS, HEAD_DIM)
    scores = low_back(jnp.einsum('slhd,smhd->shlm', queries, key_rows, precision=lax.Precision.HIGHEST) * HEAD_DIM ** (-0.5))
    scores = jnp.where(allowed[None, None], scores, MASKED)
    probabilities_reduced = low(jax.nn.softmax(scores, axis=-1))
    context = jnp.einsum('shlm,smhd->slhd', probabilities_reduced, value_rows, precision=lax.Precision.HIGHEST).reshape(inputs.shape)
    context = low(low_back(context))
    attended = low_back(product(context, w_proj) + bias_proj)
    middle = inputs + gamma_attn[:, None, :] * attended
    normed_mlp = low(modulate(middle, scale_mlp, shift_mlp))
    hidden_pre = low_back(product(normed_mlp, w_up) + bias_up)
    hidden = low(jax.nn.gelu(hidden_pre, approximate=True))
    branch = low_back(product(hidden, w_down) + bias_down)
    return middle + gamma_mlp[:, None, :] * branch

def reference(inputs, condition, scale_tokens, w_ada, bias_ada, w_qkv, bias_query, bias_value, gain_query, gain_key, w_proj, bias_proj, w_up, bias_up, w_down, bias_down, cotangent):
    weights = tuple((member.astype(jnp.float32) for member in (w_ada, bias_ada, w_qkv, bias_query, bias_value, gain_query, gain_key, w_proj, bias_proj, w_up, bias_up, w_down, bias_down)))
    allowed = block_mask(scale_tokens)
    grouped = (inputs.reshape(-1, SEQ_DEV, SEQ_LEN, D), condition.reshape(-1, SEQ_DEV, COND), cotangent.reshape(-1, SEQ_DEV, SEQ_LEN, D))

    def one_group(totals, member):
        batch_rows, batch_cond, upstream = member
        result, pullback = jax.vjp(lambda rows_now, cond_now, params_now: forward(rows_now, cond_now, params_now, allowed), batch_rows.astype(jnp.float32), batch_cond.astype(jnp.float32), weights)
        rows_grad, cond_grad, weight_grads = pullback(upstream.astype(jnp.float32))
        totals = jax.tree.map(lambda first_operand, second_operand: first_operand + second_operand, totals, weight_grads)
        return (totals, (result.astype(jnp.bfloat16), rows_grad, cond_grad))
    totals, (outputs, input_grads, condition_grads) = lax.scan(one_group, jax.tree.map(jnp.zeros_like, weights), grouped)
    return (outputs.reshape(inputs.shape), input_grads.reshape(inputs.shape), condition_grads.reshape(condition.shape), totals[0], totals[1], totals[2], totals[3], totals[4], totals[5], totals[6], totals[7], totals[8], totals[9], totals[10], totals[11], totals[12])
```

```python
import jax
import jax.numpy as jnp
from jax import lax
from jax.sharding import PartitionSpec as P

HEADS = 16
HEAD_DIM = 64
SEQ_LEN = 680
AXES = ("wide", "narrow")

EPSILON = 1e-06
MASKED = -1000000000.0


def layer_norm(values):
    centred = values - jnp.mean(values, axis=-1, keepdims=True)
    return centred * lax.rsqrt(jnp.mean(centred * centred, axis=-1, keepdims=True) + EPSILON)


def modulate(values, scaling, offset):
    return layer_norm(values) * (1.0 + scaling[:, None, :]) + offset[:, None, :]


def head_norm(values, channel_gain):
    shaped = values.reshape(values.shape[0], values.shape[1], HEADS, HEAD_DIM)
    scaled = shaped * lax.rsqrt(jnp.mean(shaped * shaped, axis=-1, keepdims=True) + EPSILON)
    return scaled * channel_gain.reshape(HEADS, HEAD_DIM)


def gelu_tanh(values):
    return jax.nn.gelu(values, approximate=True)


def block_mask(scale_tokens):
    block_ends = jnp.cumsum(scale_tokens)
    places = jnp.arange(SEQ_LEN, dtype=jnp.int32)
    limits = jnp.min(
        jnp.where(block_ends[None, :] > places[:, None], block_ends[None, :], SEQ_LEN), axis=1
    )
    return places[None, :] < limits[:, None]


def matmul_rows(first_operand, second_operand):
    return jnp.einsum(
        "fyg,gq->fyq", first_operand, second_operand, preferred_element_type=jnp.float32
    )


def matmul_back(first_operand, second_operand):
    return jnp.einsum(
        "rfw,uw->rfu", first_operand, second_operand, preferred_element_type=jnp.float32
    )


def weight_grad(first_operand, second_operand):
    return jnp.einsum(
        "crk,cre->ke", first_operand, second_operand, preferred_element_type=jnp.float32
    )


def masked_scores(query_sequence, key_sequence, allowed):
    scores = jnp.einsum(
        "nkz,vkz->knv", query_sequence, key_sequence, preferred_element_type=jnp.float32
    ) * HEAD_DIM ** (-0.5)
    return jnp.where(allowed[None], scores, MASKED)


def attend_forward(query_sequence, key_sequence, value_sequence, allowed):
    scores = masked_scores(query_sequence, key_sequence, allowed)
    row_max = jnp.max(scores, axis=-1, keepdims=True)
    exponent = jnp.exp(scores - row_max)
    row_total = jnp.sum(exponent, axis=-1, keepdims=True)
    probabilities_reduced = (exponent / row_total).astype(jnp.bfloat16)
    context = jnp.einsum(
        "wcv,vwn->cwn", probabilities_reduced, value_sequence, preferred_element_type=jnp.float32
    ).astype(jnp.bfloat16)
    return (context, row_max[..., 0] + jnp.log(row_total[..., 0]))


def attend_backward(
    query_sequence, key_sequence, value_sequence, logsum, context_gradient, allowed
):
    scores = masked_scores(query_sequence, key_sequence, allowed)
    attention_probabilities = jnp.exp(scores - logsum[..., None])
    prob_grad = jnp.einsum(
        "nkz,vkz->knv", context_gradient, value_sequence, preferred_element_type=jnp.float32
    )
    value_grad = jnp.einsum(
        "fgs,gfu->sfu",
        attention_probabilities.astype(jnp.bfloat16),
        context_gradient,
        preferred_element_type=jnp.float32,
    )
    score_gradient = (
        attention_probabilities
        * (prob_grad - jnp.sum(prob_grad * attention_probabilities, axis=-1, keepdims=True))
    ).astype(jnp.bfloat16)
    query_grad = jnp.einsum(
        "wcv,vwn->cwn", score_gradient, key_sequence, preferred_element_type=jnp.float32
    ) * HEAD_DIM ** (-0.5)
    key_grad = jnp.einsum(
        "fgs,gfu->sfu", score_gradient, query_sequence, preferred_element_type=jnp.float32
    ) * HEAD_DIM ** (-0.5)
    return (query_grad, key_grad, value_grad)


def gather_vectors(vectors, count):
    packed = lax.all_gather(jnp.concatenate(vectors), AXES, axis=0, tiled=False)
    out, start = [], 0
    for member in vectors:
        size = member.shape[0]
        out.append(packed[:, start : start + size].reshape(count * size).astype(jnp.float32))
        start += size
    return out


def scatter_vectors(vectors, count):
    packed = jnp.concatenate([member.reshape(count, -1) for member in vectors], axis=1)
    summed = lax.psum_scatter(packed, AXES, scatter_dimension=0, tiled=True)[0]
    out, start = [], 0
    for member in vectors:
        size = member.shape[0] // count
        out.append(summed[start : start + size])
        start += size
    return out


def scatter_matrix(member):
    return lax.psum_scatter(
        member.astype(jnp.bfloat16), AXES, scatter_dimension=0, tiled=True
    ).astype(jnp.float32)


def shards(
    inputs,
    condition,
    scale_tokens,
    w_ada,
    bias_ada,
    w_qkv,
    bias_query,
    bias_value,
    gain_query,
    gain_key,
    w_proj,
    bias_proj,
    w_up,
    bias_up,
    w_down,
    bias_down,
    cotangent,
):
    count = lax.axis_size("wide") * lax.axis_size("narrow")
    me = lax.axis_index("wide") * lax.axis_size("narrow") + lax.axis_index("narrow")
    ada_bias, query_bias, value_bias, query_gain, key_gain, proj_bias, up_bias, down_bias = (
        gather_vectors(
            (bias_ada, bias_query, bias_value, gain_query, gain_key, bias_proj, bias_up, bias_down),
            count,
        )
    )
    qkv_full = lax.all_gather(w_qkv, AXES, axis=0, tiled=True)
    proj_full = lax.all_gather(w_proj, AXES, axis=0, tiled=True)
    up_full = lax.all_gather(w_up, AXES, axis=0, tiled=True)
    down_full = lax.all_gather(w_down, AXES, axis=0, tiled=True)
    sequences, length, width = inputs.shape
    head_shape = (sequences, length, HEADS, HEAD_DIM)
    allowed = block_mask(scale_tokens)
    input_rows = inputs.astype(jnp.float32)
    cond_rows = condition.astype(jnp.float32)
    activated = jax.nn.silu(cond_rows).astype(jnp.bfloat16)
    ada_rows = w_ada.shape[0]
    ada_cols = w_ada.shape[1]
    activated_all = lax.all_gather(activated, AXES, axis=0, tiled=True)
    activated_mine = lax.dynamic_slice_in_dim(activated_all, me * ada_rows, ada_rows, axis=1)
    ada_partial = jnp.dot(activated_mine, w_ada, preferred_element_type=jnp.float32)
    adaptive = lax.psum_scatter(ada_partial, AXES, scatter_dimension=0, tiled=True) + ada_bias
    gamma_attn, gamma_mlp, scale_attn, scale_mlp, shift_attn, shift_mlp = jnp.split(
        adaptive, 6, axis=1
    )
    normed_attn = modulate(input_rows, scale_attn, shift_attn).astype(jnp.bfloat16)
    projected = matmul_rows(normed_attn, qkv_full)
    query_pre = projected[..., :width] + query_bias
    key_pre = projected[..., width : 2 * width]
    queries = head_norm(query_pre, query_gain).astype(jnp.bfloat16)
    key_rows = head_norm(key_pre, key_gain).astype(jnp.bfloat16)
    value_rows = (projected[..., 2 * width :] + value_bias).astype(jnp.bfloat16).reshape(head_shape)
    context, logsum = jax.vmap(
        lambda q, k, v: attend_forward(q, k, v, allowed)
    )(queries, key_rows, value_rows)
    context = context.reshape(sequences, length, width)
    attended = matmul_rows(context, proj_full) + proj_bias
    middle = input_rows + gamma_attn[:, None, :] * attended
    normed_mlp = modulate(middle, scale_mlp, shift_mlp).astype(jnp.bfloat16)
    hidden_pre = matmul_rows(normed_mlp, up_full) + up_bias
    hidden = gelu_tanh(hidden_pre).astype(jnp.bfloat16)
    branch = matmul_rows(hidden, down_full) + down_bias
    layer_output = (middle + gamma_mlp[:, None, :] * branch).astype(jnp.bfloat16)
    upstream = cotangent.astype(jnp.float32)
    gamma_mlp_grad = jnp.sum(upstream * branch, axis=1)
    branch_grad = (upstream * gamma_mlp[:, None, :]).astype(jnp.bfloat16)
    down_sum = scatter_matrix(weight_grad(hidden, branch_grad))
    down_bias_grad = jnp.sum(branch_grad.astype(jnp.float32), axis=(0, 1))
    hidden_grad = matmul_back(branch_grad, down_full)
    gelu_pull = jax.vjp(gelu_tanh, hidden_pre)[1]
    pre_grad = gelu_pull(hidden_grad)[0].astype(jnp.bfloat16)
    up_sum = scatter_matrix(weight_grad(normed_mlp, pre_grad))
    up_bias_grad = jnp.sum(pre_grad.astype(jnp.float32), axis=(0, 1))
    normed_mlp_grad = matmul_back(pre_grad, up_full)
    mlp_pull = jax.vjp(modulate, middle, scale_mlp, shift_mlp)[1]
    middle_part, scale_mlp_grad, shift_mlp_grad = mlp_pull(normed_mlp_grad)
    middle_grad = upstream + middle_part
    gamma_attn_grad = jnp.sum(middle_grad * attended, axis=1)
    attended_grad = (middle_grad * gamma_attn[:, None, :]).astype(jnp.bfloat16)
    proj_sum = scatter_matrix(weight_grad(context, attended_grad))
    proj_bias_grad = jnp.sum(attended_grad.astype(jnp.float32), axis=(0, 1))
    context_gradient = (
        matmul_back(attended_grad, proj_full).astype(jnp.bfloat16).reshape(head_shape)
    )
    query_grad, key_grad, value_grad = jax.vmap(
        lambda q, k, v, l, c: attend_backward(q, k, v, l, c, allowed)
    )(queries, key_rows, value_rows, logsum, context_gradient)
    query_pull = jax.vjp(head_norm, query_pre, query_gain)[1]
    query_pre_grad, query_gain_grad = query_pull(query_grad)
    key_pull = jax.vjp(head_norm, key_pre, key_gain)[1]
    key_pre_grad, key_gain_grad = key_pull(key_grad)
    value_grad = value_grad.reshape(sequences, length, width)
    query_bias_grad = jnp.sum(query_pre_grad, axis=(0, 1))
    value_bias_grad = jnp.sum(value_grad, axis=(0, 1))
    projected_grad = jnp.concatenate([query_pre_grad, key_pre_grad, value_grad], axis=2).astype(
        jnp.bfloat16
    )
    qkv_sum = scatter_matrix(weight_grad(normed_attn, projected_grad))
    normed_attn_grad = matmul_back(projected_grad, qkv_full)
    attn_pull = jax.vjp(modulate, input_rows, scale_attn, shift_attn)[1]
    input_part, scale_attn_grad, shift_attn_grad = attn_pull(normed_attn_grad)
    input_grad = middle_grad + input_part
    adaptive_grad = jnp.concatenate(
        [
            gamma_attn_grad,
            gamma_mlp_grad,
            scale_attn_grad,
            scale_mlp_grad,
            shift_attn_grad,
            shift_mlp_grad,
        ],
        axis=1,
    ).astype(jnp.bfloat16)
    adaptive_grad_all = lax.all_gather(adaptive_grad, AXES, axis=0, tiled=True)
    ada_sum = jnp.einsum(
        "sc,sn->cn", activated_mine, adaptive_grad_all, preferred_element_type=jnp.float32
    )
    bias_share = ada_cols // count
    ada_bias_sum = jnp.sum(
        lax.dynamic_slice_in_dim(adaptive_grad_all, me * bias_share, bias_share, axis=1).astype(
            jnp.float32
        ),
        axis=0,
    )
    activated_grad_cols = jnp.einsum(
        "sn,cn->sc", adaptive_grad_all, w_ada, preferred_element_type=jnp.float32
    )
    activated_grad = lax.all_to_all(
        activated_grad_cols, AXES, split_axis=0, concat_axis=1, tiled=True
    )
    silu_pull = jax.vjp(jax.nn.silu, cond_rows)[1]
    condition_grad = silu_pull(activated_grad)[0]
    (
        query_bias_sum,
        value_bias_sum,
        query_gain_sum,
        key_gain_sum,
        proj_bias_sum,
        up_bias_sum,
        down_bias_sum,
    ) = scatter_vectors(
        (
            query_bias_grad,
            value_bias_grad,
            query_gain_grad,
            key_gain_grad,
            proj_bias_grad,
            up_bias_grad,
            down_bias_grad,
        ),
        count,
    )
    return (
        layer_output,
        input_grad,
        condition_grad,
        ada_sum,
        ada_bias_sum,
        qkv_sum,
        query_bias_sum,
        value_bias_sum,
        query_gain_sum,
        key_gain_sum,
        proj_sum,
        proj_bias_sum,
        up_sum,
        up_bias_sum,
        down_sum,
        down_bias_sum,
    )


def solution(mesh):
    row = P(AXES, None, None)
    mat = P(AXES, None)
    vec = P(AXES)
    return jax.shard_map(
        shards,
        mesh=mesh,
        in_specs=(row, mat, P(), mat, vec, mat, vec, vec, vec, vec, mat, vec, mat, vec, mat, vec, row),
        out_specs=(row, row, mat, mat, vec, mat, vec, vec, vec, vec, mat, vec, mat, vec, mat, vec),
        check_vma=False,
    )
```

```python
import jax
import jax.numpy as jnp
from jax import lax
from jax.sharding import PartitionSpec as P


HEADS = 16
HEAD_DIM = 64
SEQ_LEN = 680
AXES = ("wide", "narrow")

EPSILON = 1e-06
MASKED = -1000000000.0


def layer_norm(values):
    centred = values - jnp.mean(values, axis=-1, keepdims=True)
    return centred * lax.rsqrt(jnp.mean(centred * centred, axis=-1, keepdims=True) + EPSILON)


def modulate(values, scaling, offset):
    return layer_norm(values) * (1.0 + scaling[:, None, :]) + offset[:, None, :]


def head_norm(values, channel_gain):
    shaped = values.reshape(values.shape[0], values.shape[1], HEADS, HEAD_DIM)
    scaled = shaped * lax.rsqrt(jnp.mean(shaped * shaped, axis=-1, keepdims=True) + EPSILON)
    return scaled * channel_gain.reshape(HEADS, HEAD_DIM)


def gelu_tanh(values):
    return jax.nn.gelu(values, approximate=True)


def block_mask(scale_tokens):
    block_ends = jnp.cumsum(scale_tokens)
    places = jnp.arange(SEQ_LEN, dtype=jnp.int32)
    limits = jnp.min(
        jnp.where(block_ends[None, :] > places[:, None], block_ends[None, :], SEQ_LEN), axis=1
    )
    return places[None, :] < limits[:, None]


def matmul_rows(first_operand, second_operand):
    return jnp.einsum(
        "fyg,gq->fyq", first_operand, second_operand, preferred_element_type=jnp.float32
    )


def matmul_back(first_operand, second_operand):
    return jnp.einsum(
        "rfw,uw->rfu", first_operand, second_operand, preferred_element_type=jnp.float32
    )


def weight_grad(first_operand, second_operand):
    return jnp.einsum(
        "crk,cre->ke", first_operand, second_operand, preferred_element_type=jnp.float32
    )


def masked_scores(query_sequence, key_sequence, allowed):
    scores = jnp.einsum(
        "nkz,vkz->knv", query_sequence, key_sequence, preferred_element_type=jnp.float32
    ) * HEAD_DIM ** (-0.5)
    return jnp.where(allowed[None], scores, MASKED)


def attend_forward(query_sequence, key_sequence, value_sequence, allowed):
    scores = masked_scores(query_sequence, key_sequence, allowed)
    row_max = jnp.max(scores, axis=-1, keepdims=True)
    exponent = jnp.exp(scores - row_max)
    row_total = jnp.sum(exponent, axis=-1, keepdims=True)
    probabilities_reduced = (exponent / row_total).astype(jnp.bfloat16)
    context = jnp.einsum(
        "wcv,vwn->cwn", probabilities_reduced, value_sequence, preferred_element_type=jnp.float32
    ).astype(jnp.bfloat16)
    return (context, row_max[..., 0] + jnp.log(row_total[..., 0]))


def attend_backward(
    query_sequence, key_sequence, value_sequence, logsum, context_gradient, allowed
):
    scores = masked_scores(query_sequence, key_sequence, allowed)
    attention_probabilities = jnp.exp(scores - logsum[..., None])
    prob_grad = jnp.einsum(
        "nkz,vkz->knv", context_gradient, value_sequence, preferred_element_type=jnp.float32
    )
    value_grad = jnp.einsum(
        "fgs,gfu->sfu",
        attention_probabilities.astype(jnp.bfloat16),
        context_gradient,
        preferred_element_type=jnp.float32,
    )
    score_gradient = (
        attention_probabilities
        * (prob_grad - jnp.sum(prob_grad * attention_probabilities, axis=-1, keepdims=True))
    ).astype(jnp.bfloat16)
    query_grad = jnp.einsum(
        "wcv,vwn->cwn", score_gradient, key_sequence, preferred_element_type=jnp.float32
    ) * HEAD_DIM ** (-0.5)
    key_grad = jnp.einsum(
        "fgs,gfu->sfu", score_gradient, query_sequence, preferred_element_type=jnp.float32
    ) * HEAD_DIM ** (-0.5)
    return (query_grad, key_grad, value_grad)


def nested_gather(member):
    return lax.all_gather(
        lax.all_gather(member, "narrow", axis=0, tiled=True), "wide", axis=0, tiled=True
    )


LANES = 1024


def pack_rows(pieces, count):
    flat = jnp.concatenate([piece.reshape(count, -1) for piece in pieces], axis=1)
    pad = -flat.shape[1] % (LANES * 16)
    if pad:
        flat = jnp.concatenate([flat, jnp.zeros((count, pad), flat.dtype)], axis=1)
    return flat.reshape(count * (flat.shape[1] // LANES), LANES)


def unpack_rows(flat, members, count, leading):
    flat = flat.reshape(leading, -1)
    out, start = [], 0
    for member in members:
        size = member.size // count
        out.append(flat[:, start : start + size])
        start += size
    return out


def gather_packed(members, count):
    got = lax.all_gather(pack_rows([m[None] for m in members], 1), AXES, axis=0, tiled=True)
    pieces = unpack_rows(got, [m[None] for m in members], 1, count)
    return [
        piece.reshape((count * member.shape[0],) + member.shape[1:])
        for piece, member in zip(pieces, members)
    ]


def scatter_packed(members, count):
    flat = pack_rows([member.astype(jnp.bfloat16) for member in members], count)
    half = lax.psum_scatter(flat, "wide", scatter_dimension=0, tiled=True)
    got = lax.psum_scatter(half, "narrow", scatter_dimension=0, tiled=True)
    pieces = unpack_rows(got.astype(jnp.float32), members, count, 1)
    return [
        piece.reshape((member.shape[0] // count,) + member.shape[1:])
        for piece, member in zip(pieces, members)
    ]


def layer(
    inputs,
    condition,
    scale_tokens,
    w_ada,
    bias_ada,
    w_qkv,
    bias_query,
    bias_value,
    gain_query,
    gain_key,
    w_proj,
    bias_proj,
    w_up,
    bias_up,
    w_down,
    bias_down,
    cotangent,
):
    count = lax.axis_size("wide") * lax.axis_size("narrow")
    me = lax.axis_index("wide") * lax.axis_size("narrow") + lax.axis_index("narrow")
    sequences, length, width = inputs.shape
    head_shape = (sequences, length, HEADS, HEAD_DIM)
    cond_rows = condition.astype(jnp.float32)
    activated = jax.nn.silu(cond_rows).astype(jnp.bfloat16)
    vectors = (bias_ada, bias_query, bias_value, gain_query, gain_key, bias_proj, bias_up, bias_down)
    small = nested_gather(
        jnp.concatenate([activated.reshape(-1)] + list(vectors))[None, :]
    )
    activated_all = small[:, : activated.size].reshape(count * sequences, activated.shape[1])
    unpacked, start = [], activated.size
    for member in vectors:
        size = member.shape[0]
        unpacked.append(small[:, start : start + size].reshape(count * size).astype(jnp.float32))
        start += size
    ada_bias, query_bias, value_bias, query_gain, key_gain, proj_bias, up_bias, down_bias = unpacked
    (qkv_full,) = gather_packed((w_qkv,), count)
    proj_full, up_full, down_full = gather_packed((w_proj, w_up, w_down), count)
    allowed = block_mask(scale_tokens)
    input_rows = inputs.astype(jnp.float32)
    ada_rows = w_ada.shape[0]
    ada_cols = w_ada.shape[1]
    activated_mine = lax.dynamic_slice_in_dim(activated_all, me * ada_rows, ada_rows, axis=1)
    ada_partial = jnp.dot(activated_mine, w_ada, preferred_element_type=jnp.float32)
    ada_parts = lax.all_to_all(
        ada_partial.reshape(count, sequences, ada_cols), AXES, split_axis=0, concat_axis=0, tiled=True
    )
    adaptive = jnp.sum(ada_parts, axis=0) + ada_bias
    gamma_attn, gamma_mlp, scale_attn, scale_mlp, shift_attn, shift_mlp = jnp.split(
        adaptive, 6, axis=1
    )
    normed_attn = modulate(input_rows, scale_attn, shift_attn).astype(jnp.bfloat16)
    projected = matmul_rows(normed_attn, qkv_full)
    query_pre = projected[..., :width] + query_bias
    key_pre = projected[..., width : 2 * width]
    queries = head_norm(query_pre, query_gain).astype(jnp.bfloat16)
    key_rows = head_norm(key_pre, key_gain).astype(jnp.bfloat16)
    value_rows = (projected[..., 2 * width :] + value_bias).astype(jnp.bfloat16).reshape(head_shape)
    context, logsum = jax.vmap(
        lambda q, k, v: attend_forward(q, k, v, allowed)
    )(queries, key_rows, value_rows)
    context = context.reshape(sequences, length, width)
    attended = matmul_rows(context, proj_full) + proj_bias
    middle = input_rows + gamma_attn[:, None, :] * attended
    normed_mlp = modulate(middle, scale_mlp, shift_mlp).astype(jnp.bfloat16)
    hidden_pre = matmul_rows(normed_mlp, up_full) + up_bias
    hidden = gelu_tanh(hidden_pre).astype(jnp.bfloat16)
    branch = matmul_rows(hidden, down_full) + down_bias
    layer_output = (middle + gamma_mlp[:, None, :] * branch).astype(jnp.bfloat16)
    upstream = cotangent.astype(jnp.float32)
    gamma_mlp_grad = jnp.sum(upstream * branch, axis=1)
    branch_grad = (upstream * gamma_mlp[:, None, :]).astype(jnp.bfloat16)
    down_grad = weight_grad(hidden, branch_grad)
    down_bias_grad = jnp.sum(branch_grad.astype(jnp.float32), axis=(0, 1))
    hidden_grad = matmul_back(branch_grad, down_full)
    gelu_pull = jax.vjp(gelu_tanh, hidden_pre)[1]
    pre_grad = gelu_pull(hidden_grad)[0].astype(jnp.bfloat16)
    up_grad = weight_grad(normed_mlp, pre_grad)
    down_sum, up_sum = scatter_packed((down_grad, up_grad), count)
    up_bias_grad = jnp.sum(pre_grad.astype(jnp.float32), axis=(0, 1))
    normed_mlp_grad = matmul_back(pre_grad, up_full)
    mlp_pull = jax.vjp(modulate, middle, scale_mlp, shift_mlp)[1]
    middle_part, scale_mlp_grad, shift_mlp_grad = mlp_pull(normed_mlp_grad)
    middle_grad = upstream + middle_part
    gamma_attn_grad = jnp.sum(middle_grad * attended, axis=1)
    attended_grad = (middle_grad * gamma_attn[:, None, :]).astype(jnp.bfloat16)
    proj_grad = weight_grad(context, attended_grad)
    proj_bias_grad = jnp.sum(attended_grad.astype(jnp.float32), axis=(0, 1))
    context_gradient = (
        matmul_back(attended_grad, proj_full).astype(jnp.bfloat16).reshape(head_shape)
    )
    query_grad, key_grad, value_grad = jax.vmap(
        lambda q, k, v, l, c: attend_backward(q, k, v, l, c, allowed)
    )(queries, key_rows, value_rows, logsum, context_gradient)
    query_pull = jax.vjp(head_norm, query_pre, query_gain)[1]
    query_pre_grad, query_gain_grad = query_pull(query_grad)
    key_pull = jax.vjp(head_norm, key_pre, key_gain)[1]
    key_pre_grad, key_gain_grad = key_pull(key_grad)
    value_grad = value_grad.reshape(sequences, length, width)
    query_bias_grad = jnp.sum(query_pre_grad, axis=(0, 1))
    value_bias_grad = jnp.sum(value_grad, axis=(0, 1))
    projected_grad = jnp.concatenate([query_pre_grad, key_pre_grad, value_grad], axis=2).astype(
        jnp.bfloat16
    )
    qkv_grad = weight_grad(normed_attn, projected_grad)
    (
        proj_sum,
        qkv_sum,
        query_bias_sum,
        value_bias_sum,
        query_gain_sum,
        key_gain_sum,
        proj_bias_sum,
        up_bias_sum,
        down_bias_sum,
    ) = scatter_packed(
        (
            proj_grad,
            qkv_grad,
            query_bias_grad,
            value_bias_grad,
            query_gain_grad,
            key_gain_grad,
            proj_bias_grad,
            up_bias_grad,
            down_bias_grad,
        ),
        count,
    )
    normed_attn_grad = matmul_back(projected_grad, qkv_full)
    attn_pull = jax.vjp(modulate, input_rows, scale_attn, shift_attn)[1]
    input_part, scale_attn_grad, shift_attn_grad = attn_pull(normed_attn_grad)
    input_grad = middle_grad + input_part
    adaptive_grad = jnp.concatenate(
        [
            gamma_attn_grad,
            gamma_mlp_grad,
            scale_attn_grad,
            scale_mlp_grad,
            shift_attn_grad,
            shift_mlp_grad,
        ],
        axis=1,
    ).astype(jnp.bfloat16)
    adaptive_grad_all = nested_gather(adaptive_grad)
    ada_sum = jnp.einsum(
        "sc,sn->cn", activated_mine, adaptive_grad_all, preferred_element_type=jnp.float32
    )
    bias_share = ada_cols // count
    ada_bias_sum = jnp.sum(
        lax.dynamic_slice_in_dim(adaptive_grad_all, me * bias_share, bias_share, axis=1).astype(
            jnp.float32
        ),
        axis=0,
    )
    activated_grad_cols = jnp.einsum(
        "sn,cn->sc", adaptive_grad_all, w_ada, preferred_element_type=jnp.float32
    )
    activated_grad = lax.all_to_all(
        activated_grad_cols, AXES, split_axis=0, concat_axis=1, tiled=True
    )
    silu_pull = jax.vjp(jax.nn.silu, cond_rows)[1]
    condition_grad = silu_pull(activated_grad)[0]
    return (
        layer_output,
        input_grad,
        condition_grad,
        ada_sum,
        ada_bias_sum,
        qkv_sum,
        query_bias_sum,
        value_bias_sum,
        query_gain_sum,
        key_gain_sum,
        proj_sum,
        proj_bias_sum,
        up_sum,
        up_bias_sum,
        down_sum,
        down_bias_sum,
    )


def solution(mesh):
    row = P(AXES, None, None)
    mat = P(AXES, None)
    vec = P(AXES)
    return jax.shard_map(
        layer,
        mesh=mesh,
        in_specs=(row, mat, P(), mat, vec, mat, vec, vec, vec, vec, mat, vec, mat, vec, mat, vec, row),
        out_specs=(row, row, mat, mat, vec, mat, vec, vec, vec, vec, mat, vec, mat, vec, mat, vec),
        check_vma=False,
    )
```

```python
import jax
import jax.numpy as jnp
from jax import lax
from jax.sharding import PartitionSpec as P


HEADS = 16
HEAD_DIM = 64
SEQ_LEN = 680
AXES = ("wide", "narrow")

EPSILON = 1e-06
MASKED = -1000000000.0


def layer_norm(values):
    centred = values - jnp.mean(values, axis=-1, keepdims=True)
    return centred * lax.rsqrt(jnp.mean(centred * centred, axis=-1, keepdims=True) + EPSILON)


def modulate(values, scaling, offset):
    return layer_norm(values) * (1.0 + scaling[:, None, :]) + offset[:, None, :]


def head_norm(values, channel_gain):
    shaped = values.reshape(values.shape[0], values.shape[1], HEADS, HEAD_DIM)
    scaled = shaped * lax.rsqrt(jnp.mean(shaped * shaped, axis=-1, keepdims=True) + EPSILON)
    return scaled * channel_gain.reshape(HEADS, HEAD_DIM)


def gelu_tanh(values):
    return jax.nn.gelu(values, approximate=True)


def block_mask(scale_tokens):
    block_ends = jnp.cumsum(scale_tokens)
    places = jnp.arange(SEQ_LEN, dtype=jnp.int32)
    limits = jnp.min(
        jnp.where(block_ends[None, :] > places[:, None], block_ends[None, :], SEQ_LEN), axis=1
    )
    return places[None, :] < limits[:, None]


def matmul_rows(first_operand, second_operand):
    return jnp.einsum(
        "fyg,gq->fyq", first_operand, second_operand, preferred_element_type=jnp.float32
    )


def matmul_back(first_operand, second_operand):
    return jnp.einsum(
        "rfw,uw->rfu", first_operand, second_operand, preferred_element_type=jnp.float32
    )


def weight_grad(first_operand, second_operand):
    return jnp.einsum(
        "crk,cre->ke", first_operand, second_operand, preferred_element_type=jnp.float32
    )


def masked_scores(query_sequence, key_sequence, allowed):
    scores = jnp.einsum(
        "nkz,vkz->knv", query_sequence, key_sequence, preferred_element_type=jnp.float32
    ) * HEAD_DIM ** (-0.5)
    return jnp.where(allowed[None], scores, MASKED)


def attend_forward(query_sequence, key_sequence, value_sequence, allowed):
    scores = masked_scores(query_sequence, key_sequence, allowed)
    row_max = jnp.max(scores, axis=-1, keepdims=True)
    exponent = jnp.exp(scores - row_max)
    row_total = jnp.sum(exponent, axis=-1, keepdims=True)
    probabilities_reduced = (exponent / row_total).astype(jnp.bfloat16)
    context = jnp.einsum(
        "wcv,vwn->cwn", probabilities_reduced, value_sequence, preferred_element_type=jnp.float32
    ).astype(jnp.bfloat16)
    return (context, row_max[..., 0] + jnp.log(row_total[..., 0]))


def attend_backward(
    query_sequence, key_sequence, value_sequence, logsum, context_gradient, allowed
):
    scores = masked_scores(query_sequence, key_sequence, allowed)
    attention_probabilities = jnp.exp(scores - logsum[..., None])
    prob_grad = jnp.einsum(
        "nkz,vkz->knv", context_gradient, value_sequence, preferred_element_type=jnp.float32
    )
    value_grad = jnp.einsum(
        "fgs,gfu->sfu",
        attention_probabilities.astype(jnp.bfloat16),
        context_gradient,
        preferred_element_type=jnp.float32,
    )
    score_gradient = (
        attention_probabilities
        * (prob_grad - jnp.sum(prob_grad * attention_probabilities, axis=-1, keepdims=True))
    ).astype(jnp.bfloat16)
    query_grad = jnp.einsum(
        "wcv,vwn->cwn", score_gradient, key_sequence, preferred_element_type=jnp.float32
    ) * HEAD_DIM ** (-0.5)
    key_grad = jnp.einsum(
        "fgs,gfu->sfu", score_gradient, query_sequence, preferred_element_type=jnp.float32
    ) * HEAD_DIM ** (-0.5)
    return (query_grad, key_grad, value_grad)


def nested_gather(member):
    return lax.all_gather(
        lax.all_gather(member, "narrow", axis=0, tiled=True), "wide", axis=0, tiled=True
    )


LANES = 1024
TILE_ROWS = 16


def shard_rows(shard):
    rows, cols = shard.shape
    blocks = cols // LANES
    if blocks == 1:
        return shard
    return shard.reshape(rows, blocks, LANES).transpose(1, 0, 2).reshape(blocks * rows, LANES)


def rows_shard(piece, cols):
    blocks = cols // LANES
    if blocks == 1:
        return piece
    rows = piece.shape[0] // blocks
    return piece.reshape(blocks, rows, LANES).transpose(1, 0, 2).reshape(rows, cols)


def pad_rows(flat):
    pad = -flat.shape[1] % TILE_ROWS
    if pad:
        flat = jnp.concatenate([flat, jnp.zeros((flat.shape[0], pad, LANES), flat.dtype)], axis=1)
    return flat


def gather_packed(members, count):
    flat = pad_rows(jnp.concatenate([shard_rows(m) for m in members], axis=0)[None])
    got = lax.all_gather(flat[0], AXES, axis=0, tiled=True).reshape(count, flat.shape[1], LANES)
    out, start = [], 0
    for member in members:
        rows, cols = member.shape
        blocks = cols // LANES
        piece = got[:, start : start + blocks * rows]
        start += blocks * rows
        full = piece.reshape(count, blocks, rows, LANES).transpose(0, 2, 1, 3)
        out.append(full.reshape(count * rows, cols))
    return out


def scatter_packed(matrices, vectors, count):
    pieces = []
    for member in matrices:
        rows, cols = member.shape
        shard = member.astype(jnp.bfloat16).reshape(count, rows // count, cols)
        blocks = cols // LANES
        shard = shard.reshape(count, rows // count, blocks, LANES).transpose(0, 2, 1, 3)
        pieces.append(shard.reshape(count, blocks * rows // count, LANES))
    if vectors:
        small = jnp.concatenate([v.reshape(count, -1) for v in vectors], axis=1)
        pad = -small.shape[1] % LANES
        small = jnp.concatenate([small, jnp.zeros((count, pad), small.dtype)], axis=1)
        pieces.append(small.astype(jnp.bfloat16).reshape(count, -1, LANES))
    flat = pad_rows(jnp.concatenate(pieces, axis=1))
    flat = flat.reshape(count * flat.shape[1], LANES)
    half = lax.psum_scatter(flat, "wide", scatter_dimension=0, tiled=True)
    got = lax.psum_scatter(half, "narrow", scatter_dimension=0, tiled=True)
    got = got.astype(jnp.float32)
    out, start = [], 0
    for member in matrices:
        rows, cols = member.shape
        blocks = cols // LANES
        size = blocks * rows // count
        out.append(rows_shard(got[start : start + size], cols))
        start += size
    if vectors:
        tail = got[start:].reshape(-1)
        offset = 0
        for v in vectors:
            size = v.shape[0] // count
            out.append(tail[offset : offset + size])
            offset += size
    return out


def layer(
    inputs,
    condition,
    scale_tokens,
    w_ada,
    bias_ada,
    w_qkv,
    bias_query,
    bias_value,
    gain_query,
    gain_key,
    w_proj,
    bias_proj,
    w_up,
    bias_up,
    w_down,
    bias_down,
    cotangent,
):
    count = lax.axis_size("wide") * lax.axis_size("narrow")
    me = lax.axis_index("wide") * lax.axis_size("narrow") + lax.axis_index("narrow")
    sequences, length, width = inputs.shape
    head_shape = (sequences, length, HEADS, HEAD_DIM)
    cond_rows = condition.astype(jnp.float32)
    activated = jax.nn.silu(cond_rows).astype(jnp.bfloat16)
    vectors = (bias_ada, bias_query, bias_value, gain_query, gain_key, bias_proj, bias_up, bias_down)
    small = nested_gather(
        jnp.concatenate([activated.reshape(-1)] + list(vectors))[None, :]
    )
    activated_all = small[:, : activated.size].reshape(count * sequences, activated.shape[1])
    unpacked, start = [], activated.size
    for member in vectors:
        size = member.shape[0]
        unpacked.append(small[:, start : start + size].reshape(count * size).astype(jnp.float32))
        start += size
    ada_bias, query_bias, value_bias, query_gain, key_gain, proj_bias, up_bias, down_bias = unpacked
    qkv_full = lax.all_gather(w_qkv, AXES, axis=0, tiled=True)
    proj_full, up_full, down_full = gather_packed((w_proj, w_up, w_down), count)
    allowed = block_mask(scale_tokens)
    input_rows = inputs.astype(jnp.float32)
    ada_rows = w_ada.shape[0]
    ada_cols = w_ada.shape[1]
    activated_mine = lax.dynamic_slice_in_dim(activated_all, me * ada_rows, ada_rows, axis=1)
    ada_partial = jnp.dot(activated_mine, w_ada, preferred_element_type=jnp.float32)
    ada_parts = lax.all_to_all(
        ada_partial.reshape(count, sequences, ada_cols), AXES, split_axis=0, concat_axis=0, tiled=True
    )
    adaptive = jnp.sum(ada_parts, axis=0) + ada_bias
    gamma_attn, gamma_mlp, scale_attn, scale_mlp, shift_attn, shift_mlp = jnp.split(
        adaptive, 6, axis=1
    )
    normed_attn = modulate(input_rows, scale_attn, shift_attn).astype(jnp.bfloat16)
    projected = matmul_rows(normed_attn, qkv_full)
    query_pre = projected[..., :width] + query_bias
    key_pre = projected[..., width : 2 * width]
    queries = head_norm(query_pre, query_gain).astype(jnp.bfloat16)
    key_rows = head_norm(key_pre, key_gain).astype(jnp.bfloat16)
    value_rows = (projected[..., 2 * width :] + value_bias).astype(jnp.bfloat16).reshape(head_shape)
    context, logsum = jax.vmap(
        lambda q, k, v: attend_forward(q, k, v, allowed)
    )(queries, key_rows, value_rows)
    context = context.reshape(sequences, length, width)
    attended = matmul_rows(context, proj_full) + proj_bias
    middle = input_rows + gamma_attn[:, None, :] * attended
    normed_mlp = modulate(middle, scale_mlp, shift_mlp).astype(jnp.bfloat16)
    hidden_pre = matmul_rows(normed_mlp, up_full) + up_bias
    hidden = gelu_tanh(hidden_pre).astype(jnp.bfloat16)
    branch = matmul_rows(hidden, down_full) + down_bias
    layer_output = (middle + gamma_mlp[:, None, :] * branch).astype(jnp.bfloat16)
    upstream = cotangent.astype(jnp.float32)
    gamma_mlp_grad = jnp.sum(upstream * branch, axis=1)
    branch_grad = (upstream * gamma_mlp[:, None, :]).astype(jnp.bfloat16)
    down_grad = weight_grad(hidden, branch_grad)
    down_bias_grad = jnp.sum(branch_grad.astype(jnp.float32), axis=(0, 1))
    hidden_grad = matmul_back(branch_grad, down_full)
    gelu_pull = jax.vjp(gelu_tanh, hidden_pre)[1]
    pre_grad = gelu_pull(hidden_grad)[0].astype(jnp.bfloat16)
    up_grad = weight_grad(normed_mlp, pre_grad)
    up_bias_grad = jnp.sum(pre_grad.astype(jnp.float32), axis=(0, 1))
    normed_mlp_grad = matmul_back(pre_grad, up_full)
    mlp_pull = jax.vjp(modulate, middle, scale_mlp, shift_mlp)[1]
    middle_part, scale_mlp_grad, shift_mlp_grad = mlp_pull(normed_mlp_grad)
    middle_grad = upstream + middle_part
    gamma_attn_grad = jnp.sum(middle_grad * attended, axis=1)
    attended_grad = (middle_grad * gamma_attn[:, None, :]).astype(jnp.bfloat16)
    proj_grad = weight_grad(context, attended_grad)
    proj_bias_grad = jnp.sum(attended_grad.astype(jnp.float32), axis=(0, 1))
    down_sum, up_sum, proj_sum = scatter_packed((down_grad, up_grad, proj_grad), (), count)
    context_gradient = (
        matmul_back(attended_grad, proj_full).astype(jnp.bfloat16).reshape(head_shape)
    )
    query_grad, key_grad, value_grad = jax.vmap(
        lambda q, k, v, l, c: attend_backward(q, k, v, l, c, allowed)
    )(queries, key_rows, value_rows, logsum, context_gradient)
    query_pull = jax.vjp(head_norm, query_pre, query_gain)[1]
    query_pre_grad, query_gain_grad = query_pull(query_grad)
    key_pull = jax.vjp(head_norm, key_pre, key_gain)[1]
    key_pre_grad, key_gain_grad = key_pull(key_grad)
    value_grad = value_grad.reshape(sequences, length, width)
    query_bias_grad = jnp.sum(query_pre_grad, axis=(0, 1))
    value_bias_grad = jnp.sum(value_grad, axis=(0, 1))
    projected_grad = jnp.concatenate([query_pre_grad, key_pre_grad, value_grad], axis=2).astype(
        jnp.bfloat16
    )
    qkv_grad = weight_grad(normed_attn, projected_grad)
    (
        qkv_sum,
        query_bias_sum,
        value_bias_sum,
        query_gain_sum,
        key_gain_sum,
        proj_bias_sum,
        up_bias_sum,
        down_bias_sum,
    ) = scatter_packed(
        (qkv_grad,),
        (
            query_bias_grad,
            value_bias_grad,
            query_gain_grad,
            key_gain_grad,
            proj_bias_grad,
            up_bias_grad,
            down_bias_grad,
        ),
        count,
    )
    return tail(
        projected_grad, qkv_full, input_rows, scale_attn, shift_attn, middle_grad,
        gamma_attn_grad, gamma_mlp_grad, scale_mlp_grad, shift_mlp_grad, activated_mine,
        w_ada, cond_rows, me, count, layer_output, qkv_sum, query_bias_sum, value_bias_sum,
        query_gain_sum, key_gain_sum, proj_sum, proj_bias_sum, up_sum, up_bias_sum, down_sum,
        down_bias_sum,
    )


def tail(
    projected_grad, qkv_full, input_rows, scale_attn, shift_attn, middle_grad,
    gamma_attn_grad, gamma_mlp_grad, scale_mlp_grad, shift_mlp_grad, activated_mine,
    w_ada, cond_rows, me, count, layer_output, qkv_sum, query_bias_sum, value_bias_sum,
    query_gain_sum, key_gain_sum, proj_sum, proj_bias_sum, up_sum, up_bias_sum, down_sum,
    down_bias_sum,
):
    ada_cols = w_ada.shape[1]
    normed_attn_grad = matmul_back(projected_grad, qkv_full)
    attn_pull = jax.vjp(modulate, input_rows, scale_attn, shift_attn)[1]
    input_part, scale_attn_grad, shift_attn_grad = attn_pull(normed_attn_grad)
    input_grad = middle_grad + input_part
    adaptive_grad = jnp.concatenate(
        [
            gamma_attn_grad,
            gamma_mlp_grad,
            scale_attn_grad,
            scale_mlp_grad,
            shift_attn_grad,
            shift_mlp_grad,
        ],
        axis=1,
    ).astype(jnp.bfloat16)
    adaptive_grad_all = nested_gather(adaptive_grad)
    ada_sum = jnp.einsum(
        "sc,sn->cn", activated_mine, adaptive_grad_all, preferred_element_type=jnp.float32
    )
    bias_share = ada_cols // count
    ada_bias_sum = jnp.sum(
        lax.dynamic_slice_in_dim(adaptive_grad_all, me * bias_share, bias_share, axis=1).astype(
            jnp.float32
        ),
        axis=0,
    )
    activated_grad_cols = jnp.einsum(
        "sn,cn->sc", adaptive_grad_all, w_ada, preferred_element_type=jnp.float32
    )
    activated_grad = lax.all_to_all(
        activated_grad_cols, AXES, split_axis=0, concat_axis=1, tiled=True
    )
    silu_pull = jax.vjp(jax.nn.silu, cond_rows)[1]
    condition_grad = silu_pull(activated_grad)[0]
    return (
        layer_output,
        input_grad,
        condition_grad,
        ada_sum,
        ada_bias_sum,
        qkv_sum,
        query_bias_sum,
        value_bias_sum,
        query_gain_sum,
        key_gain_sum,
        proj_sum,
        proj_bias_sum,
        up_sum,
        up_bias_sum,
        down_sum,
        down_bias_sum,
    )


def solution(mesh):
    row = P(AXES, None, None)
    mat = P(AXES, None)
    vec = P(AXES)
    return jax.shard_map(
        layer,
        mesh=mesh,
        in_specs=(row, mat, P(), mat, vec, mat, vec, vec, vec, vec, mat, vec, mat, vec, mat, vec, row),
        out_specs=(row, row, mat, mat, vec, mat, vec, vec, vec, vec, mat, vec, mat, vec, mat, vec),
        check_vma=False,
    )
```

```python
import jax
import jax.numpy as jnp
from jax import lax
from jax.sharding import PartitionSpec as P


HEADS = 16
HEAD_DIM = 64
SEQ_LEN = 680
AXES = ("wide", "narrow")

EPSILON = 1e-06
MASKED = -1000000000.0


def layer_norm(values):
    centred = values - jnp.mean(values, axis=-1, keepdims=True)
    return centred * lax.rsqrt(jnp.mean(centred * centred, axis=-1, keepdims=True) + EPSILON)


def modulate(values, scaling, offset):
    return layer_norm(values) * (1.0 + scaling[:, None, :]) + offset[:, None, :]


def head_norm(values, channel_gain):
    shaped = values.reshape(values.shape[0], values.shape[1], HEADS, HEAD_DIM)
    scaled = shaped * lax.rsqrt(jnp.mean(shaped * shaped, axis=-1, keepdims=True) + EPSILON)
    return scaled * channel_gain.reshape(HEADS, HEAD_DIM)


def gelu_tanh(values):
    return jax.nn.gelu(values, approximate=True)


def block_mask(scale_tokens):
    block_ends = jnp.cumsum(scale_tokens)
    places = jnp.arange(SEQ_LEN, dtype=jnp.int32)
    limits = jnp.min(
        jnp.where(block_ends[None, :] > places[:, None], block_ends[None, :], SEQ_LEN), axis=1
    )
    return places[None, :] < limits[:, None]


def matmul_rows(first_operand, second_operand):
    return jnp.einsum(
        "fyg,gq->fyq", first_operand, second_operand, preferred_element_type=jnp.float32
    )


def matmul_back(first_operand, second_operand):
    return jnp.einsum(
        "rfw,uw->rfu", first_operand, second_operand, preferred_element_type=jnp.float32
    )


def weight_grad(first_operand, second_operand):
    return jnp.einsum(
        "crk,cre->ke", first_operand, second_operand, preferred_element_type=jnp.float32
    )


def masked_scores(query_sequence, key_sequence, allowed):
    scores = jnp.einsum(
        "nkz,vkz->knv", query_sequence, key_sequence, preferred_element_type=jnp.float32
    ) * HEAD_DIM ** (-0.5)
    return jnp.where(allowed[None], scores, MASKED)


def attend_forward(query_sequence, key_sequence, value_sequence, allowed):
    scores = masked_scores(query_sequence, key_sequence, allowed)
    row_max = jnp.max(scores, axis=-1, keepdims=True)
    exponent = jnp.exp(scores - row_max)
    row_total = jnp.sum(exponent, axis=-1, keepdims=True)
    probabilities_reduced = (exponent / row_total).astype(jnp.bfloat16)
    context = jnp.einsum(
        "wcv,vwn->cwn", probabilities_reduced, value_sequence, preferred_element_type=jnp.float32
    ).astype(jnp.bfloat16)
    return (context, row_max[..., 0] + jnp.log(row_total[..., 0]))


def attend_backward(
    query_sequence, key_sequence, value_sequence, logsum, context_gradient, allowed
):
    scores = masked_scores(query_sequence, key_sequence, allowed)
    attention_probabilities = jnp.exp(scores - logsum[..., None])
    prob_grad = jnp.einsum(
        "nkz,vkz->knv", context_gradient, value_sequence, preferred_element_type=jnp.float32
    )
    value_grad = jnp.einsum(
        "fgs,gfu->sfu",
        attention_probabilities.astype(jnp.bfloat16),
        context_gradient,
        preferred_element_type=jnp.float32,
    )
    score_gradient = (
        attention_probabilities
        * (prob_grad - jnp.sum(prob_grad * attention_probabilities, axis=-1, keepdims=True))
    ).astype(jnp.bfloat16)
    query_grad = jnp.einsum(
        "wcv,vwn->cwn", score_gradient, key_sequence, preferred_element_type=jnp.float32
    ) * HEAD_DIM ** (-0.5)
    key_grad = jnp.einsum(
        "fgs,gfu->sfu", score_gradient, query_sequence, preferred_element_type=jnp.float32
    ) * HEAD_DIM ** (-0.5)
    return (query_grad, key_grad, value_grad)


def nested_gather(member):
    return lax.all_gather(
        lax.all_gather(member, "narrow", axis=0, tiled=True), "wide", axis=0, tiled=True
    )


LANES = 1024
TILE_ROWS = 16


def shard_rows(shard):
    rows, cols = shard.shape
    blocks = cols // LANES
    if blocks == 1:
        return shard
    return shard.reshape(rows, blocks, LANES).transpose(1, 0, 2).reshape(blocks * rows, LANES)


def rows_shard(piece, cols):
    blocks = cols // LANES
    if blocks == 1:
        return piece
    rows = piece.shape[0] // blocks
    return piece.reshape(blocks, rows, LANES).transpose(1, 0, 2).reshape(rows, cols)


def pad_rows(flat):
    pad = -flat.shape[1] % TILE_ROWS
    if pad:
        flat = jnp.concatenate([flat, jnp.zeros((flat.shape[0], pad, LANES), flat.dtype)], axis=1)
    return flat


def gather_packed(members, count):
    flat = pad_rows(jnp.concatenate([shard_rows(m) for m in members], axis=0)[None])
    got = lax.all_gather(flat[0], AXES, axis=0, tiled=True).reshape(count, flat.shape[1], LANES)
    out, start = [], 0
    for member in members:
        rows, cols = member.shape
        blocks = cols // LANES
        piece = got[:, start : start + blocks * rows]
        start += blocks * rows
        full = piece.reshape(count, blocks, rows, LANES).transpose(0, 2, 1, 3)
        out.append(full.reshape(count * rows, cols))
    return out


def narrow_sum(half):
    size = lax.axis_size("narrow")
    if size != 2:
        return lax.psum_scatter(half, "narrow", scatter_dimension=0, tiled=True).astype(jnp.float32)
    rows = half.shape[0] // 2
    here = lax.axis_index("narrow")
    keep = lax.dynamic_slice_in_dim(half, here * rows, rows, axis=0)
    send = lax.dynamic_slice_in_dim(half, (1 - here) * rows, rows, axis=0)
    got = lax.ppermute(send, "narrow", [(0, 1), (1, 0)])
    return keep.astype(jnp.float32) + got.astype(jnp.float32)


def scatter_packed(matrices, vectors, count):
    pieces = []
    for member in matrices:
        rows, cols = member.shape
        shard = member.astype(jnp.bfloat16).reshape(count, rows // count, cols)
        blocks = cols // LANES
        shard = shard.reshape(count, rows // count, blocks, LANES).transpose(0, 2, 1, 3)
        pieces.append(shard.reshape(count, blocks * rows // count, LANES))
    if vectors:
        small = jnp.concatenate([v.reshape(count, -1) for v in vectors], axis=1)
        pad = -small.shape[1] % LANES
        small = jnp.concatenate([small, jnp.zeros((count, pad), small.dtype)], axis=1)
        pieces.append(small.astype(jnp.bfloat16).reshape(count, -1, LANES))
    flat = pad_rows(jnp.concatenate(pieces, axis=1))
    flat = flat.reshape(count * flat.shape[1], LANES)
    half = lax.psum_scatter(flat, "wide", scatter_dimension=0, tiled=True)
    got = narrow_sum(half)
    out, start = [], 0
    for member in matrices:
        rows, cols = member.shape
        blocks = cols // LANES
        size = blocks * rows // count
        out.append(rows_shard(got[start : start + size], cols))
        start += size
    if vectors:
        tail = got[start:].reshape(-1)
        offset = 0
        for v in vectors:
            size = v.shape[0] // count
            out.append(tail[offset : offset + size])
            offset += size
    return out


def layer(
    inputs,
    condition,
    scale_tokens,
    w_ada,
    bias_ada,
    w_qkv,
    bias_query,
    bias_value,
    gain_query,
    gain_key,
    w_proj,
    bias_proj,
    w_up,
    bias_up,
    w_down,
    bias_down,
    cotangent,
):
    count = lax.axis_size("wide") * lax.axis_size("narrow")
    me = lax.axis_index("wide") * lax.axis_size("narrow") + lax.axis_index("narrow")
    sequences, length, width = inputs.shape
    head_shape = (sequences, length, HEADS, HEAD_DIM)
    cond_rows = condition.astype(jnp.float32)
    activated = jax.nn.silu(cond_rows).astype(jnp.bfloat16)
    vectors = (bias_ada, bias_query, bias_value, gain_query, gain_key, bias_proj, bias_up, bias_down)
    small = nested_gather(
        jnp.concatenate([activated.reshape(-1)] + list(vectors))[None, :]
    )
    activated_all = small[:, : activated.size].reshape(count * sequences, activated.shape[1])
    unpacked, start = [], activated.size
    for member in vectors:
        size = member.shape[0]
        unpacked.append(small[:, start : start + size].reshape(count * size).astype(jnp.float32))
        start += size
    ada_bias, query_bias, value_bias, query_gain, key_gain, proj_bias, up_bias, down_bias = unpacked
    qkv_full = lax.all_gather(w_qkv, AXES, axis=0, tiled=True)
    proj_full, up_full, down_full = gather_packed((w_proj, w_up, w_down), count)
    allowed = block_mask(scale_tokens)
    input_rows = inputs.astype(jnp.float32)
    ada_rows = w_ada.shape[0]
    ada_cols = w_ada.shape[1]
    activated_mine = lax.dynamic_slice_in_dim(activated_all, me * ada_rows, ada_rows, axis=1)
    ada_partial = jnp.dot(activated_mine, w_ada, preferred_element_type=jnp.float32)
    ada_parts = lax.all_to_all(
        ada_partial.reshape(count, sequences, ada_cols), AXES, split_axis=0, concat_axis=0, tiled=True
    )
    adaptive = jnp.sum(ada_parts, axis=0) + ada_bias
    gamma_attn, gamma_mlp, scale_attn, scale_mlp, shift_attn, shift_mlp = jnp.split(
        adaptive, 6, axis=1
    )
    normed_attn = modulate(input_rows, scale_attn, shift_attn).astype(jnp.bfloat16)
    projected = matmul_rows(normed_attn, qkv_full)
    query_pre = projected[..., :width] + query_bias
    key_pre = projected[..., width : 2 * width]
    queries = head_norm(query_pre, query_gain).astype(jnp.bfloat16)
    key_rows = head_norm(key_pre, key_gain).astype(jnp.bfloat16)
    value_rows = (projected[..., 2 * width :] + value_bias).astype(jnp.bfloat16).reshape(head_shape)
    context, logsum = jax.vmap(
        lambda q, k, v: attend_forward(q, k, v, allowed)
    )(queries, key_rows, value_rows)
    context = context.reshape(sequences, length, width)
    attended = matmul_rows(context, proj_full) + proj_bias
    middle = input_rows + gamma_attn[:, None, :] * attended
    normed_mlp = modulate(middle, scale_mlp, shift_mlp).astype(jnp.bfloat16)
    hidden_pre = matmul_rows(normed_mlp, up_full) + up_bias
    hidden = gelu_tanh(hidden_pre).astype(jnp.bfloat16)
    branch = matmul_rows(hidden, down_full) + down_bias
    layer_output = (middle + gamma_mlp[:, None, :] * branch).astype(jnp.bfloat16)
    upstream = cotangent.astype(jnp.float32)
    gamma_mlp_grad = jnp.sum(upstream * branch, axis=1)
    branch_grad = (upstream * gamma_mlp[:, None, :]).astype(jnp.bfloat16)
    down_grad = weight_grad(hidden, branch_grad)
    down_bias_grad = jnp.sum(branch_grad.astype(jnp.float32), axis=(0, 1))
    hidden_grad = matmul_back(branch_grad, down_full)
    gelu_pull = jax.vjp(gelu_tanh, hidden_pre)[1]
    pre_grad = gelu_pull(hidden_grad)[0].astype(jnp.bfloat16)
    up_grad = weight_grad(normed_mlp, pre_grad)
    up_bias_grad = jnp.sum(pre_grad.astype(jnp.float32), axis=(0, 1))
    normed_mlp_grad = matmul_back(pre_grad, up_full)
    mlp_pull = jax.vjp(modulate, middle, scale_mlp, shift_mlp)[1]
    middle_part, scale_mlp_grad, shift_mlp_grad = mlp_pull(normed_mlp_grad)
    middle_grad = upstream + middle_part
    gamma_attn_grad = jnp.sum(middle_grad * attended, axis=1)
    attended_grad = (middle_grad * gamma_attn[:, None, :]).astype(jnp.bfloat16)
    proj_grad = weight_grad(context, attended_grad)
    proj_bias_grad = jnp.sum(attended_grad.astype(jnp.float32), axis=(0, 1))
    down_sum, up_sum, proj_sum = scatter_packed((down_grad, up_grad, proj_grad), (), count)
    context_gradient = (
        matmul_back(attended_grad, proj_full).astype(jnp.bfloat16).reshape(head_shape)
    )
    query_grad, key_grad, value_grad = jax.vmap(
        lambda q, k, v, l, c: attend_backward(q, k, v, l, c, allowed)
    )(queries, key_rows, value_rows, logsum, context_gradient)
    query_pull = jax.vjp(head_norm, query_pre, query_gain)[1]
    query_pre_grad, query_gain_grad = query_pull(query_grad)
    key_pull = jax.vjp(head_norm, key_pre, key_gain)[1]
    key_pre_grad, key_gain_grad = key_pull(key_grad)
    value_grad = value_grad.reshape(sequences, length, width)
    query_bias_grad = jnp.sum(query_pre_grad, axis=(0, 1))
    value_bias_grad = jnp.sum(value_grad, axis=(0, 1))
    projected_grad = jnp.concatenate([query_pre_grad, key_pre_grad, value_grad], axis=2).astype(
        jnp.bfloat16
    )
    qkv_grad = weight_grad(normed_attn, projected_grad)
    (
        qkv_sum,
        query_bias_sum,
        value_bias_sum,
        query_gain_sum,
        key_gain_sum,
        proj_bias_sum,
        up_bias_sum,
        down_bias_sum,
    ) = scatter_packed(
        (qkv_grad,),
        (
            query_bias_grad,
            value_bias_grad,
            query_gain_grad,
            key_gain_grad,
            proj_bias_grad,
            up_bias_grad,
            down_bias_grad,
        ),
        count,
    )
    return tail(
        projected_grad, qkv_full, input_rows, scale_attn, shift_attn, middle_grad,
        gamma_attn_grad, gamma_mlp_grad, scale_mlp_grad, shift_mlp_grad, activated_mine,
        w_ada, cond_rows, me, count, layer_output, qkv_sum, query_bias_sum, value_bias_sum,
        query_gain_sum, key_gain_sum, proj_sum, proj_bias_sum, up_sum, up_bias_sum, down_sum,
        down_bias_sum,
    )


def tail(
    projected_grad, qkv_full, input_rows, scale_attn, shift_attn, middle_grad,
    gamma_attn_grad, gamma_mlp_grad, scale_mlp_grad, shift_mlp_grad, activated_mine,
    w_ada, cond_rows, me, count, layer_output, qkv_sum, query_bias_sum, value_bias_sum,
    query_gain_sum, key_gain_sum, proj_sum, proj_bias_sum, up_sum, up_bias_sum, down_sum,
    down_bias_sum,
):
    ada_cols = w_ada.shape[1]
    normed_attn_grad = matmul_back(projected_grad, qkv_full)
    attn_pull = jax.vjp(modulate, input_rows, scale_attn, shift_attn)[1]
    input_part, scale_attn_grad, shift_attn_grad = attn_pull(normed_attn_grad)
    input_grad = middle_grad + input_part
    adaptive_grad = jnp.concatenate(
        [
            gamma_attn_grad,
            gamma_mlp_grad,
            scale_attn_grad,
            scale_mlp_grad,
            shift_attn_grad,
            shift_mlp_grad,
        ],
        axis=1,
    ).astype(jnp.bfloat16)
    adaptive_grad_all = nested_gather(adaptive_grad)
    ada_sum = jnp.einsum(
        "sc,sn->cn", activated_mine, adaptive_grad_all, preferred_element_type=jnp.float32
    )
    bias_share = ada_cols // count
    ada_bias_sum = jnp.sum(
        lax.dynamic_slice_in_dim(adaptive_grad_all, me * bias_share, bias_share, axis=1).astype(
            jnp.float32
        ),
        axis=0,
    )
    activated_grad_cols = jnp.einsum(
        "sn,cn->sc", adaptive_grad_all, w_ada, preferred_element_type=jnp.float32
    )
    activated_grad = lax.all_to_all(
        activated_grad_cols, AXES, split_axis=0, concat_axis=1, tiled=True
    )
    silu_pull = jax.vjp(jax.nn.silu, cond_rows)[1]
    condition_grad = silu_pull(activated_grad)[0]
    return (
        layer_output,
        input_grad,
        condition_grad,
        ada_sum,
        ada_bias_sum,
        qkv_sum,
        query_bias_sum,
        value_bias_sum,
        query_gain_sum,
        key_gain_sum,
        proj_sum,
        proj_bias_sum,
        up_sum,
        up_bias_sum,
        down_sum,
        down_bias_sum,
    )


def solution(mesh):
    row = P(AXES, None, None)
    mat = P(AXES, None)
    vec = P(AXES)
    return jax.shard_map(
        layer,
        mesh=mesh,
        in_specs=(row, mat, P(), mat, vec, mat, vec, vec, vec, vec, mat, vec, mat, vec, mat, vec, row),
        out_specs=(row, row, mat, mat, vec, mat, vec, vec, vec, vec, mat, vec, mat, vec, mat, vec),
        check_vma=False,
    )
```

```python
import jax
import jax.numpy as jnp
from jax import lax
from jax.sharding import PartitionSpec as P


HEADS = 16
HEAD_DIM = 64
SEQ_LEN = 680
AXES = ("wide", "narrow")

EPSILON = 1e-06
MASKED = -1000000000.0


def layer_norm(values):
    centred = values - jnp.mean(values, axis=-1, keepdims=True)
    return centred * lax.rsqrt(jnp.mean(centred * centred, axis=-1, keepdims=True) + EPSILON)


def modulate(values, scaling, offset):
    return layer_norm(values) * (1.0 + scaling[:, None, :]) + offset[:, None, :]


def head_norm(values, channel_gain):
    shaped = values.reshape(values.shape[0], values.shape[1], HEADS, HEAD_DIM)
    scaled = shaped * lax.rsqrt(jnp.mean(shaped * shaped, axis=-1, keepdims=True) + EPSILON)
    return scaled * channel_gain.reshape(HEADS, HEAD_DIM)


def gelu_tanh(values):
    return jax.nn.gelu(values, approximate=True)


def block_mask(scale_tokens):
    block_ends = jnp.cumsum(scale_tokens)
    places = jnp.arange(SEQ_LEN, dtype=jnp.int32)
    limits = jnp.min(
        jnp.where(block_ends[None, :] > places[:, None], block_ends[None, :], SEQ_LEN), axis=1
    )
    return places[None, :] < limits[:, None]


def matmul_rows(first_operand, second_operand):
    return jnp.einsum(
        "fyg,gq->fyq", first_operand, second_operand, preferred_element_type=jnp.float32
    )


def matmul_back(first_operand, second_operand):
    return jnp.einsum(
        "rfw,uw->rfu", first_operand, second_operand, preferred_element_type=jnp.float32
    )


def weight_grad(first_operand, second_operand):
    return jnp.einsum(
        "crk,cre->ke", first_operand, second_operand, preferred_element_type=jnp.float32
    )


def masked_scores(query_sequence, key_sequence, allowed):
    scores = jnp.einsum(
        "nkz,vkz->knv", query_sequence, key_sequence, preferred_element_type=jnp.float32
    ) * HEAD_DIM ** (-0.5)
    return jnp.where(allowed[None], scores, MASKED)


def attend_forward(query_sequence, key_sequence, value_sequence, allowed):
    scores = masked_scores(query_sequence, key_sequence, allowed)
    row_max = jnp.max(scores, axis=-1, keepdims=True)
    exponent = jnp.exp(scores - row_max)
    row_total = jnp.sum(exponent, axis=-1, keepdims=True)
    probabilities_reduced = (exponent / row_total).astype(jnp.bfloat16)
    context = jnp.einsum(
        "wcv,vwn->cwn", probabilities_reduced, value_sequence, preferred_element_type=jnp.float32
    ).astype(jnp.bfloat16)
    return (context, row_max[..., 0] + jnp.log(row_total[..., 0]))


def attend_backward(
    query_sequence, key_sequence, value_sequence, logsum, context_gradient, allowed
):
    scores = masked_scores(query_sequence, key_sequence, allowed)
    attention_probabilities = jnp.exp(scores - logsum[..., None])
    prob_grad = jnp.einsum(
        "nkz,vkz->knv", context_gradient, value_sequence, preferred_element_type=jnp.float32
    )
    value_grad = jnp.einsum(
        "fgs,gfu->sfu",
        attention_probabilities.astype(jnp.bfloat16),
        context_gradient,
        preferred_element_type=jnp.float32,
    )
    score_gradient = (
        attention_probabilities
        * (prob_grad - jnp.sum(prob_grad * attention_probabilities, axis=-1, keepdims=True))
    ).astype(jnp.bfloat16)
    query_grad = jnp.einsum(
        "wcv,vwn->cwn", score_gradient, key_sequence, preferred_element_type=jnp.float32
    ) * HEAD_DIM ** (-0.5)
    key_grad = jnp.einsum(
        "fgs,gfu->sfu", score_gradient, query_sequence, preferred_element_type=jnp.float32
    ) * HEAD_DIM ** (-0.5)
    return (query_grad, key_grad, value_grad)


def nested_gather(member):
    return lax.all_gather(
        lax.all_gather(member, "narrow", axis=0, tiled=True), "wide", axis=0, tiled=True
    )


LANES = 1024
TILE_ROWS = 16


def shard_rows(shard):
    rows, cols = shard.shape
    blocks = cols // LANES
    if blocks == 1:
        return shard
    return shard.reshape(rows, blocks, LANES).transpose(1, 0, 2).reshape(blocks * rows, LANES)


def rows_shard(piece, cols):
    blocks = cols // LANES
    if blocks == 1:
        return piece
    rows = piece.shape[0] // blocks
    return piece.reshape(blocks, rows, LANES).transpose(1, 0, 2).reshape(rows, cols)


def pad_rows(flat):
    pad = -flat.shape[1] % TILE_ROWS
    if pad:
        flat = jnp.concatenate([flat, jnp.zeros((flat.shape[0], pad, LANES), flat.dtype)], axis=1)
    return flat


def gather_packed(members, count):
    flat = pad_rows(jnp.concatenate([shard_rows(m) for m in members], axis=0)[None])
    got = lax.all_gather(flat[0], AXES, axis=0, tiled=True).reshape(count, flat.shape[1], LANES)
    out, start = [], 0
    for member in members:
        rows, cols = member.shape
        blocks = cols // LANES
        piece = got[:, start : start + blocks * rows]
        start += blocks * rows
        full = piece.reshape(count, blocks, rows, LANES).transpose(0, 2, 1, 3)
        out.append(full.reshape(count * rows, cols))
    return out


def narrow_sum(half):
    size = lax.axis_size("narrow")
    if size != 2:
        return lax.psum_scatter(half, "narrow", scatter_dimension=0, tiled=True).astype(jnp.float32)
    rows = half.shape[0] // 2
    here = lax.axis_index("narrow")
    keep = lax.dynamic_slice_in_dim(half, here * rows, rows, axis=0)
    send = lax.dynamic_slice_in_dim(half, (1 - here) * rows, rows, axis=0)
    got = lax.ppermute(send, "narrow", [(0, 1), (1, 0)])
    return keep.astype(jnp.float32) + got.astype(jnp.float32)


def scatter_packed(matrices, vectors, count):
    pieces = []
    for member in matrices:
        rows, cols = member.shape
        shard = member.astype(jnp.bfloat16).reshape(count, rows // count, cols)
        blocks = cols // LANES
        shard = shard.reshape(count, rows // count, blocks, LANES).transpose(0, 2, 1, 3)
        pieces.append(shard.reshape(count, blocks * rows // count, LANES))
    if vectors:
        small = jnp.concatenate([v.reshape(count, -1) for v in vectors], axis=1)
        pad = -small.shape[1] % LANES
        small = jnp.concatenate([small, jnp.zeros((count, pad), small.dtype)], axis=1)
        pieces.append(small.astype(jnp.bfloat16).reshape(count, -1, LANES))
    flat = pad_rows(jnp.concatenate(pieces, axis=1))
    flat = flat.reshape(count * flat.shape[1], LANES)
    half = lax.psum_scatter(flat, "wide", scatter_dimension=0, tiled=True)
    got = narrow_sum(half)
    out, start = [], 0
    for member in matrices:
        rows, cols = member.shape
        blocks = cols // LANES
        size = blocks * rows // count
        out.append(rows_shard(got[start : start + size], cols))
        start += size
    if vectors:
        tail = got[start:].reshape(-1)
        offset = 0
        for v in vectors:
            size = v.shape[0] // count
            out.append(tail[offset : offset + size])
            offset += size
    return out


def layer(
    inputs,
    condition,
    scale_tokens,
    w_ada,
    bias_ada,
    w_qkv,
    bias_query,
    bias_value,
    gain_query,
    gain_key,
    w_proj,
    bias_proj,
    w_up,
    bias_up,
    w_down,
    bias_down,
    cotangent,
):
    count = lax.axis_size("wide") * lax.axis_size("narrow")
    me = lax.axis_index("wide") * lax.axis_size("narrow") + lax.axis_index("narrow")
    sequences, length, width = inputs.shape
    head_shape = (sequences, length, HEADS, HEAD_DIM)
    cond_rows = condition.astype(jnp.float32)
    activated = jax.nn.silu(cond_rows).astype(jnp.bfloat16)
    vectors = (bias_ada, bias_query, bias_value, gain_query, gain_key, bias_proj, bias_up, bias_down)
    small = nested_gather(
        jnp.concatenate([activated.reshape(-1)] + list(vectors))[None, :]
    )
    activated_all = small[:, : activated.size].reshape(count * sequences, activated.shape[1])
    unpacked, start = [], activated.size
    for member in vectors:
        size = member.shape[0]
        unpacked.append(small[:, start : start + size].reshape(count * size).astype(jnp.float32))
        start += size
    ada_bias, query_bias, value_bias, query_gain, key_gain, proj_bias, up_bias, down_bias = unpacked
    qkv_full = lax.all_gather(w_qkv, AXES, axis=0, tiled=True)
    proj_full, up_full, down_full = gather_packed((w_proj, w_up, w_down), count)
    allowed = block_mask(scale_tokens)
    input_rows = inputs.astype(jnp.float32)
    ada_rows = w_ada.shape[0]
    ada_cols = w_ada.shape[1]
    activated_mine = lax.dynamic_slice_in_dim(activated_all, me * ada_rows, ada_rows, axis=1)
    ada_partial = jnp.dot(activated_mine, w_ada, preferred_element_type=jnp.float32)
    ada_parts = lax.all_to_all(
        ada_partial.reshape(count, sequences, ada_cols), AXES, split_axis=0, concat_axis=0, tiled=True
    )
    adaptive = jnp.sum(ada_parts, axis=0) + ada_bias
    gamma_attn, gamma_mlp, scale_attn, scale_mlp, shift_attn, shift_mlp = jnp.split(
        adaptive, 6, axis=1
    )
    normed_attn = modulate(input_rows, scale_attn, shift_attn).astype(jnp.bfloat16)
    projected = matmul_rows(normed_attn, qkv_full)
    query_pre = projected[..., :width] + query_bias
    key_pre = projected[..., width : 2 * width]
    queries = head_norm(query_pre, query_gain).astype(jnp.bfloat16)
    key_rows = head_norm(key_pre, key_gain).astype(jnp.bfloat16)
    value_rows = (projected[..., 2 * width :] + value_bias).astype(jnp.bfloat16).reshape(head_shape)
    context, logsum = jax.vmap(
        lambda q, k, v: attend_forward(q, k, v, allowed)
    )(queries, key_rows, value_rows)
    context = context.reshape(sequences, length, width)
    attended = matmul_rows(context, proj_full) + proj_bias
    middle = input_rows + gamma_attn[:, None, :] * attended
    normed_mlp = modulate(middle, scale_mlp, shift_mlp).astype(jnp.bfloat16)
    hidden_pre = matmul_rows(normed_mlp, up_full) + up_bias
    hidden = gelu_tanh(hidden_pre).astype(jnp.bfloat16)
    branch = matmul_rows(hidden, down_full) + down_bias
    layer_output = (middle + gamma_mlp[:, None, :] * branch).astype(jnp.bfloat16)
    upstream = cotangent.astype(jnp.float32)
    gamma_mlp_grad = jnp.sum(upstream * branch, axis=1)
    branch_grad = (upstream * gamma_mlp[:, None, :]).astype(jnp.bfloat16)
    down_grad = weight_grad(hidden, branch_grad)
    (down_sum,) = scatter_packed((down_grad,), (), count)
    down_bias_grad = jnp.sum(branch_grad.astype(jnp.float32), axis=(0, 1))
    return mlp_back(
        branch_grad, down_full, hidden_pre, normed_mlp, up_full, middle, scale_mlp, shift_mlp,
        upstream, attended, gamma_attn, context, proj_full, head_shape, queries, key_rows,
        value_rows, logsum, allowed, query_pre, query_gain, key_pre, key_gain, sequences,
        length, width, normed_attn, qkv_full, input_rows, scale_attn, shift_attn,
        gamma_mlp_grad, activated_mine, w_ada, cond_rows, me, count, layer_output,
        down_sum, down_bias_grad,
    )


def mlp_back(
    branch_grad, down_full, hidden_pre, normed_mlp, up_full, middle, scale_mlp, shift_mlp,
    upstream, attended, gamma_attn, context, proj_full, head_shape, queries, key_rows,
    value_rows, logsum, allowed, query_pre, query_gain, key_pre, key_gain, sequences,
    length, width, normed_attn, qkv_full, input_rows, scale_attn, shift_attn,
    gamma_mlp_grad, activated_mine, w_ada, cond_rows, me, count, layer_output,
    down_sum, down_bias_grad,
):
    hidden_grad = matmul_back(branch_grad, down_full)
    gelu_pull = jax.vjp(gelu_tanh, hidden_pre)[1]
    pre_grad = gelu_pull(hidden_grad)[0].astype(jnp.bfloat16)
    up_grad = weight_grad(normed_mlp, pre_grad)
    up_bias_grad = jnp.sum(pre_grad.astype(jnp.float32), axis=(0, 1))
    normed_mlp_grad = matmul_back(pre_grad, up_full)
    mlp_pull = jax.vjp(modulate, middle, scale_mlp, shift_mlp)[1]
    middle_part, scale_mlp_grad, shift_mlp_grad = mlp_pull(normed_mlp_grad)
    middle_grad = upstream + middle_part
    gamma_attn_grad = jnp.sum(middle_grad * attended, axis=1)
    attended_grad = (middle_grad * gamma_attn[:, None, :]).astype(jnp.bfloat16)
    proj_grad = weight_grad(context, attended_grad)
    proj_bias_grad = jnp.sum(attended_grad.astype(jnp.float32), axis=(0, 1))
    up_sum, proj_sum = scatter_packed((up_grad, proj_grad), (), count)
    context_gradient = (
        matmul_back(attended_grad, proj_full).astype(jnp.bfloat16).reshape(head_shape)
    )
    query_grad, key_grad, value_grad = jax.vmap(
        lambda q, k, v, l, c: attend_backward(q, k, v, l, c, allowed)
    )(queries, key_rows, value_rows, logsum, context_gradient)
    query_pull = jax.vjp(head_norm, query_pre, query_gain)[1]
    query_pre_grad, query_gain_grad = query_pull(query_grad)
    key_pull = jax.vjp(head_norm, key_pre, key_gain)[1]
    key_pre_grad, key_gain_grad = key_pull(key_grad)
    value_grad = value_grad.reshape(sequences, length, width)
    query_bias_grad = jnp.sum(query_pre_grad, axis=(0, 1))
    value_bias_grad = jnp.sum(value_grad, axis=(0, 1))
    projected_grad = jnp.concatenate([query_pre_grad, key_pre_grad, value_grad], axis=2).astype(
        jnp.bfloat16
    )
    qkv_grad = weight_grad(normed_attn, projected_grad)
    (
        qkv_sum,
        query_bias_sum,
        value_bias_sum,
        query_gain_sum,
        key_gain_sum,
        proj_bias_sum,
        up_bias_sum,
        down_bias_sum,
    ) = scatter_packed(
        (qkv_grad,),
        (
            query_bias_grad,
            value_bias_grad,
            query_gain_grad,
            key_gain_grad,
            proj_bias_grad,
            up_bias_grad,
            down_bias_grad,
        ),
        count,
    )
    return tail(
        projected_grad, qkv_full, input_rows, scale_attn, shift_attn, middle_grad,
        gamma_attn_grad, gamma_mlp_grad, scale_mlp_grad, shift_mlp_grad, activated_mine,
        w_ada, cond_rows, me, count, layer_output, qkv_sum, query_bias_sum, value_bias_sum,
        query_gain_sum, key_gain_sum, proj_sum, proj_bias_sum, up_sum, up_bias_sum, down_sum,
        down_bias_sum,
    )


def tail(
    projected_grad, qkv_full, input_rows, scale_attn, shift_attn, middle_grad,
    gamma_attn_grad, gamma_mlp_grad, scale_mlp_grad, shift_mlp_grad, activated_mine,
    w_ada, cond_rows, me, count, layer_output, qkv_sum, query_bias_sum, value_bias_sum,
    query_gain_sum, key_gain_sum, proj_sum, proj_bias_sum, up_sum, up_bias_sum, down_sum,
    down_bias_sum,
):
    ada_cols = w_ada.shape[1]
    normed_attn_grad = matmul_back(projected_grad, qkv_full)
    attn_pull = jax.vjp(modulate, input_rows, scale_attn, shift_attn)[1]
    input_part, scale_attn_grad, shift_attn_grad = attn_pull(normed_attn_grad)
    input_grad = middle_grad + input_part
    adaptive_grad = jnp.concatenate(
        [
            gamma_attn_grad,
            gamma_mlp_grad,
            scale_attn_grad,
            scale_mlp_grad,
            shift_attn_grad,
            shift_mlp_grad,
        ],
        axis=1,
    ).astype(jnp.bfloat16)
    adaptive_grad_all = nested_gather(adaptive_grad)
    ada_sum = jnp.einsum(
        "sc,sn->cn", activated_mine, adaptive_grad_all, preferred_element_type=jnp.float32
    )
    bias_share = ada_cols // count
    ada_bias_sum = jnp.sum(
        lax.dynamic_slice_in_dim(adaptive_grad_all, me * bias_share, bias_share, axis=1).astype(
            jnp.float32
        ),
        axis=0,
    )
    activated_grad_cols = jnp.einsum(
        "sn,cn->sc", adaptive_grad_all, w_ada, preferred_element_type=jnp.float32
    )
    activated_grad = lax.all_to_all(
        activated_grad_cols, AXES, split_axis=0, concat_axis=1, tiled=True
    )
    silu_pull = jax.vjp(jax.nn.silu, cond_rows)[1]
    condition_grad = silu_pull(activated_grad)[0]
    return (
        layer_output,
        input_grad,
        condition_grad,
        ada_sum,
        ada_bias_sum,
        qkv_sum,
        query_bias_sum,
        value_bias_sum,
        query_gain_sum,
        key_gain_sum,
        proj_sum,
        proj_bias_sum,
        up_sum,
        up_bias_sum,
        down_sum,
        down_bias_sum,
    )


def solution(mesh):
    row = P(AXES, None, None)
    mat = P(AXES, None)
    vec = P(AXES)
    return jax.shard_map(
        layer,
        mesh=mesh,
        in_specs=(row, mat, P(), mat, vec, mat, vec, vec, vec, vec, mat, vec, mat, vec, mat, vec, row),
        out_specs=(row, row, mat, mat, vec, mat, vec, vec, vec, vec, mat, vec, mat, vec, mat, vec),
        check_vma=False,
    )
```

```python
import jax
import jax.numpy as jnp
from jax import lax
from jax.sharding import PartitionSpec as P


HEADS = 16
HEAD_DIM = 64
SEQ_LEN = 680
AXES = ("wide", "narrow")

EPSILON = 1e-06
MASKED = -1000000000.0


def layer_norm(values):
    centred = values - jnp.mean(values, axis=-1, keepdims=True)
    return centred * lax.rsqrt(jnp.mean(centred * centred, axis=-1, keepdims=True) + EPSILON)


def modulate(values, scaling, offset):
    return layer_norm(values) * (1.0 + scaling[:, None, :]) + offset[:, None, :]


def head_norm(values, channel_gain):
    shaped = values.reshape(values.shape[0], values.shape[1], HEADS, HEAD_DIM)
    scaled = shaped * lax.rsqrt(jnp.mean(shaped * shaped, axis=-1, keepdims=True) + EPSILON)
    return scaled * channel_gain.reshape(HEADS, HEAD_DIM)


def gelu_tanh(values):
    return jax.nn.gelu(values, approximate=True)


def block_mask(scale_tokens):
    block_ends = jnp.cumsum(scale_tokens)
    places = jnp.arange(SEQ_LEN, dtype=jnp.int32)
    limits = jnp.min(
        jnp.where(block_ends[None, :] > places[:, None], block_ends[None, :], SEQ_LEN), axis=1
    )
    return places[None, :] < limits[:, None]


def matmul_rows(first_operand, second_operand):
    return jnp.einsum(
        "fyg,gq->fyq", first_operand, second_operand, preferred_element_type=jnp.float32
    )


def matmul_back(first_operand, second_operand):
    return jnp.einsum(
        "rfw,uw->rfu", first_operand, second_operand, preferred_element_type=jnp.float32
    )


def weight_grad(first_operand, second_operand):
    return jnp.einsum(
        "crk,cre->ke", first_operand, second_operand, preferred_element_type=jnp.float32
    )


def masked_scores(query_sequence, key_sequence, allowed):
    scores = jnp.einsum(
        "nkz,vkz->knv", query_sequence, key_sequence, preferred_element_type=jnp.float32
    ) * HEAD_DIM ** (-0.5)
    return jnp.where(allowed[None], scores, MASKED)


def attend_forward(query_sequence, key_sequence, value_sequence, allowed):
    scores = masked_scores(query_sequence, key_sequence, allowed)
    row_max = jnp.max(scores, axis=-1, keepdims=True)
    exponent = jnp.exp(scores - row_max)
    row_total = jnp.sum(exponent, axis=-1, keepdims=True)
    probabilities_reduced = (exponent / row_total).astype(jnp.bfloat16)
    context = jnp.einsum(
        "wcv,vwn->cwn", probabilities_reduced, value_sequence, preferred_element_type=jnp.float32
    ).astype(jnp.bfloat16)
    return (context, row_max[..., 0] + jnp.log(row_total[..., 0]))


def attend_backward(
    query_sequence, key_sequence, value_sequence, logsum, context_gradient, allowed
):
    scores = masked_scores(query_sequence, key_sequence, allowed)
    attention_probabilities = jnp.exp(scores - logsum[..., None])
    prob_grad = jnp.einsum(
        "nkz,vkz->knv", context_gradient, value_sequence, preferred_element_type=jnp.float32
    )
    value_grad = jnp.einsum(
        "fgs,gfu->sfu",
        attention_probabilities.astype(jnp.bfloat16),
        context_gradient,
        preferred_element_type=jnp.float32,
    )
    score_gradient = (
        attention_probabilities
        * (prob_grad - jnp.sum(prob_grad * attention_probabilities, axis=-1, keepdims=True))
    ).astype(jnp.bfloat16)
    query_grad = jnp.einsum(
        "wcv,vwn->cwn", score_gradient, key_sequence, preferred_element_type=jnp.float32
    ) * HEAD_DIM ** (-0.5)
    key_grad = jnp.einsum(
        "fgs,gfu->sfu", score_gradient, query_sequence, preferred_element_type=jnp.float32
    ) * HEAD_DIM ** (-0.5)
    return (query_grad, key_grad, value_grad)


def nested_gather(member):
    return lax.all_gather(
        lax.all_gather(member, "narrow", axis=0, tiled=True), "wide", axis=0, tiled=True
    )


LANES = 1024
TILE_ROWS = 16


def shard_rows(shard):
    rows, cols = shard.shape
    blocks = cols // LANES
    if blocks == 1:
        return shard
    return shard.reshape(rows, blocks, LANES).transpose(1, 0, 2).reshape(blocks * rows, LANES)


def rows_shard(piece, cols):
    blocks = cols // LANES
    if blocks == 1:
        return piece
    rows = piece.shape[0] // blocks
    return piece.reshape(blocks, rows, LANES).transpose(1, 0, 2).reshape(rows, cols)


def pad_rows(flat):
    pad = -flat.shape[1] % TILE_ROWS
    if pad:
        flat = jnp.concatenate([flat, jnp.zeros((flat.shape[0], pad, LANES), flat.dtype)], axis=1)
    return flat


def gather_packed(members, count):
    flat = pad_rows(jnp.concatenate([shard_rows(m) for m in members], axis=0)[None])
    got = lax.all_gather(flat[0], AXES, axis=0, tiled=True).reshape(count, flat.shape[1], LANES)
    out, start = [], 0
    for member in members:
        rows, cols = member.shape
        blocks = cols // LANES
        piece = got[:, start : start + blocks * rows]
        start += blocks * rows
        full = piece.reshape(count, blocks, rows, LANES).transpose(0, 2, 1, 3)
        out.append(full.reshape(count * rows, cols))
    return out


def narrow_sum(half):
    size = lax.axis_size("narrow")
    if size != 2:
        return lax.psum_scatter(half, "narrow", scatter_dimension=0, tiled=True).astype(jnp.float32)
    rows = half.shape[0] // 2
    here = lax.axis_index("narrow")
    keep = lax.dynamic_slice_in_dim(half, here * rows, rows, axis=0)
    send = lax.dynamic_slice_in_dim(half, (1 - here) * rows, rows, axis=0)
    got = lax.ppermute(send, "narrow", [(0, 1), (1, 0)])
    return keep.astype(jnp.float32) + got.astype(jnp.float32)


def scatter_packed(matrices, vectors, count):
    pieces = []
    for member in matrices:
        rows, cols = member.shape
        shard = member.astype(jnp.bfloat16).reshape(count, rows // count, cols)
        blocks = cols // LANES
        shard = shard.reshape(count, rows // count, blocks, LANES).transpose(0, 2, 1, 3)
        pieces.append(shard.reshape(count, blocks * rows // count, LANES))
    if vectors:
        small = jnp.concatenate([v.reshape(count, -1) for v in vectors], axis=1)
        pad = -small.shape[1] % LANES
        small = jnp.concatenate([small, jnp.zeros((count, pad), small.dtype)], axis=1)
        pieces.append(small.astype(jnp.bfloat16).reshape(count, -1, LANES))
    flat = pad_rows(jnp.concatenate(pieces, axis=1))
    flat = flat.reshape(count * flat.shape[1], LANES)
    half = lax.psum_scatter(flat, "wide", scatter_dimension=0, tiled=True)
    got = narrow_sum(half)
    out, start = [], 0
    for member in matrices:
        rows, cols = member.shape
        blocks = cols // LANES
        size = blocks * rows // count
        out.append(rows_shard(got[start : start + size], cols))
        start += size
    if vectors:
        tail = got[start:].reshape(-1)
        offset = 0
        for v in vectors:
            size = v.shape[0] // count
            out.append(tail[offset : offset + size])
            offset += size
    return out


def scatter_natural(member):
    half = lax.psum_scatter(member.astype(jnp.bfloat16), "wide", scatter_dimension=0, tiled=True)
    return narrow_sum(half)


def sum_small(vectors, count):
    small = jnp.concatenate([v.reshape(count, -1) for v in vectors], axis=1)
    parts = lax.all_to_all(
        small.reshape(count, 1, small.shape[1]), AXES, split_axis=0, concat_axis=0, tiled=True
    )
    total = jnp.sum(parts, axis=0)[0]
    out, offset = [], 0
    for v in vectors:
        size = v.shape[0] // count
        out.append(total[offset : offset + size])
        offset += size
    return out


def layer(
    inputs,
    condition,
    scale_tokens,
    w_ada,
    bias_ada,
    w_qkv,
    bias_query,
    bias_value,
    gain_query,
    gain_key,
    w_proj,
    bias_proj,
    w_up,
    bias_up,
    w_down,
    bias_down,
    cotangent,
):
    count = lax.axis_size("wide") * lax.axis_size("narrow")
    me = lax.axis_index("wide") * lax.axis_size("narrow") + lax.axis_index("narrow")
    sequences, length, width = inputs.shape
    head_shape = (sequences, length, HEADS, HEAD_DIM)
    cond_rows = condition.astype(jnp.float32)
    activated = jax.nn.silu(cond_rows).astype(jnp.bfloat16)
    vectors = (bias_ada, bias_query, bias_value, gain_query, gain_key, bias_proj, bias_up, bias_down)
    small = nested_gather(
        jnp.concatenate([activated.reshape(-1)] + list(vectors))[None, :]
    )
    activated_all = small[:, : activated.size].reshape(count * sequences, activated.shape[1])
    unpacked, start = [], activated.size
    for member in vectors:
        size = member.shape[0]
        unpacked.append(small[:, start : start + size].reshape(count * size).astype(jnp.float32))
        start += size
    ada_bias, query_bias, value_bias, query_gain, key_gain, proj_bias, up_bias, down_bias = unpacked
    first = lax.all_gather(jnp.concatenate([w_qkv, w_proj], axis=1), AXES, axis=0, tiled=True)
    qkv_full = first[:, : w_qkv.shape[1]]
    proj_full = first[:, w_qkv.shape[1] :]
    up_full, down_full = gather_packed((w_up, w_down), count)
    allowed = block_mask(scale_tokens)
    input_rows = inputs.astype(jnp.float32)
    ada_rows = w_ada.shape[0]
    ada_cols = w_ada.shape[1]
    activated_mine = lax.dynamic_slice_in_dim(activated_all, me * ada_rows, ada_rows, axis=1)
    ada_partial = jnp.dot(activated_mine, w_ada, preferred_element_type=jnp.float32)
    ada_parts = lax.all_to_all(
        ada_partial.reshape(count, sequences, ada_cols), AXES, split_axis=0, concat_axis=0, tiled=True
    )
    adaptive = jnp.sum(ada_parts, axis=0) + ada_bias
    gamma_attn, gamma_mlp, scale_attn, scale_mlp, shift_attn, shift_mlp = jnp.split(
        adaptive, 6, axis=1
    )
    normed_attn = modulate(input_rows, scale_attn, shift_attn).astype(jnp.bfloat16)
    projected = matmul_rows(normed_attn, qkv_full)
    query_pre = projected[..., :width] + query_bias
    key_pre = projected[..., width : 2 * width]
    queries = head_norm(query_pre, query_gain).astype(jnp.bfloat16)
    key_rows = head_norm(key_pre, key_gain).astype(jnp.bfloat16)
    value_rows = (projected[..., 2 * width :] + value_bias).astype(jnp.bfloat16).reshape(head_shape)
    context, logsum = jax.vmap(
        lambda q, k, v: attend_forward(q, k, v, allowed)
    )(queries, key_rows, value_rows)
    context = context.reshape(sequences, length, width)
    attended = matmul_rows(context, proj_full) + proj_bias
    middle = input_rows + gamma_attn[:, None, :] * attended
    normed_mlp = modulate(middle, scale_mlp, shift_mlp).astype(jnp.bfloat16)
    hidden_pre = matmul_rows(normed_mlp, up_full) + up_bias
    hidden = gelu_tanh(hidden_pre).astype(jnp.bfloat16)
    branch = matmul_rows(hidden, down_full) + down_bias
    layer_output = (middle + gamma_mlp[:, None, :] * branch).astype(jnp.bfloat16)
    upstream = cotangent.astype(jnp.float32)
    gamma_mlp_grad = jnp.sum(upstream * branch, axis=1)
    branch_grad = (upstream * gamma_mlp[:, None, :]).astype(jnp.bfloat16)
    down_grad = weight_grad(hidden, branch_grad)
    (down_sum,) = scatter_packed((down_grad,), (), count)
    down_bias_grad = jnp.sum(branch_grad.astype(jnp.float32), axis=(0, 1))
    return mlp_back(
        branch_grad, down_full, hidden_pre, normed_mlp, up_full, middle, scale_mlp, shift_mlp,
        upstream, attended, gamma_attn, context, proj_full, head_shape, queries, key_rows,
        value_rows, logsum, allowed, query_pre, query_gain, key_pre, key_gain, sequences,
        length, width, normed_attn, qkv_full, input_rows, scale_attn, shift_attn,
        gamma_mlp_grad, activated_mine, w_ada, cond_rows, me, count, layer_output,
        down_sum, down_bias_grad,
    )


def mlp_back(
    branch_grad, down_full, hidden_pre, normed_mlp, up_full, middle, scale_mlp, shift_mlp,
    upstream, attended, gamma_attn, context, proj_full, head_shape, queries, key_rows,
    value_rows, logsum, allowed, query_pre, query_gain, key_pre, key_gain, sequences,
    length, width, normed_attn, qkv_full, input_rows, scale_attn, shift_attn,
    gamma_mlp_grad, activated_mine, w_ada, cond_rows, me, count, layer_output,
    down_sum, down_bias_grad,
):
    hidden_grad = matmul_back(branch_grad, down_full)
    gelu_pull = jax.vjp(gelu_tanh, hidden_pre)[1]
    pre_grad = gelu_pull(hidden_grad)[0].astype(jnp.bfloat16)
    up_grad = weight_grad(normed_mlp, pre_grad)
    up_bias_grad = jnp.sum(pre_grad.astype(jnp.float32), axis=(0, 1))
    normed_mlp_grad = matmul_back(pre_grad, up_full)
    mlp_pull = jax.vjp(modulate, middle, scale_mlp, shift_mlp)[1]
    middle_part, scale_mlp_grad, shift_mlp_grad = mlp_pull(normed_mlp_grad)
    middle_grad = upstream + middle_part
    gamma_attn_grad = jnp.sum(middle_grad * attended, axis=1)
    attended_grad = (middle_grad * gamma_attn[:, None, :]).astype(jnp.bfloat16)
    proj_grad = weight_grad(context, attended_grad)
    proj_bias_grad = jnp.sum(attended_grad.astype(jnp.float32), axis=(0, 1))
    up_sum, proj_sum = scatter_packed((up_grad, proj_grad), (), count)
    context_gradient = (
        matmul_back(attended_grad, proj_full).astype(jnp.bfloat16).reshape(head_shape)
    )
    query_grad, key_grad, value_grad = jax.vmap(
        lambda q, k, v, l, c: attend_backward(q, k, v, l, c, allowed)
    )(queries, key_rows, value_rows, logsum, context_gradient)
    query_pull = jax.vjp(head_norm, query_pre, query_gain)[1]
    query_pre_grad, query_gain_grad = query_pull(query_grad)
    key_pull = jax.vjp(head_norm, key_pre, key_gain)[1]
    key_pre_grad, key_gain_grad = key_pull(key_grad)
    value_grad = value_grad.reshape(sequences, length, width)
    query_bias_grad = jnp.sum(query_pre_grad, axis=(0, 1))
    value_bias_grad = jnp.sum(value_grad, axis=(0, 1))
    projected_grad = jnp.concatenate([query_pre_grad, key_pre_grad, value_grad], axis=2).astype(
        jnp.bfloat16
    )
    qkv_grad = weight_grad(normed_attn, projected_grad)
    qkv_sum = scatter_natural(qkv_grad)
    (
        query_bias_sum,
        value_bias_sum,
        query_gain_sum,
        key_gain_sum,
        proj_bias_sum,
        up_bias_sum,
        down_bias_sum,
    ) = sum_small(
        (
            query_bias_grad,
            value_bias_grad,
            query_gain_grad,
            key_gain_grad,
            proj_bias_grad,
            up_bias_grad,
            down_bias_grad,
        ),
        count,
    )
    return tail(
        projected_grad, qkv_full, input_rows, scale_attn, shift_attn, middle_grad,
        gamma_attn_grad, gamma_mlp_grad, scale_mlp_grad, shift_mlp_grad, activated_mine,
        w_ada, cond_rows, me, count, layer_output, qkv_sum, query_bias_sum, value_bias_sum,
        query_gain_sum, key_gain_sum, proj_sum, proj_bias_sum, up_sum, up_bias_sum, down_sum,
        down_bias_sum,
    )


def tail(
    projected_grad, qkv_full, input_rows, scale_attn, shift_attn, middle_grad,
    gamma_attn_grad, gamma_mlp_grad, scale_mlp_grad, shift_mlp_grad, activated_mine,
    w_ada, cond_rows, me, count, layer_output, qkv_sum, query_bias_sum, value_bias_sum,
    query_gain_sum, key_gain_sum, proj_sum, proj_bias_sum, up_sum, up_bias_sum, down_sum,
    down_bias_sum,
):
    ada_cols = w_ada.shape[1]
    normed_attn_grad = matmul_back(projected_grad, qkv_full)
    attn_pull = jax.vjp(modulate, input_rows, scale_attn, shift_attn)[1]
    input_part, scale_attn_grad, shift_attn_grad = attn_pull(normed_attn_grad)
    input_grad = middle_grad + input_part
    adaptive_grad = jnp.concatenate(
        [
            gamma_attn_grad,
            gamma_mlp_grad,
            scale_attn_grad,
            scale_mlp_grad,
            shift_attn_grad,
            shift_mlp_grad,
        ],
        axis=1,
    ).astype(jnp.bfloat16)
    adaptive_grad_all = nested_gather(adaptive_grad)
    ada_sum = jnp.einsum(
        "sc,sn->cn", activated_mine, adaptive_grad_all, preferred_element_type=jnp.float32
    )
    bias_share = ada_cols // count
    ada_bias_sum = jnp.sum(
        lax.dynamic_slice_in_dim(adaptive_grad_all, me * bias_share, bias_share, axis=1).astype(
            jnp.float32
        ),
        axis=0,
    )
    activated_grad_cols = jnp.einsum(
        "sn,cn->sc", adaptive_grad_all, w_ada, preferred_element_type=jnp.float32
    )
    activated_grad = lax.all_to_all(
        activated_grad_cols, AXES, split_axis=0, concat_axis=1, tiled=True
    )
    silu_pull = jax.vjp(jax.nn.silu, cond_rows)[1]
    condition_grad = silu_pull(activated_grad)[0]
    return (
        layer_output,
        input_grad,
        condition_grad,
        ada_sum,
        ada_bias_sum,
        qkv_sum,
        query_bias_sum,
        value_bias_sum,
        query_gain_sum,
        key_gain_sum,
        proj_sum,
        proj_bias_sum,
        up_sum,
        up_bias_sum,
        down_sum,
        down_bias_sum,
    )


def solution(mesh):
    row = P(AXES, None, None)
    mat = P(AXES, None)
    vec = P(AXES)
    return jax.shard_map(
        layer,
        mesh=mesh,
        in_specs=(row, mat, P(), mat, vec, mat, vec, vec, vec, vec, mat, vec, mat, vec, mat, vec, row),
        out_specs=(row, row, mat, mat, vec, mat, vec, vec, vec, vec, mat, vec, mat, vec, mat, vec),
        check_vma=False,
    )
```

```python
import jax
import jax.numpy as jnp
from jax import lax
from jax.sharding import PartitionSpec as P


HEADS = 16
HEAD_DIM = 64
SEQ_LEN = 680
AXES = ("wide", "narrow")

EPSILON = 1e-06
MASKED = -1000000000.0


def layer_norm(values):
    centred = values - jnp.mean(values, axis=-1, keepdims=True)
    return centred * lax.rsqrt(jnp.mean(centred * centred, axis=-1, keepdims=True) + EPSILON)


def modulate(values, scaling, offset):
    return layer_norm(values) * (1.0 + scaling[:, None, :]) + offset[:, None, :]


def head_norm(values, channel_gain):
    shaped = values.reshape(values.shape[0], values.shape[1], HEADS, HEAD_DIM)
    scaled = shaped * lax.rsqrt(jnp.mean(shaped * shaped, axis=-1, keepdims=True) + EPSILON)
    return scaled * channel_gain.reshape(HEADS, HEAD_DIM)


def gelu_tanh(values):
    return jax.nn.gelu(values, approximate=True)


def block_mask(scale_tokens):
    block_ends = jnp.cumsum(scale_tokens)
    places = jnp.arange(SEQ_LEN, dtype=jnp.int32)
    limits = jnp.min(
        jnp.where(block_ends[None, :] > places[:, None], block_ends[None, :], SEQ_LEN), axis=1
    )
    return places[None, :] < limits[:, None]


def matmul_rows(first_operand, second_operand):
    return jnp.einsum(
        "fyg,gq->fyq", first_operand, second_operand, preferred_element_type=jnp.float32
    )


def matmul_back(first_operand, second_operand):
    return jnp.einsum(
        "rfw,uw->rfu", first_operand, second_operand, preferred_element_type=jnp.float32
    )


def weight_grad(first_operand, second_operand):
    return jnp.einsum(
        "crk,cre->ke", first_operand, second_operand, preferred_element_type=jnp.float32
    )


def masked_scores(query_sequence, key_sequence, allowed):
    scores = jnp.einsum(
        "nkz,vkz->knv", query_sequence, key_sequence, preferred_element_type=jnp.float32
    ) * HEAD_DIM ** (-0.5)
    return jnp.where(allowed[None], scores, MASKED)


def attend_forward(query_sequence, key_sequence, value_sequence, allowed):
    scores = masked_scores(query_sequence, key_sequence, allowed)
    row_max = jnp.max(scores, axis=-1, keepdims=True)
    exponent = jnp.exp(scores - row_max)
    row_total = jnp.sum(exponent, axis=-1, keepdims=True)
    probabilities_reduced = (exponent / row_total).astype(jnp.bfloat16)
    context = jnp.einsum(
        "wcv,vwn->cwn", probabilities_reduced, value_sequence, preferred_element_type=jnp.float32
    ).astype(jnp.bfloat16)
    return (context, row_max[..., 0] + jnp.log(row_total[..., 0]))


def attend_backward(
    query_sequence, key_sequence, value_sequence, logsum, context_gradient, allowed
):
    scores = masked_scores(query_sequence, key_sequence, allowed)
    attention_probabilities = jnp.exp(scores - logsum[..., None])
    prob_grad = jnp.einsum(
        "nkz,vkz->knv", context_gradient, value_sequence, preferred_element_type=jnp.float32
    )
    value_grad = jnp.einsum(
        "fgs,gfu->sfu",
        attention_probabilities.astype(jnp.bfloat16),
        context_gradient,
        preferred_element_type=jnp.float32,
    )
    score_gradient = (
        attention_probabilities
        * (prob_grad - jnp.sum(prob_grad * attention_probabilities, axis=-1, keepdims=True))
    ).astype(jnp.bfloat16)
    query_grad = jnp.einsum(
        "wcv,vwn->cwn", score_gradient, key_sequence, preferred_element_type=jnp.float32
    ) * HEAD_DIM ** (-0.5)
    key_grad = jnp.einsum(
        "fgs,gfu->sfu", score_gradient, query_sequence, preferred_element_type=jnp.float32
    ) * HEAD_DIM ** (-0.5)
    return (query_grad, key_grad, value_grad)


def nested_gather(member):
    return lax.all_gather(
        lax.all_gather(member, "narrow", axis=0, tiled=True), "wide", axis=0, tiled=True
    )


def narrow_sum(half):
    size = lax.axis_size("narrow")
    if size != 2:
        return lax.psum_scatter(half, "narrow", scatter_dimension=0, tiled=True).astype(jnp.float32)
    rows = half.shape[0] // 2
    here = lax.axis_index("narrow")
    keep = lax.dynamic_slice_in_dim(half, here * rows, rows, axis=0)
    send = lax.dynamic_slice_in_dim(half, (1 - here) * rows, rows, axis=0)
    got = lax.ppermute(send, "narrow", [(0, 1), (1, 0)])
    return keep.astype(jnp.float32) + got.astype(jnp.float32)


def scatter_natural(member):
    half = lax.psum_scatter(member.astype(jnp.bfloat16), "wide", scatter_dimension=0, tiled=True)
    return narrow_sum(half)


def sum_small(vectors, count):
    small = jnp.concatenate([v.reshape(count, -1) for v in vectors], axis=1)
    parts = lax.all_to_all(
        small.reshape(count, 1, small.shape[1]), AXES, split_axis=0, concat_axis=0, tiled=True
    )
    total = jnp.sum(parts, axis=0)[0]
    out, offset = [], 0
    for v in vectors:
        size = v.shape[0] // count
        out.append(total[offset : offset + size])
        offset += size
    return out


def layer(
    inputs,
    condition,
    scale_tokens,
    w_ada,
    bias_ada,
    w_qkv,
    bias_query,
    bias_value,
    gain_query,
    gain_key,
    w_proj,
    bias_proj,
    w_up,
    bias_up,
    w_down,
    bias_down,
    cotangent,
):
    count = lax.axis_size("wide") * lax.axis_size("narrow")
    me = lax.axis_index("wide") * lax.axis_size("narrow") + lax.axis_index("narrow")
    sequences, length, width = inputs.shape
    head_shape = (sequences, length, HEADS, HEAD_DIM)
    cond_rows = condition.astype(jnp.float32)
    activated = jax.nn.silu(cond_rows).astype(jnp.bfloat16)
    vectors = (bias_ada, bias_query, bias_value, gain_query, gain_key, bias_proj, bias_up, bias_down)
    small = nested_gather(
        jnp.concatenate([activated.reshape(-1)] + list(vectors))[None, :]
    )
    activated_all = small[:, : activated.size].reshape(count * sequences, activated.shape[1])
    unpacked, start = [], activated.size
    for member in vectors:
        size = member.shape[0]
        unpacked.append(small[:, start : start + size].reshape(count * size).astype(jnp.float32))
        start += size
    ada_bias, query_bias, value_bias, query_gain, key_gain, proj_bias, up_bias, down_bias = unpacked
    first = lax.all_gather(
        jnp.concatenate([w_qkv, w_proj, w_up], axis=1), AXES, axis=0, tiled=True
    )
    qkv_cols, proj_cols = w_qkv.shape[1], w_proj.shape[1]
    qkv_full = first[:, :qkv_cols]
    proj_full = first[:, qkv_cols : qkv_cols + proj_cols]
    up_full = first[:, qkv_cols + proj_cols :]
    down_full = lax.all_gather(w_down, AXES, axis=0, tiled=True)
    allowed = block_mask(scale_tokens)
    input_rows = inputs.astype(jnp.float32)
    ada_rows = w_ada.shape[0]
    ada_cols = w_ada.shape[1]
    activated_mine = lax.dynamic_slice_in_dim(activated_all, me * ada_rows, ada_rows, axis=1)
    ada_partial = jnp.dot(activated_mine, w_ada, preferred_element_type=jnp.float32)
    ada_parts = lax.all_to_all(
        ada_partial.reshape(count, sequences, ada_cols), AXES, split_axis=0, concat_axis=0, tiled=True
    )
    adaptive = jnp.sum(ada_parts, axis=0) + ada_bias
    gamma_attn, gamma_mlp, scale_attn, scale_mlp, shift_attn, shift_mlp = jnp.split(
        adaptive, 6, axis=1
    )
    normed_attn = modulate(input_rows, scale_attn, shift_attn).astype(jnp.bfloat16)
    projected = matmul_rows(normed_attn, qkv_full)
    query_pre = projected[..., :width] + query_bias
    key_pre = projected[..., width : 2 * width]
    queries = head_norm(query_pre, query_gain).astype(jnp.bfloat16)
    key_rows = head_norm(key_pre, key_gain).astype(jnp.bfloat16)
    value_rows = (projected[..., 2 * width :] + value_bias).astype(jnp.bfloat16).reshape(head_shape)
    context, logsum = jax.vmap(
        lambda q, k, v: attend_forward(q, k, v, allowed)
    )(queries, key_rows, value_rows)
    context = context.reshape(sequences, length, width)
    attended = matmul_rows(context, proj_full) + proj_bias
    middle = input_rows + gamma_attn[:, None, :] * attended
    normed_mlp = modulate(middle, scale_mlp, shift_mlp).astype(jnp.bfloat16)
    hidden_pre = matmul_rows(normed_mlp, up_full) + up_bias
    hidden = gelu_tanh(hidden_pre).astype(jnp.bfloat16)
    branch = matmul_rows(hidden, down_full) + down_bias
    layer_output = (middle + gamma_mlp[:, None, :] * branch).astype(jnp.bfloat16)
    upstream = cotangent.astype(jnp.float32)
    gamma_mlp_grad = jnp.sum(upstream * branch, axis=1)
    branch_grad = (upstream * gamma_mlp[:, None, :]).astype(jnp.bfloat16)
    down_grad = weight_grad(hidden, branch_grad)
    down_sum = scatter_natural(down_grad)
    down_bias_grad = jnp.sum(branch_grad.astype(jnp.float32), axis=(0, 1))
    return mlp_back(
        branch_grad, down_full, hidden_pre, normed_mlp, up_full, middle, scale_mlp, shift_mlp,
        upstream, attended, gamma_attn, context, proj_full, head_shape, queries, key_rows,
        value_rows, logsum, allowed, query_pre, query_gain, key_pre, key_gain, sequences,
        length, width, normed_attn, qkv_full, input_rows, scale_attn, shift_attn,
        gamma_mlp_grad, activated_mine, w_ada, cond_rows, me, count, layer_output,
        down_sum, down_bias_grad,
    )


def mlp_back(
    branch_grad, down_full, hidden_pre, normed_mlp, up_full, middle, scale_mlp, shift_mlp,
    upstream, attended, gamma_attn, context, proj_full, head_shape, queries, key_rows,
    value_rows, logsum, allowed, query_pre, query_gain, key_pre, key_gain, sequences,
    length, width, normed_attn, qkv_full, input_rows, scale_attn, shift_attn,
    gamma_mlp_grad, activated_mine, w_ada, cond_rows, me, count, layer_output,
    down_sum, down_bias_grad,
):
    hidden_grad = matmul_back(branch_grad, down_full)
    gelu_pull = jax.vjp(gelu_tanh, hidden_pre)[1]
    pre_grad = gelu_pull(hidden_grad)[0].astype(jnp.bfloat16)
    up_grad = weight_grad(normed_mlp, pre_grad)
    up_bias_grad = jnp.sum(pre_grad.astype(jnp.float32), axis=(0, 1))
    normed_mlp_grad = matmul_back(pre_grad, up_full)
    mlp_pull = jax.vjp(modulate, middle, scale_mlp, shift_mlp)[1]
    middle_part, scale_mlp_grad, shift_mlp_grad = mlp_pull(normed_mlp_grad)
    middle_grad = upstream + middle_part
    gamma_attn_grad = jnp.sum(middle_grad * attended, axis=1)
    attended_grad = (middle_grad * gamma_attn[:, None, :]).astype(jnp.bfloat16)
    proj_grad = weight_grad(context, attended_grad)
    proj_bias_grad = jnp.sum(attended_grad.astype(jnp.float32), axis=(0, 1))
    both_sum = scatter_natural(jnp.concatenate([up_grad, proj_grad], axis=1))
    up_sum = both_sum[:, : up_grad.shape[1]]
    proj_sum = both_sum[:, up_grad.shape[1] :]
    context_gradient = (
        matmul_back(attended_grad, proj_full).astype(jnp.bfloat16).reshape(head_shape)
    )
    query_grad, key_grad, value_grad = jax.vmap(
        lambda q, k, v, l, c: attend_backward(q, k, v, l, c, allowed)
    )(queries, key_rows, value_rows, logsum, context_gradient)
    query_pull = jax.vjp(head_norm, query_pre, query_gain)[1]
    query_pre_grad, query_gain_grad = query_pull(query_grad)
    key_pull = jax.vjp(head_norm, key_pre, key_gain)[1]
    key_pre_grad, key_gain_grad = key_pull(key_grad)
    value_grad = value_grad.reshape(sequences, length, width)
    query_bias_grad = jnp.sum(query_pre_grad, axis=(0, 1))
    value_bias_grad = jnp.sum(value_grad, axis=(0, 1))
    projected_grad = jnp.concatenate([query_pre_grad, key_pre_grad, value_grad], axis=2).astype(
        jnp.bfloat16
    )
    qkv_grad = weight_grad(normed_attn, projected_grad)
    qkv_sum = scatter_natural(qkv_grad)
    (
        query_bias_sum,
        value_bias_sum,
        query_gain_sum,
        key_gain_sum,
        proj_bias_sum,
        up_bias_sum,
        down_bias_sum,
    ) = sum_small(
        (
            query_bias_grad,
            value_bias_grad,
            query_gain_grad,
            key_gain_grad,
            proj_bias_grad,
            up_bias_grad,
            down_bias_grad,
        ),
        count,
    )
    return tail(
        projected_grad, qkv_full, input_rows, scale_attn, shift_attn, middle_grad,
        gamma_attn_grad, gamma_mlp_grad, scale_mlp_grad, shift_mlp_grad, activated_mine,
        w_ada, cond_rows, me, count, layer_output, qkv_sum, query_bias_sum, value_bias_sum,
        query_gain_sum, key_gain_sum, proj_sum, proj_bias_sum, up_sum, up_bias_sum, down_sum,
        down_bias_sum,
    )


def tail(
    projected_grad, qkv_full, input_rows, scale_attn, shift_attn, middle_grad,
    gamma_attn_grad, gamma_mlp_grad, scale_mlp_grad, shift_mlp_grad, activated_mine,
    w_ada, cond_rows, me, count, layer_output, qkv_sum, query_bias_sum, value_bias_sum,
    query_gain_sum, key_gain_sum, proj_sum, proj_bias_sum, up_sum, up_bias_sum, down_sum,
    down_bias_sum,
):
    ada_cols = w_ada.shape[1]
    normed_attn_grad = matmul_back(projected_grad, qkv_full)
    attn_pull = jax.vjp(modulate, input_rows, scale_attn, shift_attn)[1]
    input_part, scale_attn_grad, shift_attn_grad = attn_pull(normed_attn_grad)
    input_grad = middle_grad + input_part
    adaptive_grad = jnp.concatenate(
        [
            gamma_attn_grad,
            gamma_mlp_grad,
            scale_attn_grad,
            scale_mlp_grad,
            shift_attn_grad,
            shift_mlp_grad,
        ],
        axis=1,
    ).astype(jnp.bfloat16)
    adaptive_grad_all = nested_gather(adaptive_grad)
    ada_sum = jnp.einsum(
        "sc,sn->cn", activated_mine, adaptive_grad_all, preferred_element_type=jnp.float32
    )
    bias_share = ada_cols // count
    ada_bias_sum = jnp.sum(
        lax.dynamic_slice_in_dim(adaptive_grad_all, me * bias_share, bias_share, axis=1).astype(
            jnp.float32
        ),
        axis=0,
    )
    activated_grad_cols = jnp.einsum(
        "sn,cn->sc", adaptive_grad_all, w_ada, preferred_element_type=jnp.float32
    )
    activated_grad = lax.all_to_all(
        activated_grad_cols, AXES, split_axis=0, concat_axis=1, tiled=True
    )
    silu_pull = jax.vjp(jax.nn.silu, cond_rows)[1]
    condition_grad = silu_pull(activated_grad)[0]
    return (
        layer_output,
        input_grad,
        condition_grad,
        ada_sum,
        ada_bias_sum,
        qkv_sum,
        query_bias_sum,
        value_bias_sum,
        query_gain_sum,
        key_gain_sum,
        proj_sum,
        proj_bias_sum,
        up_sum,
        up_bias_sum,
        down_sum,
        down_bias_sum,
    )


def solution(mesh):
    row = P(AXES, None, None)
    mat = P(AXES, None)
    vec = P(AXES)
    return jax.shard_map(
        layer,
        mesh=mesh,
        in_specs=(row, mat, P(), mat, vec, mat, vec, vec, vec, vec, mat, vec, mat, vec, mat, vec, row),
        out_specs=(row, row, mat, mat, vec, mat, vec, vec, vec, vec, mat, vec, mat, vec, mat, vec),
        check_vma=False,
    )
```

```python
import jax
import jax.numpy as jnp
from jax import lax
from jax.sharding import PartitionSpec as P


HEADS = 16
HEAD_DIM = 64
SEQ_LEN = 680
AXES = ("wide", "narrow")

EPSILON = 1e-06
MASKED = -1000000000.0


def layer_norm(values):
    centred = values - jnp.mean(values, axis=-1, keepdims=True)
    return centred * lax.rsqrt(jnp.mean(centred * centred, axis=-1, keepdims=True) + EPSILON)


def modulate(values, scaling, offset):
    return layer_norm(values) * (1.0 + scaling[:, None, :]) + offset[:, None, :]


def head_norm(values, channel_gain):
    shaped = values.reshape(values.shape[0], values.shape[1], HEADS, HEAD_DIM)
    scaled = shaped * lax.rsqrt(jnp.mean(shaped * shaped, axis=-1, keepdims=True) + EPSILON)
    return scaled * channel_gain.reshape(HEADS, HEAD_DIM)


def gelu_tanh(values):
    return jax.nn.gelu(values, approximate=True)


def block_mask(scale_tokens):
    block_ends = jnp.cumsum(scale_tokens)
    places = jnp.arange(SEQ_LEN, dtype=jnp.int32)
    limits = jnp.min(
        jnp.where(block_ends[None, :] > places[:, None], block_ends[None, :], SEQ_LEN), axis=1
    )
    return places[None, :] < limits[:, None]


def matmul_rows(first_operand, second_operand):
    return jnp.einsum(
        "fyg,gq->fyq", first_operand, second_operand, preferred_element_type=jnp.float32
    )


def matmul_back(first_operand, second_operand):
    return jnp.einsum(
        "rfw,uw->rfu", first_operand, second_operand, preferred_element_type=jnp.float32
    )


def weight_grad(first_operand, second_operand):
    return jnp.einsum(
        "crk,cre->ke", first_operand, second_operand, preferred_element_type=jnp.float32
    )


def masked_scores(query_sequence, key_sequence, allowed):
    scores = jnp.einsum(
        "nkz,vkz->knv", query_sequence, key_sequence, preferred_element_type=jnp.float32
    ) * HEAD_DIM ** (-0.5)
    return jnp.where(allowed[None], scores, MASKED)


def attend_forward(query_sequence, key_sequence, value_sequence, allowed):
    scores = masked_scores(query_sequence, key_sequence, allowed)
    row_max = jnp.max(scores, axis=-1, keepdims=True)
    exponent = jnp.exp(scores - row_max)
    row_total = jnp.sum(exponent, axis=-1, keepdims=True)
    probabilities_reduced = (exponent / row_total).astype(jnp.bfloat16)
    context = jnp.einsum(
        "wcv,vwn->cwn", probabilities_reduced, value_sequence, preferred_element_type=jnp.float32
    ).astype(jnp.bfloat16)
    return (context, row_max[..., 0] + jnp.log(row_total[..., 0]))


def attend_backward(
    query_sequence, key_sequence, value_sequence, logsum, context_gradient, allowed
):
    scores = masked_scores(query_sequence, key_sequence, allowed)
    attention_probabilities = jnp.exp(scores - logsum[..., None])
    prob_grad = jnp.einsum(
        "nkz,vkz->knv", context_gradient, value_sequence, preferred_element_type=jnp.float32
    )
    value_grad = jnp.einsum(
        "fgs,gfu->sfu",
        attention_probabilities.astype(jnp.bfloat16),
        context_gradient,
        preferred_element_type=jnp.float32,
    )
    score_gradient = (
        attention_probabilities
        * (prob_grad - jnp.sum(prob_grad * attention_probabilities, axis=-1, keepdims=True))
    ).astype(jnp.bfloat16)
    query_grad = jnp.einsum(
        "wcv,vwn->cwn", score_gradient, key_sequence, preferred_element_type=jnp.float32
    ) * HEAD_DIM ** (-0.5)
    key_grad = jnp.einsum(
        "fgs,gfu->sfu", score_gradient, query_sequence, preferred_element_type=jnp.float32
    ) * HEAD_DIM ** (-0.5)
    return (query_grad, key_grad, value_grad)


def nested_gather(member):
    return lax.all_gather(
        lax.all_gather(member, "narrow", axis=0, tiled=True), "wide", axis=0, tiled=True
    )


def narrow_sum(half):
    size = lax.axis_size("narrow")
    if size != 2:
        return lax.psum_scatter(half, "narrow", scatter_dimension=0, tiled=True).astype(jnp.float32)
    rows = half.shape[0] // 2
    here = lax.axis_index("narrow")
    keep = lax.dynamic_slice_in_dim(half, here * rows, rows, axis=0)
    send = lax.dynamic_slice_in_dim(half, (1 - here) * rows, rows, axis=0)
    got = lax.ppermute(send, "narrow", [(0, 1), (1, 0)])
    return keep.astype(jnp.float32) + got.astype(jnp.float32)


def tree_sum(member):
    wide, narrow = lax.axis_size("wide"), lax.axis_size("narrow")
    if (wide, narrow) != (16, 2):
        return scatter_natural(member)
    w = lax.axis_index("wide")
    x = lax.axis_index("narrow")
    rows = member.shape[0] // 32
    part = member.astype(jnp.bfloat16).reshape((4, 2, 2, 2, rows) + member.shape[1:])

    def swap(total, axis, mine, axis_name, flip):
        keep = lax.dynamic_index_in_dim(total, mine, axis, keepdims=False)
        send = lax.dynamic_index_in_dim(total, 1 - mine, axis, keepdims=False)
        size = lax.axis_size(axis_name)
        pairs = [(i, i ^ flip) for i in range(size)]
        got = lax.ppermute(send.astype(jnp.bfloat16), axis_name, pairs)
        return keep.astype(jnp.float32) + got.astype(jnp.float32)

    total = swap(part, 2, w % 2, "wide", 1)
    total = swap(total, 2, x, "narrow", 1)
    total = swap(total, 1, (w // 2) % 2, "wide", 2)
    total = swap(total.reshape((2, 2, rows) + member.shape[1:]), 0, w // 8, "wide", 8)
    return swap(total, 0, (w // 4) % 2, "wide", 4)


def scatter_natural(member):
    half = lax.psum_scatter(member.astype(jnp.bfloat16), "wide", scatter_dimension=0, tiled=True)
    return narrow_sum(half)


def sum_small(vectors, count):
    small = jnp.concatenate([v.reshape(count, -1) for v in vectors], axis=1)
    parts = lax.all_to_all(
        small.reshape(count, 1, small.shape[1]), AXES, split_axis=0, concat_axis=0, tiled=True
    )
    total = jnp.sum(parts, axis=0)[0]
    out, offset = [], 0
    for v in vectors:
        size = v.shape[0] // count
        out.append(total[offset : offset + size])
        offset += size
    return out


def layer(
    inputs,
    condition,
    scale_tokens,
    w_ada,
    bias_ada,
    w_qkv,
    bias_query,
    bias_value,
    gain_query,
    gain_key,
    w_proj,
    bias_proj,
    w_up,
    bias_up,
    w_down,
    bias_down,
    cotangent,
):
    count = lax.axis_size("wide") * lax.axis_size("narrow")
    me = lax.axis_index("wide") * lax.axis_size("narrow") + lax.axis_index("narrow")
    sequences, length, width = inputs.shape
    head_shape = (sequences, length, HEADS, HEAD_DIM)
    cond_rows = condition.astype(jnp.float32)
    activated = jax.nn.silu(cond_rows).astype(jnp.bfloat16)
    vectors = (bias_ada, bias_query, bias_value, gain_query, gain_key, bias_proj, bias_up, bias_down)
    small = nested_gather(
        jnp.concatenate([activated.reshape(-1)] + list(vectors))[None, :]
    )
    activated_all = small[:, : activated.size].reshape(count * sequences, activated.shape[1])
    unpacked, start = [], activated.size
    for member in vectors:
        size = member.shape[0]
        unpacked.append(small[:, start : start + size].reshape(count * size).astype(jnp.float32))
        start += size
    ada_bias, query_bias, value_bias, query_gain, key_gain, proj_bias, up_bias, down_bias = unpacked
    first = lax.all_gather(
        jnp.concatenate([w_qkv, w_proj, w_up], axis=1), AXES, axis=0, tiled=True
    )
    qkv_cols, proj_cols = w_qkv.shape[1], w_proj.shape[1]
    qkv_full = first[:, :qkv_cols]
    proj_full = first[:, qkv_cols : qkv_cols + proj_cols]
    up_full = first[:, qkv_cols + proj_cols :]
    down_full = lax.all_gather(w_down, AXES, axis=0, tiled=True)
    allowed = block_mask(scale_tokens)
    input_rows = inputs.astype(jnp.float32)
    ada_rows = w_ada.shape[0]
    ada_cols = w_ada.shape[1]
    activated_mine = lax.dynamic_slice_in_dim(activated_all, me * ada_rows, ada_rows, axis=1)
    ada_partial = jnp.dot(activated_mine, w_ada, preferred_element_type=jnp.float32)
    ada_parts = lax.all_to_all(
        ada_partial.reshape(count, sequences, ada_cols), AXES, split_axis=0, concat_axis=0, tiled=True
    )
    adaptive = jnp.sum(ada_parts, axis=0) + ada_bias
    gamma_attn, gamma_mlp, scale_attn, scale_mlp, shift_attn, shift_mlp = jnp.split(
        adaptive, 6, axis=1
    )
    normed_attn = modulate(input_rows, scale_attn, shift_attn).astype(jnp.bfloat16)
    projected = matmul_rows(normed_attn, qkv_full)
    query_pre = projected[..., :width] + query_bias
    key_pre = projected[..., width : 2 * width]
    queries = head_norm(query_pre, query_gain).astype(jnp.bfloat16)
    key_rows = head_norm(key_pre, key_gain).astype(jnp.bfloat16)
    value_rows = (projected[..., 2 * width :] + value_bias).astype(jnp.bfloat16).reshape(head_shape)
    context, logsum = jax.vmap(
        lambda q, k, v: attend_forward(q, k, v, allowed)
    )(queries, key_rows, value_rows)
    context = context.reshape(sequences, length, width)
    attended = matmul_rows(context, proj_full) + proj_bias
    middle = input_rows + gamma_attn[:, None, :] * attended
    normed_mlp = modulate(middle, scale_mlp, shift_mlp).astype(jnp.bfloat16)
    hidden_pre = matmul_rows(normed_mlp, up_full) + up_bias
    hidden = gelu_tanh(hidden_pre).astype(jnp.bfloat16)
    branch = matmul_rows(hidden, down_full) + down_bias
    layer_output = (middle + gamma_mlp[:, None, :] * branch).astype(jnp.bfloat16)
    upstream = cotangent.astype(jnp.float32)
    gamma_mlp_grad = jnp.sum(upstream * branch, axis=1)
    branch_grad = (upstream * gamma_mlp[:, None, :]).astype(jnp.bfloat16)
    down_grad = weight_grad(hidden, branch_grad)
    down_sum = tree_sum(down_grad)
    down_bias_grad = jnp.sum(branch_grad.astype(jnp.float32), axis=(0, 1))
    return mlp_back(
        branch_grad, down_full, hidden_pre, normed_mlp, up_full, middle, scale_mlp, shift_mlp,
        upstream, attended, gamma_attn, context, proj_full, head_shape, queries, key_rows,
        value_rows, logsum, allowed, query_pre, query_gain, key_pre, key_gain, sequences,
        length, width, normed_attn, qkv_full, input_rows, scale_attn, shift_attn,
        gamma_mlp_grad, activated_mine, w_ada, cond_rows, me, count, layer_output,
        down_sum, down_bias_grad,
    )


def mlp_back(
    branch_grad, down_full, hidden_pre, normed_mlp, up_full, middle, scale_mlp, shift_mlp,
    upstream, attended, gamma_attn, context, proj_full, head_shape, queries, key_rows,
    value_rows, logsum, allowed, query_pre, query_gain, key_pre, key_gain, sequences,
    length, width, normed_attn, qkv_full, input_rows, scale_attn, shift_attn,
    gamma_mlp_grad, activated_mine, w_ada, cond_rows, me, count, layer_output,
    down_sum, down_bias_grad,
):
    hidden_grad = matmul_back(branch_grad, down_full)
    gelu_pull = jax.vjp(gelu_tanh, hidden_pre)[1]
    pre_grad = gelu_pull(hidden_grad)[0].astype(jnp.bfloat16)
    up_grad = weight_grad(normed_mlp, pre_grad)
    up_bias_grad = jnp.sum(pre_grad.astype(jnp.float32), axis=(0, 1))
    normed_mlp_grad = matmul_back(pre_grad, up_full)
    mlp_pull = jax.vjp(modulate, middle, scale_mlp, shift_mlp)[1]
    middle_part, scale_mlp_grad, shift_mlp_grad = mlp_pull(normed_mlp_grad)
    middle_grad = upstream + middle_part
    gamma_attn_grad = jnp.sum(middle_grad * attended, axis=1)
    attended_grad = (middle_grad * gamma_attn[:, None, :]).astype(jnp.bfloat16)
    proj_grad = weight_grad(context, attended_grad)
    proj_bias_grad = jnp.sum(attended_grad.astype(jnp.float32), axis=(0, 1))
    both_sum = scatter_natural(jnp.concatenate([up_grad, proj_grad], axis=1))
    up_sum = both_sum[:, : up_grad.shape[1]]
    proj_sum = both_sum[:, up_grad.shape[1] :]
    context_gradient = (
        matmul_back(attended_grad, proj_full).astype(jnp.bfloat16).reshape(head_shape)
    )
    query_grad, key_grad, value_grad = jax.vmap(
        lambda q, k, v, l, c: attend_backward(q, k, v, l, c, allowed)
    )(queries, key_rows, value_rows, logsum, context_gradient)
    query_pull = jax.vjp(head_norm, query_pre, query_gain)[1]
    query_pre_grad, query_gain_grad = query_pull(query_grad)
    key_pull = jax.vjp(head_norm, key_pre, key_gain)[1]
    key_pre_grad, key_gain_grad = key_pull(key_grad)
    value_grad = value_grad.reshape(sequences, length, width)
    query_bias_grad = jnp.sum(query_pre_grad, axis=(0, 1))
    value_bias_grad = jnp.sum(value_grad, axis=(0, 1))
    projected_grad = jnp.concatenate([query_pre_grad, key_pre_grad, value_grad], axis=2).astype(
        jnp.bfloat16
    )
    qkv_grad = weight_grad(normed_attn, projected_grad)
    qkv_sum = scatter_natural(qkv_grad)
    (
        query_bias_sum,
        value_bias_sum,
        query_gain_sum,
        key_gain_sum,
        proj_bias_sum,
        up_bias_sum,
        down_bias_sum,
    ) = sum_small(
        (
            query_bias_grad,
            value_bias_grad,
            query_gain_grad,
            key_gain_grad,
            proj_bias_grad,
            up_bias_grad,
            down_bias_grad,
        ),
        count,
    )
    return tail(
        projected_grad, qkv_full, input_rows, scale_attn, shift_attn, middle_grad,
        gamma_attn_grad, gamma_mlp_grad, scale_mlp_grad, shift_mlp_grad, activated_mine,
        w_ada, cond_rows, me, count, layer_output, qkv_sum, query_bias_sum, value_bias_sum,
        query_gain_sum, key_gain_sum, proj_sum, proj_bias_sum, up_sum, up_bias_sum, down_sum,
        down_bias_sum,
    )


def tail(
    projected_grad, qkv_full, input_rows, scale_attn, shift_attn, middle_grad,
    gamma_attn_grad, gamma_mlp_grad, scale_mlp_grad, shift_mlp_grad, activated_mine,
    w_ada, cond_rows, me, count, layer_output, qkv_sum, query_bias_sum, value_bias_sum,
    query_gain_sum, key_gain_sum, proj_sum, proj_bias_sum, up_sum, up_bias_sum, down_sum,
    down_bias_sum,
):
    ada_cols = w_ada.shape[1]
    normed_attn_grad = matmul_back(projected_grad, qkv_full)
    attn_pull = jax.vjp(modulate, input_rows, scale_attn, shift_attn)[1]
    input_part, scale_attn_grad, shift_attn_grad = attn_pull(normed_attn_grad)
    input_grad = middle_grad + input_part
    adaptive_grad = jnp.concatenate(
        [
            gamma_attn_grad,
            gamma_mlp_grad,
            scale_attn_grad,
            scale_mlp_grad,
            shift_attn_grad,
            shift_mlp_grad,
        ],
        axis=1,
    ).astype(jnp.bfloat16)
    adaptive_grad_all = nested_gather(adaptive_grad)
    ada_sum = jnp.einsum(
        "sc,sn->cn", activated_mine, adaptive_grad_all, preferred_element_type=jnp.float32
    )
    bias_share = ada_cols // count
    ada_bias_sum = jnp.sum(
        lax.dynamic_slice_in_dim(adaptive_grad_all, me * bias_share, bias_share, axis=1).astype(
            jnp.float32
        ),
        axis=0,
    )
    activated_grad_cols = jnp.einsum(
        "sn,cn->sc", adaptive_grad_all, w_ada, preferred_element_type=jnp.float32
    )
    activated_grad = lax.all_to_all(
        activated_grad_cols, AXES, split_axis=0, concat_axis=1, tiled=True
    )
    silu_pull = jax.vjp(jax.nn.silu, cond_rows)[1]
    condition_grad = silu_pull(activated_grad)[0]
    return (
        layer_output,
        input_grad,
        condition_grad,
        ada_sum,
        ada_bias_sum,
        qkv_sum,
        query_bias_sum,
        value_bias_sum,
        query_gain_sum,
        key_gain_sum,
        proj_sum,
        proj_bias_sum,
        up_sum,
        up_bias_sum,
        down_sum,
        down_bias_sum,
    )


def solution(mesh):
    row = P(AXES, None, None)
    mat = P(AXES, None)
    vec = P(AXES)
    return jax.shard_map(
        layer,
        mesh=mesh,
        in_specs=(row, mat, P(), mat, vec, mat, vec, vec, vec, vec, mat, vec, mat, vec, mat, vec, row),
        out_specs=(row, row, mat, mat, vec, mat, vec, vec, vec, vec, mat, vec, mat, vec, mat, vec),
        check_vma=False,
    )
```

```python
import jax
import jax.numpy as jnp
from jax import lax
from jax.sharding import Mesh, PartitionSpec as P


HEADS = 16
HEAD_DIM = 64
SEQ_LEN = 680
WIDE = ("outer", "core")
AXES = ("outer", "core", "narrow")

EPSILON = 1e-06
MASKED = -1000000000.0


def layer_norm(values):
    centred = values - jnp.mean(values, axis=-1, keepdims=True)
    return centred * lax.rsqrt(jnp.mean(centred * centred, axis=-1, keepdims=True) + EPSILON)


def modulate(values, scaling, offset):
    return layer_norm(values) * (1.0 + scaling[:, None, :]) + offset[:, None, :]


def head_norm(values, channel_gain):
    shaped = values.reshape(values.shape[0], values.shape[1], HEADS, HEAD_DIM)
    scaled = shaped * lax.rsqrt(jnp.mean(shaped * shaped, axis=-1, keepdims=True) + EPSILON)
    return scaled * channel_gain.reshape(HEADS, HEAD_DIM)


def gelu_tanh(values):
    return jax.nn.gelu(values, approximate=True)


def block_mask(scale_tokens):
    block_ends = jnp.cumsum(scale_tokens)
    places = jnp.arange(SEQ_LEN, dtype=jnp.int32)
    limits = jnp.min(
        jnp.where(block_ends[None, :] > places[:, None], block_ends[None, :], SEQ_LEN), axis=1
    )
    return places[None, :] < limits[:, None]


def matmul_rows(first_operand, second_operand):
    return jnp.einsum(
        "fyg,gq->fyq", first_operand, second_operand, preferred_element_type=jnp.float32
    )


def matmul_back(first_operand, second_operand):
    return jnp.einsum(
        "rfw,uw->rfu", first_operand, second_operand, preferred_element_type=jnp.float32
    )


def weight_grad(first_operand, second_operand):
    return jnp.einsum(
        "crk,cre->ke", first_operand, second_operand, preferred_element_type=jnp.float32
    )


def masked_scores(query_sequence, key_sequence, allowed):
    scores = jnp.einsum(
        "nkz,vkz->knv", query_sequence, key_sequence, preferred_element_type=jnp.float32
    ) * HEAD_DIM ** (-0.5)
    return jnp.where(allowed[None], scores, MASKED)


def attend_forward(query_sequence, key_sequence, value_sequence, allowed):
    scores = masked_scores(query_sequence, key_sequence, allowed)
    row_max = jnp.max(scores, axis=-1, keepdims=True)
    exponent = jnp.exp(scores - row_max)
    row_total = jnp.sum(exponent, axis=-1, keepdims=True)
    probabilities_reduced = (exponent / row_total).astype(jnp.bfloat16)
    context = jnp.einsum(
        "wcv,vwn->cwn", probabilities_reduced, value_sequence, preferred_element_type=jnp.float32
    ).astype(jnp.bfloat16)
    return (context, row_max[..., 0] + jnp.log(row_total[..., 0]))


def attend_backward(
    query_sequence, key_sequence, value_sequence, logsum, context_gradient, allowed
):
    scores = masked_scores(query_sequence, key_sequence, allowed)
    attention_probabilities = jnp.exp(scores - logsum[..., None])
    prob_grad = jnp.einsum(
        "nkz,vkz->knv", context_gradient, value_sequence, preferred_element_type=jnp.float32
    )
    value_grad = jnp.einsum(
        "fgs,gfu->sfu",
        attention_probabilities.astype(jnp.bfloat16),
        context_gradient,
        preferred_element_type=jnp.float32,
    )
    score_gradient = (
        attention_probabilities
        * (prob_grad - jnp.sum(prob_grad * attention_probabilities, axis=-1, keepdims=True))
    ).astype(jnp.bfloat16)
    query_grad = jnp.einsum(
        "wcv,vwn->cwn", score_gradient, key_sequence, preferred_element_type=jnp.float32
    ) * HEAD_DIM ** (-0.5)
    key_grad = jnp.einsum(
        "fgs,gfu->sfu", score_gradient, query_sequence, preferred_element_type=jnp.float32
    ) * HEAD_DIM ** (-0.5)
    return (query_grad, key_grad, value_grad)


def nested_gather(member):
    return lax.all_gather(
        lax.all_gather(member, "narrow", axis=0, tiled=True), WIDE, axis=0, tiled=True
    )


def narrow_sum(half):
    size = lax.axis_size("narrow")
    if size != 2:
        return lax.psum_scatter(half, "narrow", scatter_dimension=0, tiled=True).astype(jnp.float32)
    rows = half.shape[0] // 2
    here = lax.axis_index("narrow")
    keep = lax.dynamic_slice_in_dim(half, here * rows, rows, axis=0)
    send = lax.dynamic_slice_in_dim(half, (1 - here) * rows, rows, axis=0)
    got = lax.ppermute(send, "narrow", [(0, 1), (1, 0)])
    return keep.astype(jnp.float32) + got.astype(jnp.float32)


def scatter_natural(member):
    outer, narrow = lax.axis_size("outer"), lax.axis_size("narrow")
    rows = member.shape[0] // (outer * 2 * narrow)
    blocks = member.reshape((outer, 2, narrow * rows) + member.shape[1:])
    here = lax.axis_index("core")
    keep = lax.dynamic_index_in_dim(blocks, here, 1, keepdims=False)
    send = lax.dynamic_index_in_dim(blocks, 1 - here, 1, keepdims=False)
    got = lax.ppermute(send.astype(jnp.bfloat16), "core", [(0, 1), (1, 0)])
    chip = (keep.astype(jnp.float32) + got.astype(jnp.float32)).astype(jnp.bfloat16)
    chip = chip.reshape((outer * narrow * rows,) + member.shape[1:])
    half = lax.psum_scatter(chip, "outer", scatter_dimension=0, tiled=True)
    return narrow_sum(half)


def sum_small(vectors, count):
    small = jnp.concatenate([v.reshape(count, -1) for v in vectors], axis=1)
    parts = lax.all_to_all(
        small.reshape(count, 1, small.shape[1]), AXES, split_axis=0, concat_axis=0, tiled=True
    )
    total = jnp.sum(parts, axis=0)[0]
    out, offset = [], 0
    for v in vectors:
        size = v.shape[0] // count
        out.append(total[offset : offset + size])
        offset += size
    return out


def layer(
    inputs,
    condition,
    scale_tokens,
    w_ada,
    bias_ada,
    w_qkv,
    bias_query,
    bias_value,
    gain_query,
    gain_key,
    w_proj,
    bias_proj,
    w_up,
    bias_up,
    w_down,
    bias_down,
    cotangent,
):
    count = lax.axis_size("outer") * 2 * lax.axis_size("narrow")
    me = (lax.axis_index("outer") * 2 + lax.axis_index("core")) * lax.axis_size(
        "narrow"
    ) + lax.axis_index("narrow")
    sequences, length, width = inputs.shape
    head_shape = (sequences, length, HEADS, HEAD_DIM)
    cond_rows = condition.astype(jnp.float32)
    activated = jax.nn.silu(cond_rows).astype(jnp.bfloat16)
    vectors = (bias_ada, bias_query, bias_value, gain_query, gain_key, bias_proj, bias_up, bias_down)
    small = nested_gather(
        jnp.concatenate([activated.reshape(-1)] + list(vectors))[None, :]
    )
    activated_all = small[:, : activated.size].reshape(count * sequences, activated.shape[1])
    unpacked, start = [], activated.size
    for member in vectors:
        size = member.shape[0]
        unpacked.append(small[:, start : start + size].reshape(count * size).astype(jnp.float32))
        start += size
    ada_bias, query_bias, value_bias, query_gain, key_gain, proj_bias, up_bias, down_bias = unpacked
    first = lax.all_gather(
        jnp.concatenate([w_qkv, w_proj, w_up], axis=1), AXES, axis=0, tiled=True
    )
    qkv_cols, proj_cols = w_qkv.shape[1], w_proj.shape[1]
    qkv_full = first[:, :qkv_cols]
    proj_full = first[:, qkv_cols : qkv_cols + proj_cols]
    up_full = first[:, qkv_cols + proj_cols :]
    down_full = lax.all_gather(w_down, AXES, axis=0, tiled=True)
    allowed = block_mask(scale_tokens)
    input_rows = inputs.astype(jnp.float32)
    ada_rows = w_ada.shape[0]
    ada_cols = w_ada.shape[1]
    activated_mine = lax.dynamic_slice_in_dim(activated_all, me * ada_rows, ada_rows, axis=1)
    ada_partial = jnp.dot(activated_mine, w_ada, preferred_element_type=jnp.float32)
    ada_parts = lax.all_to_all(
        ada_partial.reshape(count, sequences, ada_cols), AXES, split_axis=0, concat_axis=0, tiled=True
    )
    adaptive = jnp.sum(ada_parts, axis=0) + ada_bias
    gamma_attn, gamma_mlp, scale_attn, scale_mlp, shift_attn, shift_mlp = jnp.split(
        adaptive, 6, axis=1
    )
    normed_attn = modulate(input_rows, scale_attn, shift_attn).astype(jnp.bfloat16)
    projected = matmul_rows(normed_attn, qkv_full)
    query_pre = projected[..., :width] + query_bias
    key_pre = projected[..., width : 2 * width]
    queries = head_norm(query_pre, query_gain).astype(jnp.bfloat16)
    key_rows = head_norm(key_pre, key_gain).astype(jnp.bfloat16)
    value_rows = (projected[..., 2 * width :] + value_bias).astype(jnp.bfloat16).reshape(head_shape)
    context, logsum = jax.vmap(
        lambda q, k, v: attend_forward(q, k, v, allowed)
    )(queries, key_rows, value_rows)
    context = context.reshape(sequences, length, width)
    attended = matmul_rows(context, proj_full) + proj_bias
    middle = input_rows + gamma_attn[:, None, :] * attended
    normed_mlp = modulate(middle, scale_mlp, shift_mlp).astype(jnp.bfloat16)
    hidden_pre = matmul_rows(normed_mlp, up_full) + up_bias
    hidden = gelu_tanh(hidden_pre).astype(jnp.bfloat16)
    branch = matmul_rows(hidden, down_full) + down_bias
    layer_output = (middle + gamma_mlp[:, None, :] * branch).astype(jnp.bfloat16)
    upstream = cotangent.astype(jnp.float32)
    gamma_mlp_grad = jnp.sum(upstream * branch, axis=1)
    branch_grad = (upstream * gamma_mlp[:, None, :]).astype(jnp.bfloat16)
    down_grad = weight_grad(hidden, branch_grad)
    down_sum = scatter_natural(down_grad)
    down_bias_grad = jnp.sum(branch_grad.astype(jnp.float32), axis=(0, 1))
    return mlp_back(
        branch_grad, down_full, hidden_pre, normed_mlp, up_full, middle, scale_mlp, shift_mlp,
        upstream, attended, gamma_attn, context, proj_full, head_shape, queries, key_rows,
        value_rows, logsum, allowed, query_pre, query_gain, key_pre, key_gain, sequences,
        length, width, normed_attn, qkv_full, input_rows, scale_attn, shift_attn,
        gamma_mlp_grad, activated_mine, w_ada, cond_rows, me, count, layer_output,
        down_sum, down_bias_grad,
    )


def mlp_back(
    branch_grad, down_full, hidden_pre, normed_mlp, up_full, middle, scale_mlp, shift_mlp,
    upstream, attended, gamma_attn, context, proj_full, head_shape, queries, key_rows,
    value_rows, logsum, allowed, query_pre, query_gain, key_pre, key_gain, sequences,
    length, width, normed_attn, qkv_full, input_rows, scale_attn, shift_attn,
    gamma_mlp_grad, activated_mine, w_ada, cond_rows, me, count, layer_output,
    down_sum, down_bias_grad,
):
    hidden_grad = matmul_back(branch_grad, down_full)
    gelu_pull = jax.vjp(gelu_tanh, hidden_pre)[1]
    pre_grad = gelu_pull(hidden_grad)[0].astype(jnp.bfloat16)
    up_grad = weight_grad(normed_mlp, pre_grad)
    up_bias_grad = jnp.sum(pre_grad.astype(jnp.float32), axis=(0, 1))
    normed_mlp_grad = matmul_back(pre_grad, up_full)
    mlp_pull = jax.vjp(modulate, middle, scale_mlp, shift_mlp)[1]
    middle_part, scale_mlp_grad, shift_mlp_grad = mlp_pull(normed_mlp_grad)
    middle_grad = upstream + middle_part
    gamma_attn_grad = jnp.sum(middle_grad * attended, axis=1)
    attended_grad = (middle_grad * gamma_attn[:, None, :]).astype(jnp.bfloat16)
    proj_grad = weight_grad(context, attended_grad)
    proj_bias_grad = jnp.sum(attended_grad.astype(jnp.float32), axis=(0, 1))
    both_sum = scatter_natural(jnp.concatenate([up_grad, proj_grad], axis=1))
    up_sum = both_sum[:, : up_grad.shape[1]]
    proj_sum = both_sum[:, up_grad.shape[1] :]
    context_gradient = (
        matmul_back(attended_grad, proj_full).astype(jnp.bfloat16).reshape(head_shape)
    )
    query_grad, key_grad, value_grad = jax.vmap(
        lambda q, k, v, l, c: attend_backward(q, k, v, l, c, allowed)
    )(queries, key_rows, value_rows, logsum, context_gradient)
    query_pull = jax.vjp(head_norm, query_pre, query_gain)[1]
    query_pre_grad, query_gain_grad = query_pull(query_grad)
    key_pull = jax.vjp(head_norm, key_pre, key_gain)[1]
    key_pre_grad, key_gain_grad = key_pull(key_grad)
    value_grad = value_grad.reshape(sequences, length, width)
    query_bias_grad = jnp.sum(query_pre_grad, axis=(0, 1))
    value_bias_grad = jnp.sum(value_grad, axis=(0, 1))
    projected_grad = jnp.concatenate([query_pre_grad, key_pre_grad, value_grad], axis=2).astype(
        jnp.bfloat16
    )
    qkv_grad = weight_grad(normed_attn, projected_grad)
    qkv_sum = scatter_natural(qkv_grad)
    (
        query_bias_sum,
        value_bias_sum,
        query_gain_sum,
        key_gain_sum,
        proj_bias_sum,
        up_bias_sum,
        down_bias_sum,
    ) = sum_small(
        (
            query_bias_grad,
            value_bias_grad,
            query_gain_grad,
            key_gain_grad,
            proj_bias_grad,
            up_bias_grad,
            down_bias_grad,
        ),
        count,
    )
    return tail(
        projected_grad, qkv_full, input_rows, scale_attn, shift_attn, middle_grad,
        gamma_attn_grad, gamma_mlp_grad, scale_mlp_grad, shift_mlp_grad, activated_mine,
        w_ada, cond_rows, me, count, layer_output, qkv_sum, query_bias_sum, value_bias_sum,
        query_gain_sum, key_gain_sum, proj_sum, proj_bias_sum, up_sum, up_bias_sum, down_sum,
        down_bias_sum,
    )


def tail(
    projected_grad, qkv_full, input_rows, scale_attn, shift_attn, middle_grad,
    gamma_attn_grad, gamma_mlp_grad, scale_mlp_grad, shift_mlp_grad, activated_mine,
    w_ada, cond_rows, me, count, layer_output, qkv_sum, query_bias_sum, value_bias_sum,
    query_gain_sum, key_gain_sum, proj_sum, proj_bias_sum, up_sum, up_bias_sum, down_sum,
    down_bias_sum,
):
    ada_cols = w_ada.shape[1]
    normed_attn_grad = matmul_back(projected_grad, qkv_full)
    attn_pull = jax.vjp(modulate, input_rows, scale_attn, shift_attn)[1]
    input_part, scale_attn_grad, shift_attn_grad = attn_pull(normed_attn_grad)
    input_grad = middle_grad + input_part
    adaptive_grad = jnp.concatenate(
        [
            gamma_attn_grad,
            gamma_mlp_grad,
            scale_attn_grad,
            scale_mlp_grad,
            shift_attn_grad,
            shift_mlp_grad,
        ],
        axis=1,
    ).astype(jnp.bfloat16)
    adaptive_grad_all = nested_gather(adaptive_grad)
    ada_sum = jnp.einsum(
        "sc,sn->cn", activated_mine, adaptive_grad_all, preferred_element_type=jnp.float32
    )
    bias_share = ada_cols // count
    ada_bias_sum = jnp.sum(
        lax.dynamic_slice_in_dim(adaptive_grad_all, me * bias_share, bias_share, axis=1).astype(
            jnp.float32
        ),
        axis=0,
    )
    activated_grad_cols = jnp.einsum(
        "sn,cn->sc", adaptive_grad_all, w_ada, preferred_element_type=jnp.float32
    )
    activated_grad = lax.all_to_all(
        activated_grad_cols, AXES, split_axis=0, concat_axis=1, tiled=True
    )
    silu_pull = jax.vjp(jax.nn.silu, cond_rows)[1]
    condition_grad = silu_pull(activated_grad)[0]
    return (
        layer_output,
        input_grad,
        condition_grad,
        ada_sum,
        ada_bias_sum,
        qkv_sum,
        query_bias_sum,
        value_bias_sum,
        query_gain_sum,
        key_gain_sum,
        proj_sum,
        proj_bias_sum,
        up_sum,
        up_bias_sum,
        down_sum,
        down_bias_sum,
    )


def solution(mesh):
    wide, narrow = mesh.shape["wide"], mesh.shape["narrow"]
    mesh = Mesh(mesh.devices.reshape(wide // 2, 2, narrow), AXES)
    row = P(AXES, None, None)
    mat = P(AXES, None)
    vec = P(AXES)
    return jax.shard_map(
        layer,
        mesh=mesh,
        in_specs=(row, mat, P(), mat, vec, mat, vec, vec, vec, vec, mat, vec, mat, vec, mat, vec, row),
        out_specs=(row, row, mat, mat, vec, mat, vec, vec, vec, vec, mat, vec, mat, vec, mat, vec),
        check_vma=False,
    )
```

```python
import jax
import jax.numpy as jnp
from jax import lax
from jax.experimental import pallas as pl
from jax.sharding import PartitionSpec as P


HEADS = 16
HEAD_DIM = 64
SEQ_LEN = 680
AXES = ("wide", "narrow")

EPSILON = 1e-06
MASKED = -1000000000.0


def layer_norm(values):
    centred = values - jnp.mean(values, axis=-1, keepdims=True)
    return centred * lax.rsqrt(jnp.mean(centred * centred, axis=-1, keepdims=True) + EPSILON)


def modulate(values, scaling, offset):
    return layer_norm(values) * (1.0 + scaling[:, None, :]) + offset[:, None, :]


def head_norm(values, channel_gain):
    shaped = values.reshape(values.shape[0], values.shape[1], HEADS, HEAD_DIM)
    scaled = shaped * lax.rsqrt(jnp.mean(shaped * shaped, axis=-1, keepdims=True) + EPSILON)
    return scaled * channel_gain.reshape(HEADS, HEAD_DIM)


def gelu_tanh(values):
    return jax.nn.gelu(values, approximate=True)


def block_limits(scale_tokens):
    block_ends = jnp.cumsum(scale_tokens)
    places = jnp.arange(SEQ_LEN, dtype=jnp.int32)
    return jnp.min(
        jnp.where(block_ends[None, :] > places[:, None], block_ends[None, :], SEQ_LEN), axis=1
    )


def block_mask(scale_tokens):
    places = jnp.arange(SEQ_LEN, dtype=jnp.int32)
    return places[None, :] < block_limits(scale_tokens)[:, None]


def attn_kernel(limit_ref, q_ref, k_ref, v_ref, ctx_ref, lse_ref):
    length = q_ref.shape[0]
    dim = q_ref.shape[1] // 2
    cols = lax.broadcasted_iota(jnp.int32, (length, length), 1)
    allowed = cols < limit_ref[...]
    outs = []
    for i in range(2):
        q = q_ref[:, i * dim : (i + 1) * dim]
        k = k_ref[:, i * dim : (i + 1) * dim]
        v = v_ref[:, i * dim : (i + 1) * dim]
        s = lax.dot_general(q, k, (((1,), (1,)), ((), ())), preferred_element_type=jnp.float32)
        s = jnp.where(allowed, s * dim ** (-0.5), MASKED)
        m = jnp.max(s, axis=1, keepdims=True)
        e = jnp.exp(s - m)
        l = jnp.sum(e, axis=1, keepdims=True)
        p = (e / l).astype(jnp.bfloat16)
        outs.append(jnp.dot(p, v, preferred_element_type=jnp.float32).astype(jnp.bfloat16))
        lse_ref[i] = m + jnp.log(l)
    ctx_ref[...] = jnp.concatenate(outs, axis=1)


def attention_forward(queries, keys, values, limits, heads):
    length, width = queries.shape
    pair = 2 * (width // heads)
    spec = pl.BlockSpec((length, pair), lambda h: (0, h))
    return pl.pallas_call(
        attn_kernel,
        grid=(heads // 2,),
        in_specs=[pl.BlockSpec((length, 1), lambda h: (0, 0)), spec, spec, spec],
        out_specs=[spec, pl.BlockSpec((2, length, 1), lambda h: (h, 0, 0))],
        out_shape=[
            jax.ShapeDtypeStruct((length, width), jnp.bfloat16),
            jax.ShapeDtypeStruct((heads, length, 1), jnp.float32),
        ],
        cost_estimate=pl.CostEstimate(
            flops=4 * length * length * width,
            transcendentals=heads * length * length,
            bytes_accessed=4 * length * width * 2 + heads * length * 4,
        ),
    )(limits, queries, keys, values)


def matmul_rows(first_operand, second_operand):
    return jnp.einsum(
        "fyg,gq->fyq", first_operand, second_operand, preferred_element_type=jnp.float32
    )


def matmul_back(first_operand, second_operand):
    return jnp.einsum(
        "rfw,uw->rfu", first_operand, second_operand, preferred_element_type=jnp.float32
    )


def weight_grad(first_operand, second_operand):
    return jnp.einsum(
        "crk,cre->ke", first_operand, second_operand, preferred_element_type=jnp.float32
    )


def masked_scores(query_sequence, key_sequence, allowed):
    scores = jnp.einsum(
        "nkz,vkz->knv", query_sequence, key_sequence, preferred_element_type=jnp.float32
    ) * HEAD_DIM ** (-0.5)
    return jnp.where(allowed[None], scores, MASKED)


def attend_backward(
    query_sequence, key_sequence, value_sequence, logsum, context_gradient, allowed
):
    scores = masked_scores(query_sequence, key_sequence, allowed)
    attention_probabilities = jnp.exp(scores - logsum[..., None])
    prob_grad = jnp.einsum(
        "nkz,vkz->knv", context_gradient, value_sequence, preferred_element_type=jnp.float32
    )
    value_grad = jnp.einsum(
        "fgs,gfu->sfu",
        attention_probabilities.astype(jnp.bfloat16),
        context_gradient,
        preferred_element_type=jnp.float32,
    )
    score_gradient = (
        attention_probabilities
        * (prob_grad - jnp.sum(prob_grad * attention_probabilities, axis=-1, keepdims=True))
    ).astype(jnp.bfloat16)
    query_grad = jnp.einsum(
        "wcv,vwn->cwn", score_gradient, key_sequence, preferred_element_type=jnp.float32
    ) * HEAD_DIM ** (-0.5)
    key_grad = jnp.einsum(
        "fgs,gfu->sfu", score_gradient, query_sequence, preferred_element_type=jnp.float32
    ) * HEAD_DIM ** (-0.5)
    return (query_grad, key_grad, value_grad)


def nested_gather(member):
    return lax.all_gather(
        lax.all_gather(member, "narrow", axis=0, tiled=True), "wide", axis=0, tiled=True
    )


def narrow_sum(half):
    size = lax.axis_size("narrow")
    if size != 2:
        return lax.psum_scatter(half, "narrow", scatter_dimension=0, tiled=True).astype(jnp.float32)
    rows = half.shape[0] // 2
    here = lax.axis_index("narrow")
    keep = lax.dynamic_slice_in_dim(half, here * rows, rows, axis=0)
    send = lax.dynamic_slice_in_dim(half, (1 - here) * rows, rows, axis=0)
    got = lax.ppermute(send, "narrow", [(0, 1), (1, 0)])
    return keep.astype(jnp.float32) + got.astype(jnp.float32)


def scatter_natural(member):
    half = lax.psum_scatter(member.astype(jnp.bfloat16), "wide", scatter_dimension=0, tiled=True)
    return narrow_sum(half)


def sum_small(vectors, count):
    small = jnp.concatenate([v.reshape(count, -1) for v in vectors], axis=1)
    parts = lax.all_to_all(
        small.reshape(count, 1, small.shape[1]), AXES, split_axis=0, concat_axis=0, tiled=True
    )
    total = jnp.sum(parts, axis=0)[0]
    out, offset = [], 0
    for v in vectors:
        size = v.shape[0] // count
        out.append(total[offset : offset + size])
        offset += size
    return out


def layer(
    inputs,
    condition,
    scale_tokens,
    w_ada,
    bias_ada,
    w_qkv,
    bias_query,
    bias_value,
    gain_query,
    gain_key,
    w_proj,
    bias_proj,
    w_up,
    bias_up,
    w_down,
    bias_down,
    cotangent,
):
    count = lax.axis_size("wide") * lax.axis_size("narrow")
    me = lax.axis_index("wide") * lax.axis_size("narrow") + lax.axis_index("narrow")
    sequences, length, width = inputs.shape
    head_shape = (sequences, length, HEADS, HEAD_DIM)
    cond_rows = condition.astype(jnp.float32)
    activated = jax.nn.silu(cond_rows).astype(jnp.bfloat16)
    vectors = (bias_ada, bias_query, bias_value, gain_query, gain_key, bias_proj, bias_up, bias_down)
    small = nested_gather(
        jnp.concatenate([activated.reshape(-1)] + list(vectors))[None, :]
    )
    activated_all = small[:, : activated.size].reshape(count * sequences, activated.shape[1])
    unpacked, start = [], activated.size
    for member in vectors:
        size = member.shape[0]
        unpacked.append(small[:, start : start + size].reshape(count * size).astype(jnp.float32))
        start += size
    ada_bias, query_bias, value_bias, query_gain, key_gain, proj_bias, up_bias, down_bias = unpacked
    first = lax.all_gather(
        jnp.concatenate([w_qkv, w_proj, w_up], axis=1), AXES, axis=0, tiled=True
    )
    qkv_cols, proj_cols = w_qkv.shape[1], w_proj.shape[1]
    qkv_full = first[:, :qkv_cols]
    proj_full = first[:, qkv_cols : qkv_cols + proj_cols]
    up_full = first[:, qkv_cols + proj_cols :]
    down_full = lax.all_gather(w_down, AXES, axis=0, tiled=True)
    allowed = block_mask(scale_tokens)
    input_rows = inputs.astype(jnp.float32)
    ada_rows = w_ada.shape[0]
    ada_cols = w_ada.shape[1]
    activated_mine = lax.dynamic_slice_in_dim(activated_all, me * ada_rows, ada_rows, axis=1)
    ada_partial = jnp.dot(activated_mine, w_ada, preferred_element_type=jnp.float32)
    ada_parts = lax.all_to_all(
        ada_partial.reshape(count, sequences, ada_cols), AXES, split_axis=0, concat_axis=0, tiled=True
    )
    adaptive = jnp.sum(ada_parts, axis=0) + ada_bias
    gamma_attn, gamma_mlp, scale_attn, scale_mlp, shift_attn, shift_mlp = jnp.split(
        adaptive, 6, axis=1
    )
    normed_attn = modulate(input_rows, scale_attn, shift_attn).astype(jnp.bfloat16)
    projected = matmul_rows(normed_attn, qkv_full)
    query_pre = projected[..., :width] + query_bias
    key_pre = projected[..., width : 2 * width]
    queries = head_norm(query_pre, query_gain).astype(jnp.bfloat16)
    key_rows = head_norm(key_pre, key_gain).astype(jnp.bfloat16)
    value_rows = (projected[..., 2 * width :] + value_bias).astype(jnp.bfloat16).reshape(head_shape)
    limits = block_limits(scale_tokens).astype(jnp.int32)[:, None]
    context, logsum = attention_forward(
        queries.reshape(length, width),
        key_rows.reshape(length, width),
        value_rows.reshape(length, width),
        limits,
        HEADS,
    )
    context = context.reshape(sequences, length, width)
    logsum = logsum.reshape(sequences, HEADS, length)
    attended = matmul_rows(context, proj_full) + proj_bias
    middle = input_rows + gamma_attn[:, None, :] * attended
    normed_mlp = modulate(middle, scale_mlp, shift_mlp).astype(jnp.bfloat16)
    hidden_pre = matmul_rows(normed_mlp, up_full) + up_bias
    hidden = gelu_tanh(hidden_pre).astype(jnp.bfloat16)
    branch = matmul_rows(hidden, down_full) + down_bias
    layer_output = (middle + gamma_mlp[:, None, :] * branch).astype(jnp.bfloat16)
    upstream = cotangent.astype(jnp.float32)
    gamma_mlp_grad = jnp.sum(upstream * branch, axis=1)
    branch_grad = (upstream * gamma_mlp[:, None, :]).astype(jnp.bfloat16)
    down_grad = weight_grad(hidden, branch_grad)
    down_sum = scatter_natural(down_grad)
    down_bias_grad = jnp.sum(branch_grad.astype(jnp.float32), axis=(0, 1))
    return mlp_back(
        branch_grad, down_full, hidden_pre, normed_mlp, up_full, middle, scale_mlp, shift_mlp,
        upstream, attended, gamma_attn, context, proj_full, head_shape, queries, key_rows,
        value_rows, logsum, allowed, query_pre, query_gain, key_pre, key_gain, sequences,
        length, width, normed_attn, qkv_full, input_rows, scale_attn, shift_attn,
        gamma_mlp_grad, activated_mine, w_ada, cond_rows, me, count, layer_output,
        down_sum, down_bias_grad,
    )


def mlp_back(
    branch_grad, down_full, hidden_pre, normed_mlp, up_full, middle, scale_mlp, shift_mlp,
    upstream, attended, gamma_attn, context, proj_full, head_shape, queries, key_rows,
    value_rows, logsum, allowed, query_pre, query_gain, key_pre, key_gain, sequences,
    length, width, normed_attn, qkv_full, input_rows, scale_attn, shift_attn,
    gamma_mlp_grad, activated_mine, w_ada, cond_rows, me, count, layer_output,
    down_sum, down_bias_grad,
):
    hidden_grad = matmul_back(branch_grad, down_full)
    gelu_pull = jax.vjp(gelu_tanh, hidden_pre)[1]
    pre_grad = gelu_pull(hidden_grad)[0].astype(jnp.bfloat16)
    up_grad = weight_grad(normed_mlp, pre_grad)
    up_bias_grad = jnp.sum(pre_grad.astype(jnp.float32), axis=(0, 1))
    normed_mlp_grad = matmul_back(pre_grad, up_full)
    mlp_pull = jax.vjp(modulate, middle, scale_mlp, shift_mlp)[1]
    middle_part, scale_mlp_grad, shift_mlp_grad = mlp_pull(normed_mlp_grad)
    middle_grad = upstream + middle_part
    gamma_attn_grad = jnp.sum(middle_grad * attended, axis=1)
    attended_grad = (middle_grad * gamma_attn[:, None, :]).astype(jnp.bfloat16)
    proj_grad = weight_grad(context, attended_grad)
    proj_bias_grad = jnp.sum(attended_grad.astype(jnp.float32), axis=(0, 1))
    both_sum = scatter_natural(jnp.concatenate([up_grad, proj_grad], axis=1))
    up_sum = both_sum[:, : up_grad.shape[1]]
    proj_sum = both_sum[:, up_grad.shape[1] :]
    context_gradient = (
        matmul_back(attended_grad, proj_full).astype(jnp.bfloat16).reshape(head_shape)
    )
    query_grad, key_grad, value_grad = jax.vmap(
        lambda q, k, v, l, c: attend_backward(q, k, v, l, c, allowed)
    )(queries, key_rows, value_rows, logsum, context_gradient)
    query_pull = jax.vjp(head_norm, query_pre, query_gain)[1]
    query_pre_grad, query_gain_grad = query_pull(query_grad)
    key_pull = jax.vjp(head_norm, key_pre, key_gain)[1]
    key_pre_grad, key_gain_grad = key_pull(key_grad)
    value_grad = value_grad.reshape(sequences, length, width)
    query_bias_grad = jnp.sum(query_pre_grad, axis=(0, 1))
    value_bias_grad = jnp.sum(value_grad, axis=(0, 1))
    projected_grad = jnp.concatenate([query_pre_grad, key_pre_grad, value_grad], axis=2).astype(
        jnp.bfloat16
    )
    qkv_grad = weight_grad(normed_attn, projected_grad)
    qkv_sum = scatter_natural(qkv_grad)
    (
        query_bias_sum,
        value_bias_sum,
        query_gain_sum,
        key_gain_sum,
        proj_bias_sum,
        up_bias_sum,
        down_bias_sum,
    ) = sum_small(
        (
            query_bias_grad,
            value_bias_grad,
            query_gain_grad,
            key_gain_grad,
            proj_bias_grad,
            up_bias_grad,
            down_bias_grad,
        ),
        count,
    )
    return tail(
        projected_grad, qkv_full, input_rows, scale_attn, shift_attn, middle_grad,
        gamma_attn_grad, gamma_mlp_grad, scale_mlp_grad, shift_mlp_grad, activated_mine,
        w_ada, cond_rows, me, count, layer_output, qkv_sum, query_bias_sum, value_bias_sum,
        query_gain_sum, key_gain_sum, proj_sum, proj_bias_sum, up_sum, up_bias_sum, down_sum,
        down_bias_sum,
    )


def tail(
    projected_grad, qkv_full, input_rows, scale_attn, shift_attn, middle_grad,
    gamma_attn_grad, gamma_mlp_grad, scale_mlp_grad, shift_mlp_grad, activated_mine,
    w_ada, cond_rows, me, count, layer_output, qkv_sum, query_bias_sum, value_bias_sum,
    query_gain_sum, key_gain_sum, proj_sum, proj_bias_sum, up_sum, up_bias_sum, down_sum,
    down_bias_sum,
):
    ada_cols = w_ada.shape[1]
    normed_attn_grad = matmul_back(projected_grad, qkv_full)
    attn_pull = jax.vjp(modulate, input_rows, scale_attn, shift_attn)[1]
    input_part, scale_attn_grad, shift_attn_grad = attn_pull(normed_attn_grad)
    input_grad = middle_grad + input_part
    adaptive_grad = jnp.concatenate(
        [
            gamma_attn_grad,
            gamma_mlp_grad,
            scale_attn_grad,
            scale_mlp_grad,
            shift_attn_grad,
            shift_mlp_grad,
        ],
        axis=1,
    ).astype(jnp.bfloat16)
    adaptive_grad_all = nested_gather(adaptive_grad)
    ada_sum = jnp.einsum(
        "sc,sn->cn", activated_mine, adaptive_grad_all, preferred_element_type=jnp.float32
    )
    bias_share = ada_cols // count
    ada_bias_sum = jnp.sum(
        lax.dynamic_slice_in_dim(adaptive_grad_all, me * bias_share, bias_share, axis=1).astype(
            jnp.float32
        ),
        axis=0,
    )
    activated_grad_cols = jnp.einsum(
        "sn,cn->sc", adaptive_grad_all, w_ada, preferred_element_type=jnp.float32
    )
    activated_grad = lax.all_to_all(
        activated_grad_cols, AXES, split_axis=0, concat_axis=1, tiled=True
    )
    silu_pull = jax.vjp(jax.nn.silu, cond_rows)[1]
    condition_grad = silu_pull(activated_grad)[0]
    return (
        layer_output,
        input_grad,
        condition_grad,
        ada_sum,
        ada_bias_sum,
        qkv_sum,
        query_bias_sum,
        value_bias_sum,
        query_gain_sum,
        key_gain_sum,
        proj_sum,
        proj_bias_sum,
        up_sum,
        up_bias_sum,
        down_sum,
        down_bias_sum,
    )


def solution(mesh):
    row = P(AXES, None, None)
    mat = P(AXES, None)
    vec = P(AXES)
    return jax.shard_map(
        layer,
        mesh=mesh,
        in_specs=(row, mat, P(), mat, vec, mat, vec, vec, vec, vec, mat, vec, mat, vec, mat, vec, row),
        out_specs=(row, row, mat, mat, vec, mat, vec, vec, vec, vec, mat, vec, mat, vec, mat, vec),
        check_vma=False,
    )
```

```python
import jax
import jax.numpy as jnp
from jax import lax
from jax.sharding import PartitionSpec as P


HEADS = 16
HEAD_DIM = 64
SEQ_LEN = 680
AXES = ("wide", "narrow")

EPSILON = 1e-06
MASKED = -1000000000.0


def layer_norm(values):
    centred = values - jnp.mean(values, axis=-1, keepdims=True)
    return centred * lax.rsqrt(jnp.mean(centred * centred, axis=-1, keepdims=True) + EPSILON)


def modulate(values, scaling, offset):
    return layer_norm(values) * (1.0 + scaling[:, None, :]) + offset[:, None, :]


def head_norm(values, channel_gain):
    shaped = values.reshape(values.shape[0], values.shape[1], HEADS, HEAD_DIM)
    scaled = shaped * lax.rsqrt(jnp.mean(shaped * shaped, axis=-1, keepdims=True) + EPSILON)
    return scaled * channel_gain.reshape(HEADS, HEAD_DIM)


def gelu_tanh(values):
    return jax.nn.gelu(values, approximate=True)


def block_mask(scale_tokens):
    block_ends = jnp.cumsum(scale_tokens)
    places = jnp.arange(SEQ_LEN, dtype=jnp.int32)
    limits = jnp.min(
        jnp.where(block_ends[None, :] > places[:, None], block_ends[None, :], SEQ_LEN), axis=1
    )
    return places[None, :] < limits[:, None]


def matmul_rows(first_operand, second_operand):
    return jnp.einsum(
        "fyg,gq->fyq", first_operand, second_operand, preferred_element_type=jnp.float32
    )


def matmul_back(first_operand, second_operand):
    return jnp.einsum(
        "rfw,uw->rfu", first_operand, second_operand, preferred_element_type=jnp.float32
    )


def weight_grad(first_operand, second_operand):
    return jnp.einsum(
        "crk,cre->ke", first_operand, second_operand, preferred_element_type=jnp.float32
    )


def masked_scores(query_sequence, key_sequence, allowed):
    scores = jnp.einsum(
        "nkz,vkz->knv", query_sequence, key_sequence, preferred_element_type=jnp.float32
    ) * HEAD_DIM ** (-0.5)
    return jnp.where(allowed[None], scores, MASKED)


def attend_forward(query_sequence, key_sequence, value_sequence, allowed):
    scores = masked_scores(query_sequence, key_sequence, allowed)
    row_max = jnp.max(scores, axis=-1, keepdims=True)
    exponent = jnp.exp(scores - row_max)
    row_total = jnp.sum(exponent, axis=-1, keepdims=True)
    probabilities_reduced = (exponent / row_total).astype(jnp.bfloat16)
    context = jnp.einsum(
        "wcv,vwn->cwn", probabilities_reduced, value_sequence, preferred_element_type=jnp.float32
    ).astype(jnp.bfloat16)
    return (context, row_max[..., 0] + jnp.log(row_total[..., 0]))


def attend_backward(
    query_sequence, key_sequence, value_sequence, logsum, context_gradient, allowed
):
    scores = masked_scores(query_sequence, key_sequence, allowed)
    attention_probabilities = jnp.exp(scores - logsum[..., None])
    prob_grad = jnp.einsum(
        "nkz,vkz->knv", context_gradient, value_sequence, preferred_element_type=jnp.float32
    )
    value_grad = jnp.einsum(
        "fgs,gfu->sfu",
        attention_probabilities.astype(jnp.bfloat16),
        context_gradient,
        preferred_element_type=jnp.float32,
    )
    score_gradient = (
        attention_probabilities
        * (prob_grad - jnp.sum(prob_grad * attention_probabilities, axis=-1, keepdims=True))
    ).astype(jnp.bfloat16)
    query_grad = jnp.einsum(
        "wcv,vwn->cwn", score_gradient, key_sequence, preferred_element_type=jnp.float32
    ) * HEAD_DIM ** (-0.5)
    key_grad = jnp.einsum(
        "fgs,gfu->sfu", score_gradient, query_sequence, preferred_element_type=jnp.float32
    ) * HEAD_DIM ** (-0.5)
    return (query_grad, key_grad, value_grad)


def nested_gather(member):
    return lax.all_gather(
        lax.all_gather(member, "narrow", axis=0, tiled=True), "wide", axis=0, tiled=True
    )


def narrow_sum(half):
    size = lax.axis_size("narrow")
    if size != 2:
        return lax.psum_scatter(half, "narrow", scatter_dimension=0, tiled=True).astype(jnp.float32)
    rows = half.shape[0] // 2
    here = lax.axis_index("narrow")
    keep = lax.dynamic_slice_in_dim(half, here * rows, rows, axis=0)
    send = lax.dynamic_slice_in_dim(half, (1 - here) * rows, rows, axis=0)
    got = lax.ppermute(send, "narrow", [(0, 1), (1, 0)])
    return keep.astype(jnp.float32) + got.astype(jnp.float32)


def scatter_natural(member):
    half = lax.psum_scatter(member.astype(jnp.bfloat16), "wide", scatter_dimension=0, tiled=True)
    return narrow_sum(half)


def sum_small(vectors, count):
    small = jnp.concatenate([v.reshape(count, -1) for v in vectors], axis=1)
    parts = lax.all_to_all(
        small.reshape(count, 1, small.shape[1]), AXES, split_axis=0, concat_axis=0, tiled=True
    )
    total = jnp.sum(parts, axis=0)[0]
    out, offset = [], 0
    for v in vectors:
        size = v.shape[0] // count
        out.append(total[offset : offset + size])
        offset += size
    return out


def layer(
    inputs,
    condition,
    scale_tokens,
    w_ada,
    bias_ada,
    w_qkv,
    bias_query,
    bias_value,
    gain_query,
    gain_key,
    w_proj,
    bias_proj,
    w_up,
    bias_up,
    w_down,
    bias_down,
    cotangent,
):
    count = lax.axis_size("wide") * lax.axis_size("narrow")
    me = lax.axis_index("wide") * lax.axis_size("narrow") + lax.axis_index("narrow")
    sequences, length, width = inputs.shape
    head_shape = (sequences, length, HEADS, HEAD_DIM)
    cond_rows = condition.astype(jnp.float32)
    activated = jax.nn.silu(cond_rows).astype(jnp.bfloat16)
    vectors = (bias_ada, bias_query, bias_value, gain_query, gain_key, bias_proj, bias_up, bias_down)
    small = nested_gather(
        jnp.concatenate([activated.reshape(-1)] + list(vectors))[None, :]
    )
    activated_all = small[:, : activated.size].reshape(count * sequences, activated.shape[1])
    unpacked, start = [], activated.size
    for member in vectors:
        size = member.shape[0]
        unpacked.append(small[:, start : start + size].reshape(count * size).astype(jnp.float32))
        start += size
    ada_bias, query_bias, value_bias, query_gain, key_gain, proj_bias, up_bias, down_bias = unpacked
    first = lax.all_gather(
        jnp.concatenate([w_qkv, w_proj, w_up], axis=1), AXES, axis=0, tiled=True
    )
    qkv_cols, proj_cols = w_qkv.shape[1], w_proj.shape[1]
    qkv_full = first[:, :qkv_cols]
    proj_full = first[:, qkv_cols : qkv_cols + proj_cols]
    up_full = first[:, qkv_cols + proj_cols :]
    down_full = lax.all_gather(w_down, AXES, axis=0, tiled=True)
    allowed = block_mask(scale_tokens)
    input_rows = inputs.astype(jnp.float32)
    ada_rows = w_ada.shape[0]
    ada_cols = w_ada.shape[1]
    activated_mine = lax.dynamic_slice_in_dim(activated_all, me * ada_rows, ada_rows, axis=1)
    ada_partial = jnp.dot(activated_mine, w_ada, preferred_element_type=jnp.float32)
    ada_parts = lax.all_to_all(
        ada_partial.reshape(count, sequences, ada_cols), AXES, split_axis=0, concat_axis=0, tiled=True
    )
    adaptive = jnp.sum(ada_parts, axis=0) + ada_bias
    gamma_attn, gamma_mlp, scale_attn, scale_mlp, shift_attn, shift_mlp = jnp.split(
        adaptive, 6, axis=1
    )
    normed_attn = modulate(input_rows, scale_attn, shift_attn).astype(jnp.bfloat16)
    projected = matmul_rows(normed_attn, qkv_full)
    query_pre = projected[..., :width] + query_bias
    key_pre = projected[..., width : 2 * width]
    queries = head_norm(query_pre, query_gain).astype(jnp.bfloat16)
    key_rows = head_norm(key_pre, key_gain).astype(jnp.bfloat16)
    value_rows = (projected[..., 2 * width :] + value_bias).astype(jnp.bfloat16).reshape(head_shape)
    context, logsum = jax.vmap(
        lambda q, k, v: attend_forward(q, k, v, allowed)
    )(queries, key_rows, value_rows)
    context = context.reshape(sequences, length, width)
    attended = matmul_rows(context, proj_full) + proj_bias
    middle = input_rows + gamma_attn[:, None, :] * attended
    normed_mlp = modulate(middle, scale_mlp, shift_mlp).astype(jnp.bfloat16)
    hidden_pre = matmul_rows(normed_mlp, up_full) + up_bias
    hidden = gelu_tanh(hidden_pre).astype(jnp.bfloat16)
    branch = matmul_rows(hidden, down_full) + down_bias
    layer_output = (middle + gamma_mlp[:, None, :] * branch).astype(jnp.bfloat16)
    upstream = cotangent.astype(jnp.float32)
    gamma_mlp_grad = jnp.sum(upstream * branch, axis=1)
    branch_grad = (upstream * gamma_mlp[:, None, :]).astype(jnp.bfloat16)
    down_grad = weight_grad(hidden, branch_grad)
    down_sum = scatter_natural(down_grad)
    down_bias_grad = jnp.sum(branch_grad.astype(jnp.float32), axis=(0, 1))
    return mlp_back(
        branch_grad, down_full, hidden_pre, normed_mlp, up_full, middle, scale_mlp, shift_mlp,
        upstream, attended, gamma_attn, context, proj_full, head_shape, queries, key_rows,
        value_rows, logsum, allowed, query_pre, query_gain, key_pre, key_gain, sequences,
        length, width, normed_attn, qkv_full, input_rows, scale_attn, shift_attn,
        gamma_mlp_grad, activated_mine, w_ada, cond_rows, me, count, layer_output,
        down_sum, down_bias_grad,
    )


def mlp_back(
    branch_grad, down_full, hidden_pre, normed_mlp, up_full, middle, scale_mlp, shift_mlp,
    upstream, attended, gamma_attn, context, proj_full, head_shape, queries, key_rows,
    value_rows, logsum, allowed, query_pre, query_gain, key_pre, key_gain, sequences,
    length, width, normed_attn, qkv_full, input_rows, scale_attn, shift_attn,
    gamma_mlp_grad, activated_mine, w_ada, cond_rows, me, count, layer_output,
    down_sum, down_bias_grad,
):
    hidden_grad = matmul_back(branch_grad, down_full)
    gelu_pull = jax.vjp(gelu_tanh, hidden_pre)[1]
    pre_grad = gelu_pull(hidden_grad)[0].astype(jnp.bfloat16)
    up_grad = weight_grad(normed_mlp, pre_grad)
    up_bias_grad = jnp.sum(pre_grad.astype(jnp.float32), axis=(0, 1))
    normed_mlp_grad = matmul_back(pre_grad, up_full)
    mlp_pull = jax.vjp(modulate, middle, scale_mlp, shift_mlp)[1]
    middle_part, scale_mlp_grad, shift_mlp_grad = mlp_pull(normed_mlp_grad)
    middle_grad = upstream + middle_part
    gamma_attn_grad = jnp.sum(middle_grad * attended, axis=1)
    attended_grad = (middle_grad * gamma_attn[:, None, :]).astype(jnp.bfloat16)
    proj_grad = weight_grad(context, attended_grad)
    proj_bias_grad = jnp.sum(attended_grad.astype(jnp.float32), axis=(0, 1))
    up_sum = scatter_natural(up_grad)
    context_gradient = (
        matmul_back(attended_grad, proj_full).astype(jnp.bfloat16).reshape(head_shape)
    )
    query_grad, key_grad, value_grad = jax.vmap(
        lambda q, k, v, l, c: attend_backward(q, k, v, l, c, allowed)
    )(queries, key_rows, value_rows, logsum, context_gradient)
    query_pull = jax.vjp(head_norm, query_pre, query_gain)[1]
    query_pre_grad, query_gain_grad = query_pull(query_grad)
    key_pull = jax.vjp(head_norm, key_pre, key_gain)[1]
    key_pre_grad, key_gain_grad = key_pull(key_grad)
    value_grad = value_grad.reshape(sequences, length, width)
    query_bias_grad = jnp.sum(query_pre_grad, axis=(0, 1))
    value_bias_grad = jnp.sum(value_grad, axis=(0, 1))
    projected_grad = jnp.concatenate([query_pre_grad, key_pre_grad, value_grad], axis=2).astype(
        jnp.bfloat16
    )
    qkv_grad = weight_grad(normed_attn, projected_grad)
    both_sum = scatter_natural(jnp.concatenate([qkv_grad, proj_grad], axis=1))
    qkv_sum = both_sum[:, : qkv_grad.shape[1]]
    proj_sum = both_sum[:, qkv_grad.shape[1] :]
    (
        query_bias_sum,
        value_bias_sum,
        query_gain_sum,
        key_gain_sum,
        proj_bias_sum,
        up_bias_sum,
        down_bias_sum,
    ) = sum_small(
        (
            query_bias_grad,
            value_bias_grad,
            query_gain_grad,
            key_gain_grad,
            proj_bias_grad,
            up_bias_grad,
            down_bias_grad,
        ),
        count,
    )
    return tail(
        projected_grad, qkv_full, input_rows, scale_attn, shift_attn, middle_grad,
        gamma_attn_grad, gamma_mlp_grad, scale_mlp_grad, shift_mlp_grad, activated_mine,
        w_ada, cond_rows, me, count, layer_output, qkv_sum, query_bias_sum, value_bias_sum,
        query_gain_sum, key_gain_sum, proj_sum, proj_bias_sum, up_sum, up_bias_sum, down_sum,
        down_bias_sum,
    )


def tail(
    projected_grad, qkv_full, input_rows, scale_attn, shift_attn, middle_grad,
    gamma_attn_grad, gamma_mlp_grad, scale_mlp_grad, shift_mlp_grad, activated_mine,
    w_ada, cond_rows, me, count, layer_output, qkv_sum, query_bias_sum, value_bias_sum,
    query_gain_sum, key_gain_sum, proj_sum, proj_bias_sum, up_sum, up_bias_sum, down_sum,
    down_bias_sum,
):
    ada_cols = w_ada.shape[1]
    normed_attn_grad = matmul_back(projected_grad, qkv_full)
    attn_pull = jax.vjp(modulate, input_rows, scale_attn, shift_attn)[1]
    input_part, scale_attn_grad, shift_attn_grad = attn_pull(normed_attn_grad)
    input_grad = middle_grad + input_part
    adaptive_grad = jnp.concatenate(
        [
            gamma_attn_grad,
            gamma_mlp_grad,
            scale_attn_grad,
            scale_mlp_grad,
            shift_attn_grad,
            shift_mlp_grad,
        ],
        axis=1,
    ).astype(jnp.bfloat16)
    adaptive_grad_all = nested_gather(adaptive_grad)
    ada_sum = jnp.einsum(
        "sc,sn->cn", activated_mine, adaptive_grad_all, preferred_element_type=jnp.float32
    )
    bias_share = ada_cols // count
    ada_bias_sum = jnp.sum(
        lax.dynamic_slice_in_dim(adaptive_grad_all, me * bias_share, bias_share, axis=1).astype(
            jnp.float32
        ),
        axis=0,
    )
    activated_grad_cols = jnp.einsum(
        "sn,cn->sc", adaptive_grad_all, w_ada, preferred_element_type=jnp.float32
    )
    activated_grad = lax.all_to_all(
        activated_grad_cols, AXES, split_axis=0, concat_axis=1, tiled=True
    )
    silu_pull = jax.vjp(jax.nn.silu, cond_rows)[1]
    condition_grad = silu_pull(activated_grad)[0]
    return (
        layer_output,
        input_grad,
        condition_grad,
        ada_sum,
        ada_bias_sum,
        qkv_sum,
        query_bias_sum,
        value_bias_sum,
        query_gain_sum,
        key_gain_sum,
        proj_sum,
        proj_bias_sum,
        up_sum,
        up_bias_sum,
        down_sum,
        down_bias_sum,
    )


def solution(mesh):
    row = P(AXES, None, None)
    mat = P(AXES, None)
    vec = P(AXES)
    return jax.shard_map(
        layer,
        mesh=mesh,
        in_specs=(row, mat, P(), mat, vec, mat, vec, vec, vec, vec, mat, vec, mat, vec, mat, vec, row),
        out_specs=(row, row, mat, mat, vec, mat, vec, vec, vec, vec, mat, vec, mat, vec, mat, vec),
        check_vma=False,
    )
```

```python
import jax
import jax.numpy as jnp
from jax import lax
from jax.experimental import pallas as pl
from jax.sharding import PartitionSpec as P


HEADS = 16
HEAD_DIM = 64
SEQ_LEN = 680
AXES = ("wide", "narrow")

EPSILON = 1e-06
MASKED = -1000000000.0


def layer_norm(values):
    centred = values - jnp.mean(values, axis=-1, keepdims=True)
    return centred * lax.rsqrt(jnp.mean(centred * centred, axis=-1, keepdims=True) + EPSILON)


def modulate(values, scaling, offset):
    return layer_norm(values) * (1.0 + scaling[:, None, :]) + offset[:, None, :]


def head_norm(values, channel_gain):
    shaped = values.reshape(values.shape[0], values.shape[1], HEADS, HEAD_DIM)
    scaled = shaped * lax.rsqrt(jnp.mean(shaped * shaped, axis=-1, keepdims=True) + EPSILON)
    return scaled * channel_gain.reshape(HEADS, HEAD_DIM)


def gelu_tanh(values):
    return jax.nn.gelu(values, approximate=True)


def block_limits(scale_tokens):
    block_ends = jnp.cumsum(scale_tokens)
    places = jnp.arange(SEQ_LEN, dtype=jnp.int32)
    return jnp.min(
        jnp.where(block_ends[None, :] > places[:, None], block_ends[None, :], SEQ_LEN), axis=1
    )


def block_mask(scale_tokens):
    places = jnp.arange(SEQ_LEN, dtype=jnp.int32)
    return places[None, :] < block_limits(scale_tokens)[:, None]


def attn_kernel(
    limit_ref, q_ref, k_ref, v_ref, qb_ref, vb_ref, qg_ref, kg_ref,
    ctx_ref, lse_ref, qo_ref, ko_ref, vo_ref,
):
    length = q_ref.shape[0]
    dim = q_ref.shape[1] // 2
    cols = lax.broadcasted_iota(jnp.int32, (length, length), 1)
    allowed = cols < limit_ref[...]
    query_all = q_ref[...] + qb_ref[...]
    key_all = k_ref[...]
    value = (v_ref[...] + vb_ref[...]).astype(jnp.bfloat16)
    vo_ref[...] = value
    outs, queries, keys = [], [], []
    for i in range(2):
        part = slice(i * dim, (i + 1) * dim)
        qp = query_all[:, part]
        kp = key_all[:, part]
        q = (qp * lax.rsqrt(jnp.mean(qp * qp, axis=1, keepdims=True) + EPSILON) * qg_ref[:, part]).astype(jnp.bfloat16)
        k = (kp * lax.rsqrt(jnp.mean(kp * kp, axis=1, keepdims=True) + EPSILON) * kg_ref[:, part]).astype(jnp.bfloat16)
        queries.append(q)
        keys.append(k)
        s = lax.dot_general(q, k, (((1,), (1,)), ((), ())), preferred_element_type=jnp.float32)
        s = jnp.where(allowed, s * dim ** (-0.5), MASKED)
        m = jnp.max(s, axis=1, keepdims=True)
        e = jnp.exp(s - m)
        l = jnp.sum(e, axis=1, keepdims=True)
        p = (e / l).astype(jnp.bfloat16)
        outs.append(jnp.dot(p, value[:, part], preferred_element_type=jnp.float32).astype(jnp.bfloat16))
        lse_ref[i] = m + jnp.log(l)
    ctx_ref[...] = jnp.concatenate(outs, axis=1)
    qo_ref[...] = jnp.concatenate(queries, axis=1)
    ko_ref[...] = jnp.concatenate(keys, axis=1)


def attention_forward(projected, query_bias, value_bias, query_gain, key_gain, limits, heads):
    length = projected.shape[0]
    width = projected.shape[1] // 3
    pair = 2 * (width // heads)
    pairs = heads // 2
    spec = pl.BlockSpec((length, pair), lambda h: (0, h))
    vec = pl.BlockSpec((1, pair), lambda h: (0, h))
    wide = jax.ShapeDtypeStruct((length, width), jnp.bfloat16)
    return pl.pallas_call(
        attn_kernel,
        grid=(pairs,),
        in_specs=[
            pl.BlockSpec((length, 1), lambda h: (0, 0)),
            spec,
            pl.BlockSpec((length, pair), lambda h: (0, h + pairs)),
            pl.BlockSpec((length, pair), lambda h: (0, h + 2 * pairs)),
            vec, vec, vec, vec,
        ],
        out_specs=[spec, pl.BlockSpec((2, length, 1), lambda h: (h, 0, 0)), spec, spec, spec],
        out_shape=[wide, jax.ShapeDtypeStruct((heads, length, 1), jnp.float32), wide, wide, wide],
        cost_estimate=pl.CostEstimate(
            flops=4 * length * length * width,
            transcendentals=heads * length * length,
            bytes_accessed=length * width * (12 + 8) + heads * length * 4,
        ),
    )(
        limits, projected, projected, projected,
        query_bias.reshape(1, width), value_bias.reshape(1, width),
        query_gain.reshape(1, width), key_gain.reshape(1, width),
    )


def matmul_rows(first_operand, second_operand):
    return jnp.einsum(
        "fyg,gq->fyq", first_operand, second_operand, preferred_element_type=jnp.float32
    )


def matmul_back(first_operand, second_operand):
    return jnp.einsum(
        "rfw,uw->rfu", first_operand, second_operand, preferred_element_type=jnp.float32
    )


def weight_grad(first_operand, second_operand):
    return jnp.einsum(
        "crk,cre->ke", first_operand, second_operand, preferred_element_type=jnp.float32
    )


def masked_scores(query_sequence, key_sequence, allowed):
    scores = jnp.einsum(
        "nkz,vkz->knv", query_sequence, key_sequence, preferred_element_type=jnp.float32
    ) * HEAD_DIM ** (-0.5)
    return jnp.where(allowed[None], scores, MASKED)


def attend_backward(
    query_sequence, key_sequence, value_sequence, logsum, context_gradient, allowed
):
    scores = masked_scores(query_sequence, key_sequence, allowed)
    attention_probabilities = jnp.exp(scores - logsum[..., None])
    prob_grad = jnp.einsum(
        "nkz,vkz->knv", context_gradient, value_sequence, preferred_element_type=jnp.float32
    )
    value_grad = jnp.einsum(
        "fgs,gfu->sfu",
        attention_probabilities.astype(jnp.bfloat16),
        context_gradient,
        preferred_element_type=jnp.float32,
    )
    score_gradient = (
        attention_probabilities
        * (prob_grad - jnp.sum(prob_grad * attention_probabilities, axis=-1, keepdims=True))
    ).astype(jnp.bfloat16)
    query_grad = jnp.einsum(
        "wcv,vwn->cwn", score_gradient, key_sequence, preferred_element_type=jnp.float32
    ) * HEAD_DIM ** (-0.5)
    key_grad = jnp.einsum(
        "fgs,gfu->sfu", score_gradient, query_sequence, preferred_element_type=jnp.float32
    ) * HEAD_DIM ** (-0.5)
    return (query_grad, key_grad, value_grad)


def nested_gather(member):
    return lax.all_gather(
        lax.all_gather(member, "narrow", axis=0, tiled=True), "wide", axis=0, tiled=True
    )


def narrow_sum(half):
    size = lax.axis_size("narrow")
    if size != 2:
        return lax.psum_scatter(half, "narrow", scatter_dimension=0, tiled=True).astype(jnp.float32)
    rows = half.shape[0] // 2
    here = lax.axis_index("narrow")
    keep = lax.dynamic_slice_in_dim(half, here * rows, rows, axis=0)
    send = lax.dynamic_slice_in_dim(half, (1 - here) * rows, rows, axis=0)
    got = lax.ppermute(send, "narrow", [(0, 1), (1, 0)])
    return keep.astype(jnp.float32) + got.astype(jnp.float32)


def scatter_natural(member):
    half = lax.psum_scatter(member.astype(jnp.bfloat16), "wide", scatter_dimension=0, tiled=True)
    return narrow_sum(half)


def sum_small(vectors, count):
    small = jnp.concatenate([v.reshape(count, -1) for v in vectors], axis=1)
    parts = lax.all_to_all(
        small.reshape(count, 1, small.shape[1]), AXES, split_axis=0, concat_axis=0, tiled=True
    )
    total = jnp.sum(parts, axis=0)[0]
    out, offset = [], 0
    for v in vectors:
        size = v.shape[0] // count
        out.append(total[offset : offset + size])
        offset += size
    return out


def layer(
    inputs,
    condition,
    scale_tokens,
    w_ada,
    bias_ada,
    w_qkv,
    bias_query,
    bias_value,
    gain_query,
    gain_key,
    w_proj,
    bias_proj,
    w_up,
    bias_up,
    w_down,
    bias_down,
    cotangent,
):
    count = lax.axis_size("wide") * lax.axis_size("narrow")
    me = lax.axis_index("wide") * lax.axis_size("narrow") + lax.axis_index("narrow")
    sequences, length, width = inputs.shape
    head_shape = (sequences, length, HEADS, HEAD_DIM)
    cond_rows = condition.astype(jnp.float32)
    activated = jax.nn.silu(cond_rows).astype(jnp.bfloat16)
    vectors = (bias_ada, bias_query, bias_value, gain_query, gain_key, bias_proj, bias_up, bias_down)
    small = nested_gather(
        jnp.concatenate([activated.reshape(-1)] + list(vectors))[None, :]
    )
    activated_all = small[:, : activated.size].reshape(count * sequences, activated.shape[1])
    unpacked, start = [], activated.size
    for member in vectors:
        size = member.shape[0]
        unpacked.append(small[:, start : start + size].reshape(count * size).astype(jnp.float32))
        start += size
    ada_bias, query_bias, value_bias, query_gain, key_gain, proj_bias, up_bias, down_bias = unpacked
    first = lax.all_gather(
        jnp.concatenate([w_qkv, w_proj, w_up], axis=1), AXES, axis=0, tiled=True
    )
    qkv_cols, proj_cols = w_qkv.shape[1], w_proj.shape[1]
    qkv_full = first[:, :qkv_cols]
    proj_full = first[:, qkv_cols : qkv_cols + proj_cols]
    up_full = first[:, qkv_cols + proj_cols :]
    down_full = lax.all_gather(w_down, AXES, axis=0, tiled=True)
    allowed = block_mask(scale_tokens)
    input_rows = inputs.astype(jnp.float32)
    ada_rows = w_ada.shape[0]
    ada_cols = w_ada.shape[1]
    activated_mine = lax.dynamic_slice_in_dim(activated_all, me * ada_rows, ada_rows, axis=1)
    ada_partial = jnp.dot(activated_mine, w_ada, preferred_element_type=jnp.float32)
    ada_parts = lax.all_to_all(
        ada_partial.reshape(count, sequences, ada_cols), AXES, split_axis=0, concat_axis=0, tiled=True
    )
    adaptive = jnp.sum(ada_parts, axis=0) + ada_bias
    gamma_attn, gamma_mlp, scale_attn, scale_mlp, shift_attn, shift_mlp = jnp.split(
        adaptive, 6, axis=1
    )
    normed_attn = modulate(input_rows, scale_attn, shift_attn).astype(jnp.bfloat16)
    projected = matmul_rows(normed_attn, qkv_full)
    query_pre = projected[..., :width] + query_bias
    key_pre = projected[..., width : 2 * width]
    limits = block_limits(scale_tokens).astype(jnp.int32)[:, None]
    context, logsum, queries, key_rows, value_rows = attention_forward(
        projected.reshape(length, 3 * width),
        query_bias,
        value_bias,
        query_gain,
        key_gain,
        limits,
        HEADS,
    )
    queries = queries.reshape(head_shape)
    key_rows = key_rows.reshape(head_shape)
    value_rows = value_rows.reshape(head_shape)
    context = context.reshape(sequences, length, width)
    logsum = logsum.reshape(sequences, HEADS, length)
    attended = matmul_rows(context, proj_full) + proj_bias
    middle = input_rows + gamma_attn[:, None, :] * attended
    normed_mlp = modulate(middle, scale_mlp, shift_mlp).astype(jnp.bfloat16)
    hidden_pre = matmul_rows(normed_mlp, up_full) + up_bias
    hidden = gelu_tanh(hidden_pre).astype(jnp.bfloat16)
    branch = matmul_rows(hidden, down_full) + down_bias
    layer_output = (middle + gamma_mlp[:, None, :] * branch).astype(jnp.bfloat16)
    upstream = cotangent.astype(jnp.float32)
    gamma_mlp_grad = jnp.sum(upstream * branch, axis=1)
    branch_grad = (upstream * gamma_mlp[:, None, :]).astype(jnp.bfloat16)
    down_grad = weight_grad(hidden, branch_grad)
    down_sum = scatter_natural(down_grad)
    down_bias_grad = jnp.sum(branch_grad.astype(jnp.float32), axis=(0, 1))
    return mlp_back(
        branch_grad, down_full, hidden_pre, normed_mlp, up_full, middle, scale_mlp, shift_mlp,
        upstream, attended, gamma_attn, context, proj_full, head_shape, queries, key_rows,
        value_rows, logsum, allowed, query_pre, query_gain, key_pre, key_gain, sequences,
        length, width, normed_attn, qkv_full, input_rows, scale_attn, shift_attn,
        gamma_mlp_grad, activated_mine, w_ada, cond_rows, me, count, layer_output,
        down_sum, down_bias_grad,
    )


def mlp_back(
    branch_grad, down_full, hidden_pre, normed_mlp, up_full, middle, scale_mlp, shift_mlp,
    upstream, attended, gamma_attn, context, proj_full, head_shape, queries, key_rows,
    value_rows, logsum, allowed, query_pre, query_gain, key_pre, key_gain, sequences,
    length, width, normed_attn, qkv_full, input_rows, scale_attn, shift_attn,
    gamma_mlp_grad, activated_mine, w_ada, cond_rows, me, count, layer_output,
    down_sum, down_bias_grad,
):
    hidden_grad = matmul_back(branch_grad, down_full)
    gelu_pull = jax.vjp(gelu_tanh, hidden_pre)[1]
    pre_grad = gelu_pull(hidden_grad)[0].astype(jnp.bfloat16)
    up_grad = weight_grad(normed_mlp, pre_grad)
    up_bias_grad = jnp.sum(pre_grad.astype(jnp.float32), axis=(0, 1))
    normed_mlp_grad = matmul_back(pre_grad, up_full)
    mlp_pull = jax.vjp(modulate, middle, scale_mlp, shift_mlp)[1]
    middle_part, scale_mlp_grad, shift_mlp_grad = mlp_pull(normed_mlp_grad)
    middle_grad = upstream + middle_part
    gamma_attn_grad = jnp.sum(middle_grad * attended, axis=1)
    attended_grad = (middle_grad * gamma_attn[:, None, :]).astype(jnp.bfloat16)
    proj_grad = weight_grad(context, attended_grad)
    proj_bias_grad = jnp.sum(attended_grad.astype(jnp.float32), axis=(0, 1))
    both_sum = scatter_natural(jnp.concatenate([up_grad, proj_grad], axis=1))
    up_sum = both_sum[:, : up_grad.shape[1]]
    proj_sum = both_sum[:, up_grad.shape[1] :]
    context_gradient = (
        matmul_back(attended_grad, proj_full).astype(jnp.bfloat16).reshape(head_shape)
    )
    query_grad, key_grad, value_grad = jax.vmap(
        lambda q, k, v, l, c: attend_backward(q, k, v, l, c, allowed)
    )(queries, key_rows, value_rows, logsum, context_gradient)
    query_pull = jax.vjp(head_norm, query_pre, query_gain)[1]
    query_pre_grad, query_gain_grad = query_pull(query_grad)
    key_pull = jax.vjp(head_norm, key_pre, key_gain)[1]
    key_pre_grad, key_gain_grad = key_pull(key_grad)
    value_grad = value_grad.reshape(sequences, length, width)
    query_bias_grad = jnp.sum(query_pre_grad, axis=(0, 1))
    value_bias_grad = jnp.sum(value_grad, axis=(0, 1))
    projected_grad = jnp.concatenate([query_pre_grad, key_pre_grad, value_grad], axis=2).astype(
        jnp.bfloat16
    )
    qkv_grad = weight_grad(normed_attn, projected_grad)
    qkv_sum = scatter_natural(qkv_grad)
    (
        query_bias_sum,
        value_bias_sum,
        query_gain_sum,
        key_gain_sum,
        proj_bias_sum,
        up_bias_sum,
        down_bias_sum,
    ) = sum_small(
        (
            query_bias_grad,
            value_bias_grad,
            query_gain_grad,
            key_gain_grad,
            proj_bias_grad,
            up_bias_grad,
            down_bias_grad,
        ),
        count,
    )
    return tail(
        projected_grad, qkv_full, input_rows, scale_attn, shift_attn, middle_grad,
        gamma_attn_grad, gamma_mlp_grad, scale_mlp_grad, shift_mlp_grad, activated_mine,
        w_ada, cond_rows, me, count, layer_output, qkv_sum, query_bias_sum, value_bias_sum,
        query_gain_sum, key_gain_sum, proj_sum, proj_bias_sum, up_sum, up_bias_sum, down_sum,
        down_bias_sum,
    )


def tail(
    projected_grad, qkv_full, input_rows, scale_attn, shift_attn, middle_grad,
    gamma_attn_grad, gamma_mlp_grad, scale_mlp_grad, shift_mlp_grad, activated_mine,
    w_ada, cond_rows, me, count, layer_output, qkv_sum, query_bias_sum, value_bias_sum,
    query_gain_sum, key_gain_sum, proj_sum, proj_bias_sum, up_sum, up_bias_sum, down_sum,
    down_bias_sum,
):
    ada_cols = w_ada.shape[1]
    normed_attn_grad = matmul_back(projected_grad, qkv_full)
    attn_pull = jax.vjp(modulate, input_rows, scale_attn, shift_attn)[1]
    input_part, scale_attn_grad, shift_attn_grad = attn_pull(normed_attn_grad)
    input_grad = middle_grad + input_part
    adaptive_grad = jnp.concatenate(
        [
            gamma_attn_grad,
            gamma_mlp_grad,
            scale_attn_grad,
            scale_mlp_grad,
            shift_attn_grad,
            shift_mlp_grad,
        ],
        axis=1,
    ).astype(jnp.bfloat16)
    adaptive_grad_all = nested_gather(adaptive_grad)
    ada_sum = jnp.einsum(
        "sc,sn->cn", activated_mine, adaptive_grad_all, preferred_element_type=jnp.float32
    )
    bias_share = ada_cols // count
    ada_bias_sum = jnp.sum(
        lax.dynamic_slice_in_dim(adaptive_grad_all, me * bias_share, bias_share, axis=1).astype(
            jnp.float32
        ),
        axis=0,
    )
    activated_grad_cols = jnp.einsum(
        "sn,cn->sc", adaptive_grad_all, w_ada, preferred_element_type=jnp.float32
    )
    activated_grad = lax.all_to_all(
        activated_grad_cols, AXES, split_axis=0, concat_axis=1, tiled=True
    )
    silu_pull = jax.vjp(jax.nn.silu, cond_rows)[1]
    condition_grad = silu_pull(activated_grad)[0]
    return (
        layer_output,
        input_grad,
        condition_grad,
        ada_sum,
        ada_bias_sum,
        qkv_sum,
        query_bias_sum,
        value_bias_sum,
        query_gain_sum,
        key_gain_sum,
        proj_sum,
        proj_bias_sum,
        up_sum,
        up_bias_sum,
        down_sum,
        down_bias_sum,
    )


def solution(mesh):
    row = P(AXES, None, None)
    mat = P(AXES, None)
    vec = P(AXES)
    return jax.shard_map(
        layer,
        mesh=mesh,
        in_specs=(row, mat, P(), mat, vec, mat, vec, vec, vec, vec, mat, vec, mat, vec, mat, vec, row),
        out_specs=(row, row, mat, mat, vec, mat, vec, vec, vec, vec, mat, vec, mat, vec, mat, vec),
        check_vma=False,
    )
```
